128 devices in a mesh: rows: 16 (over x, z), cols: 8 (over y, core).
Axes of the slice: x: 4, y: 4, z: 4, core: 2. Of those that a mesh axis runs over, the one named last changes fastest.
Arguments:
- features: bfloat16 [4, 128, 1024, 256], P(None, 'rows', 'cols'), may hold values from -27 to 27, as said below
- masks: int32 [4, 200, 128, 1024], P(None, None, 'rows', 'cols'), may hold values from 0 to 1, as said below
- queries: float32 [4, 200, 256], replicated, may hold values from -7 to 7
- conv_weight: bfloat16 [3, 3, 256, 256], replicated, may hold values from -0.125 to 0.125
- gn_gain: float32 [256], replicated, may hold values from 0.25 to 1.75
- gn_bias: float32 [256], replicated, may hold values from -0.5 to 0.5
- query_weight: bfloat16 [256, 256], replicated, may hold values from -7 to 7
- key_weight: bfloat16 [256, 256], replicated, may hold values from -0.375 to 0.375
- value_weight: bfloat16 [256, 256], replicated, may hold values from -0.375 to 0.375
- out_weight: bfloat16 [256, 256], replicated, may hold values from -0.375 to 0.375
- ln_gain: float32 [256], replicated, may hold values from 0.25 to 1.75
- ln_bias: float32 [256], replicated, may hold values from -0.5 to 0.5
- embed_one: bfloat16 [256, 256], replicated, may hold values from -0.375 to 0.375
- embed_two: bfloat16 [256, 256], replicated, may hold values from -0.375 to 0.375
Outputs:
- updated: float32 [4, 200, 256], replicated
- logits: bfloat16 [4, 200, 128, 1024], P(None, None, 'rows', 'cols')
The draws below stay inside these ranges and needn't reach their ends.
Inputs may be any that keep to these rules, and one draw needn't show every extreme that they name: features have magnitudes that vary over the image. `masks`: each entry is 0 or 1; a query's foreground lies in one rectangle of the image, and a query may have none.
All inputs are finite; a program needn't handle non-finite values.
Results may differ from the reference program's by a relative error of at most 0.035.
Values may be sent and summed in bfloat16 or wider, within the bound.
No kernel may reach another device: no remote copies, remote signals or barrier semaphores. Data moves between devices by JAX's collectives and lax.ppermute only.
A program may use at most 256 MiB of HBM per device.

```python
import math
import jax
import jax.numpy as jnp
from jax import lax

C = 256
HEADS = 8
Q = 200
GROUPS = 32
IMAGES = 4
TR = 8
TC = 128
HD = 32
H = 128
W = 1024


def draw_features(key, part):
    keys = jax.random.split(jax.random.fold_in(key, 11), 6)
    rise = jnp.arange(H, dtype=jnp.float32) / max(H - 1, 1)
    along = jnp.arange(W, dtype=jnp.float32) / max(W - 1, 1)
    flip_rows = jax.random.randint(keys[0], (IMAGES, 1), 0, 2) == 1
    flip_cols = jax.random.randint(keys[1], (IMAGES, 1), 0, 2) == 1
    rise_img = jnp.where(flip_rows, 1.0 - rise[None, :], rise[None, :])
    along_img = jnp.where(flip_cols, 1.0 - along[None, :], along[None, :])
    row_rough = jnp.exp(jax.random.uniform(keys[2], (IMAGES, H), jnp.float32, 0.0, math.log(2.2)))
    col_rough = jnp.exp(jax.random.uniform(keys[3], (IMAGES, W), jnp.float32, 0.0, math.log(2.2)))
    level = 3.0 ** (rise_img[:, :, None] + along_img[:, None, :]) * row_rough[:, :, None] * col_rough[:, None, :]
    base = jax.random.truncated_normal(keys[5], -4.0, 4.0, (IMAGES, H, W, C), jnp.float32)
    level = 0.15 * level
    return (base * level[:, :, :, None]).astype(jnp.bfloat16)


def draw_queries(key, part):
    first_key = jax.random.fold_in(jax.random.fold_in(key, 23), 0)
    base = jax.random.truncated_normal(first_key, -4.0, 4.0, (IMAGES, Q, C), jnp.float32)
    return base


def draw_query_weight(key, part):
    first_key = jax.random.fold_in(jax.random.fold_in(key, 53), 0)
    base = jax.random.truncated_normal(first_key, -4.0, 4.0, (C, C), jnp.float32) * (1.0 / math.sqrt(C // 16))
    return base.astype(jnp.bfloat16)


def draw_masks(key, part):
    keys = jax.random.split(jax.random.fold_in(key, 37), 6)
    row_start = jax.random.randint(keys[0], (IMAGES, Q, 1, 1), 0, H)
    row_span = jax.random.randint(keys[1], (IMAGES, Q, 1, 1), TR, 4 * TR + 1)
    col_start = jax.random.randint(keys[2], (IMAGES, Q, 1, 1), 0, W)
    col_span = jax.random.randint(keys[3], (IMAGES, Q, 1, 1), TC, 3 * TC + 1)
    live = jax.random.randint(keys[4], (IMAGES, Q, 1, 1), 0, 40) > 0
    keep = jax.random.randint(keys[5], (IMAGES, Q, H, W), 0, 10) < 8
    row_pos = jnp.arange(H, dtype=jnp.int32)[None, None, :, None]
    col_pos = jnp.arange(W, dtype=jnp.int32)[None, None, None, :]
    inside = (row_pos >= row_start) & (row_pos < row_start + row_span) & (col_pos >= col_start) & (col_pos < col_start + col_span)
    return (inside & keep & live).astype(jnp.int32)


def gaussian(stream_key, extent, scale, bound, held_as=jnp.bfloat16):
    drawn = jax.random.normal(stream_key, extent, jnp.float32) * scale
    return jnp.minimum(jnp.maximum(drawn, -bound), bound).astype(held_as)


def setup_inputs(seed: int = 0) -> dict:
    seeds = jax.random.split(jax.random.key(seed), 15)
    return {
        "features": draw_features(jax.random.fold_in(seeds[14], 71), 0),
        "masks": draw_masks(jax.random.fold_in(seeds[14], 71), 0),
        "queries": draw_queries(jax.random.fold_in(seeds[14], 71), 0),
        "conv_weight": gaussian(seeds[3], (3, 3, C, C), (9 * C) ** -0.5, 0.125),
        "gn_gain": jnp.clip(1.0 + 0.15 * jax.random.normal(seeds[4], (C,), jnp.float32), 0.25, 1.75),
        "gn_bias": jnp.clip(jax.random.uniform(seeds[5], (C,), jnp.float32, -0.5, 0.5), -0.5, 0.5),
        "query_weight": draw_query_weight(jax.random.fold_in(seeds[14], 71), 0),
        "key_weight": gaussian(seeds[7], (C, C), C ** -0.5, 0.375),
        "value_weight": gaussian(seeds[8], (C, C), C ** -0.5, 0.375),
        "out_weight": gaussian(seeds[9], (C, C), C ** -0.5, 0.375),
        "ln_gain": jnp.clip(1.0 + 0.15 * jax.random.normal(seeds[10], (C,), jnp.float32), 0.25, 1.75),
        "ln_bias": jnp.clip(jax.random.uniform(seeds[11], (C,), jnp.float32, -0.5, 0.5), -0.5, 0.5),
        "embed_one": gaussian(seeds[12], (C, C), C ** -0.5, 0.375),
        "embed_two": gaussian(seeds[13], (C, C), C ** -0.5, 0.375),
    }


def reference(features, masks, queries, conv_weight, gn_gain, gn_bias, query_weight, key_weight, value_weight, out_weight, ln_gain, ln_bias, embed_one, embed_two):
    conv = lax.conv_general_dilated(features, conv_weight, (1, 1), ((1, 1), (1, 1)), dimension_numbers=('NHWC', 'HWIO', 'NHWC'), preferred_element_type=jnp.float32)
    grouped = conv.reshape(IMAGES, H * W, GROUPS, C // GROUPS)
    number = H * W * (C // GROUPS)
    mean = lax.optimization_barrier(jnp.sum(grouped, axis=(1, 3))) / number
    var = lax.optimization_barrier(jnp.sum(grouped * grouped, axis=(1, 3))) / number - mean * mean
    normed = (grouped - mean[:, None, :, None]) / jnp.sqrt(var[:, None, :, None] + 1e-05)
    mask_feat = jax.nn.relu(normed.reshape(IMAGES, H * W, C) * gn_gain + gn_bias).astype(jnp.bfloat16)
    keys = jnp.dot(mask_feat, key_weight, preferred_element_type=jnp.float32).astype(jnp.bfloat16)
    vals = jnp.dot(mask_feat, value_weight, preferred_element_type=jnp.float32).astype(jnp.bfloat16)
    qproj = jnp.dot(queries.astype(jnp.bfloat16), query_weight, preferred_element_type=jnp.float32).astype(jnp.bfloat16)
    count = lax.optimization_barrier(jnp.sum(masks, axis=(2, 3)))
    allowed = (masks.reshape(IMAGES, Q, H * W) == 1) | (count == 0)[:, :, None]
    logit_scale = 1.0 / HD ** 0.5

    def one_head(index):
        head_query_rows = lax.dynamic_slice_in_dim(qproj, index * HD, HD, 2).astype(jnp.float32)
        head_key_rows = lax.dynamic_slice_in_dim(keys, index * HD, HD, 2).astype(jnp.float32)
        head_value_rows = lax.dynamic_slice_in_dim(vals, index * HD, HD, 2).astype(jnp.float32)
        attention_scores = jnp.einsum('iam,itm->iat', head_query_rows, head_key_rows) * logit_scale
        top = lax.optimization_barrier(jnp.max(jnp.where(allowed, attention_scores, -jnp.inf), axis=2))
        attention_weights = jnp.where(allowed, jnp.exp(attention_scores - top[:, :, None]), 0.0).astype(jnp.bfloat16)
        total = lax.optimization_barrier(jnp.sum(attention_weights.astype(jnp.float32), axis=2))
        weighted_total = jnp.einsum('xsr,xry->xsy', attention_weights.astype(jnp.float32), head_value_rows)
        return weighted_total / total[:, :, None]
    heads_out = lax.map(one_head, jnp.arange(HEADS, dtype=jnp.int32))
    attn = jnp.transpose(heads_out, (1, 2, 0, 3)).reshape(IMAGES, Q, C).astype(jnp.bfloat16)
    mixed = queries + jnp.dot(attn, out_weight, preferred_element_type=jnp.float32)
    centre = lax.optimization_barrier(jnp.mean(mixed, axis=2, keepdims=True))
    spread = lax.optimization_barrier(jnp.mean((mixed - centre) ** 2, axis=2, keepdims=True))
    updated = (mixed - centre) / jnp.sqrt(spread + 1e-05) * ln_gain + ln_bias
    hidden = jax.nn.relu(jnp.dot(updated.astype(jnp.bfloat16), embed_one, preferred_element_type=jnp.float32)).astype(jnp.bfloat16)
    embed = jnp.dot(hidden, embed_two, preferred_element_type=jnp.float32).astype(jnp.bfloat16)
    pixel_feat = mask_feat.reshape(IMAGES, H, W, C)

    def one_image(index):
        image_embed = lax.dynamic_index_in_dim(embed, index, 0, False).astype(jnp.float32)
        image_feat = lax.dynamic_index_in_dim(pixel_feat, index, 0, False).astype(jnp.float32)
        return jnp.einsum('qc,hwc->qhw', image_embed, image_feat).astype(jnp.bfloat16)
    logits = lax.map(one_image, jnp.arange(IMAGES, dtype=jnp.int32))
    return (updated, logits)
```

```python
import jax
import jax.numpy as jnp
from jax import lax
from jax.experimental import pallas as pl
from jax.sharding import PartitionSpec as P

HEADS = 8
GROUPS = 32
NEG = -1e30


def with_halo(cells, sides, width):
    for axis, dim in sides:
        count = lax.axis_size(axis)
        ends = count - 1
        head = lax.slice_in_dim(cells, 0, width, axis=dim)
        tail = lax.slice_in_dim(cells, cells.shape[dim] - width, cells.shape[dim], axis=dim)
        cells = jnp.concatenate(
            [
                lax.ppermute(tail, axis, [(i, (i + 1) % count) for i in range(ends)]),
                cells,
                lax.ppermute(head, axis, [((i + 1) % count, i) for i in range(ends)]),
            ],
            axis=dim,
        )
    return cells


def butterfly_sum(x):
    for axis in ("cols", "rows"):
        n = lax.axis_size(axis)
        if n & (n - 1):
            x = jax.tree.map(lambda v: lax.psum(v, axis), x)
            continue
        k = 1
        while k < n:
            got = lax.ppermute(x, axis, [(i, i ^ k) for i in range(n)])
            x = jax.tree.map(lambda a, b: a + b, x, got)
            k *= 2
    return x


def split_parts(x, span):
    return x[:, :span], x[:, span : span + span // 32], x[:, span + span // 32 :]


def merge(a, b, span):
    wa, ta, ma = split_parts(a, span)
    wb, tb, mb = split_parts(b, span)
    m = jnp.maximum(ma, mb)
    fa = jnp.exp(ma - m)
    fb = jnp.exp(mb - m)
    t = ta * fa + tb * fb
    w = wa * jnp.repeat(fa, 32, axis=1) + wb * jnp.repeat(fb, 32, axis=1)
    return jnp.concatenate([w, t, m], axis=1)


def halving_merge(x, span):
    for axis in ("cols", "rows"):
        n = lax.axis_size(axis)
        idx = lax.axis_index(axis)
        k = n // 2
        while k >= 1:
            h = x.shape[0] // 2
            lo, hi = x[:h], x[h:]
            upper = (idx // k) % 2 == 1
            keep = jnp.where(upper, hi, lo)
            send = jnp.where(upper, lo, hi)
            got = lax.ppermute(send, axis, [(i, i ^ k) for i in range(n)])
            x = merge(keep, got, span)
            k //= 2
    return x


def doubling_gather(a):
    for axis in ("rows", "cols"):
        n = lax.axis_size(axis)
        idx = lax.axis_index(axis)
        k = 1
        while k < n:
            got = lax.ppermute(a, axis, [(i, i ^ k) for i in range(n)])
            upper = (idx // k) % 2 == 1
            a = jnp.where(upper, jnp.concatenate([got, a]), jnp.concatenate([a, got]))
            k *= 2
    return a


def attention_kernel(q_ref, k_ref, v_ref, a_ref, top_ref, tot_ref, wv_ref, *, scale):
    q = q_ref[0, 0]
    k = k_ref[0, 0]
    s = lax.dot_general(q, k, (((1,), (1,)), ((), ())), preferred_element_type=jnp.float32) * scale
    allowed = a_ref[0] != 0
    top = jnp.max(jnp.where(allowed, s, NEG), axis=1, keepdims=True)
    w = jnp.where(allowed, jnp.exp(s - top), 0.0).astype(jnp.bfloat16)
    tot_ref[0, 0] = jnp.sum(w.astype(jnp.float32), axis=1, keepdims=True)
    top_ref[0, 0] = top
    wv_ref[0, 0] = jnp.dot(w, v_ref[0, 0], preferred_element_type=jnp.float32)


def attention(qh, kh, vh, allowed, scale):
    images, heads, queries, hd = qh.shape
    pixels = kh.shape[2]
    kernel = lambda *refs: attention_kernel(*refs, scale=scale)
    return pl.pallas_call(
        kernel,
        grid=(images, heads),
        in_specs=[
            pl.BlockSpec((1, 1, queries, hd), lambda i, h: (i, h, 0, 0)),
            pl.BlockSpec((1, 1, pixels, hd), lambda i, h: (i, h, 0, 0)),
            pl.BlockSpec((1, 1, pixels, hd), lambda i, h: (i, h, 0, 0)),
            pl.BlockSpec((1, queries, pixels), lambda i, h: (i, 0, 0)),
        ],
        out_specs=[
            pl.BlockSpec((1, 1, queries, 1), lambda i, h: (i, h, 0, 0)),
            pl.BlockSpec((1, 1, queries, 1), lambda i, h: (i, h, 0, 0)),
            pl.BlockSpec((1, 1, queries, hd), lambda i, h: (i, h, 0, 0)),
        ],
        out_shape=[
            jax.ShapeDtypeStruct((images, heads, queries, 1), jnp.float32),
            jax.ShapeDtypeStruct((images, heads, queries, 1), jnp.float32),
            jax.ShapeDtypeStruct((images, heads, queries, hd), jnp.float32),
        ],
    )(qh, kh, vh, allowed)


def on_device(
    features,
    masks,
    queries,
    conv_weight,
    gn_gain,
    gn_bias,
    query_weight,
    key_weight,
    value_weight,
    out_weight,
    ln_gain,
    ln_bias,
    embed_one,
    embed_two,
):
    images, tile_rows, tile_cols, width = features.shape
    query_count = queries.shape[1]
    heads = HEADS
    head_size = width // heads
    pixels = tile_rows * tile_cols
    devices = lax.axis_size("rows") * lax.axis_size("cols")
    local_count = jnp.sum(masks, axis=(2, 3)).astype(jnp.float32)
    padded = with_halo(features, (("rows", 1), ("cols", 2)), 1)
    conv = lax.conv_general_dilated(
        padded,
        conv_weight,
        (1, 1),
        "VALID",
        dimension_numbers=("NHWC", "HWIO", "NHWC"),
        preferred_element_type=jnp.float32,
    )
    grouped = conv.reshape(images, pixels, GROUPS, width // GROUPS)
    first_sum = jnp.sum(grouped, axis=(1, 3))
    second_sum = jnp.sum(grouped * grouped, axis=(1, 3))
    stats = butterfly_sum(jnp.concatenate([local_count, first_sum, second_sum], axis=1))
    count = stats[:, :query_count]
    first_sum = stats[:, query_count : query_count + GROUPS]
    second_sum = stats[:, query_count + GROUPS :]
    number = devices * pixels * (width // GROUPS)
    mean = first_sum / number
    var = second_sum / number - mean * mean
    normed = (grouped - mean[:, None, :, None]) / jnp.sqrt(var[:, None, :, None] + 1e-05)
    mask_feat = jax.nn.relu(normed.reshape(images, pixels, width) * gn_gain + gn_bias).astype(
        jnp.bfloat16
    )
    keys = jnp.dot(mask_feat, key_weight, preferred_element_type=jnp.float32).astype(jnp.bfloat16)
    vals = jnp.dot(mask_feat, value_weight, preferred_element_type=jnp.float32).astype(jnp.bfloat16)
    qproj = jnp.dot(
        queries.astype(jnp.bfloat16), query_weight, preferred_element_type=jnp.float32
    ).astype(jnp.bfloat16)
    allowed = (
        (masks.reshape(images, query_count, pixels) == 1) | (count == 0.0)[:, :, None]
    ).astype(jnp.int32)
    by_head = lambda x: x.reshape(images, -1, heads, head_size).transpose(0, 2, 1, 3)
    top, total, weighted = attention(
        by_head(qproj), by_head(keys), by_head(vals), allowed, 1.0 / head_size**0.5
    )
    span = images * query_count * width // devices
    packed = jnp.concatenate(
        [
            weighted.transpose(0, 2, 1, 3).reshape(devices, span),
            total[..., 0].transpose(0, 2, 1).reshape(devices, span // 32),
            top[..., 0].transpose(0, 2, 1).reshape(devices, span // 32),
        ],
        axis=1,
    )
    reduced = halving_merge(packed, span)
    sums, totals, _ = split_parts(reduced, span)
    attn_block = (sums / jnp.repeat(totals, 32, axis=1)).astype(jnp.bfloat16)
    attn = doubling_gather(attn_block).reshape(images, query_count, width)
    mixed = queries + jnp.dot(attn, out_weight, preferred_element_type=jnp.float32)
    centre = jnp.mean(mixed, axis=2, keepdims=True)
    spread = jnp.mean((mixed - centre) ** 2, axis=2, keepdims=True)
    updated = (mixed - centre) / jnp.sqrt(spread + 1e-05) * ln_gain + ln_bias
    hidden = jax.nn.relu(
        jnp.dot(updated.astype(jnp.bfloat16), embed_one, preferred_element_type=jnp.float32)
    ).astype(jnp.bfloat16)
    embed = jnp.dot(hidden, embed_two, preferred_element_type=jnp.float32).astype(jnp.bfloat16)
    logits = jnp.einsum(
        "bqc,bpc->bqp", embed, mask_feat, preferred_element_type=jnp.float32
    ).astype(jnp.bfloat16)
    return (updated, logits.reshape(images, query_count, tile_rows, tile_cols))


def solution(mesh):
    return jax.shard_map(
        on_device,
        mesh=mesh,
        in_specs=(
            P(None, "rows", "cols", None),
            P(None, None, "rows", "cols"),
            P(),
            P(),
            P(),
            P(),
            P(),
            P(),
            P(),
            P(),
            P(),
            P(),
            P(),
            P(),
        ),
        out_specs=(P(), P(None, None, "rows", "cols")),
        check_vma=False,
    )
```

```python
import jax
import jax.numpy as jnp
from jax import lax
from jax.experimental import pallas as pl
from jax.sharding import PartitionSpec as P

HEADS = 8
GROUPS = 32
NEG = -1e30


def with_halo(cells, sides, width):
    for axis, dim in sides:
        count = lax.axis_size(axis)
        ends = count - 1
        head = lax.slice_in_dim(cells, 0, width, axis=dim)
        tail = lax.slice_in_dim(cells, cells.shape[dim] - width, cells.shape[dim], axis=dim)
        cells = jnp.concatenate(
            [
                lax.ppermute(tail, axis, [(i, (i + 1) % count) for i in range(ends)]),
                cells,
                lax.ppermute(head, axis, [((i + 1) % count, i) for i in range(ends)]),
            ],
            axis=dim,
        )
    return cells


def butterfly_sum(x):
    for axis in ("cols", "rows"):
        n = lax.axis_size(axis)
        if n & (n - 1):
            x = jax.tree.map(lambda v: lax.psum(v, axis), x)
            continue
        k = 1
        while k < n:
            got = lax.ppermute(x, axis, [(i, i ^ k) for i in range(n)])
            x = jax.tree.map(lambda a, b: a + b, x, got)
            k *= 2
    return x


def split_parts(x, span):
    return x[:, :span], x[:, span : span + span // 32], x[:, span + span // 32 :]


def merge(a, b, span):
    wa, ta, ma = split_parts(a, span)
    wb, tb, mb = split_parts(b, span)
    m = jnp.maximum(ma, mb)
    fa = jnp.exp(ma - m)
    fb = jnp.exp(mb - m)
    t = ta * fa + tb * fb
    w = wa * jnp.repeat(fa, 32, axis=1) + wb * jnp.repeat(fb, 32, axis=1)
    return jnp.concatenate([w, t, m], axis=1)


def halving_merge(x, span):
    for axis in ("cols", "rows"):
        n = lax.axis_size(axis)
        idx = lax.axis_index(axis)
        k = n // 2
        while k >= 1:
            h = x.shape[0] // 2
            lo, hi = x[:h], x[h:]
            upper = (idx // k) % 2 == 1
            keep = jnp.where(upper, hi, lo)
            send = jnp.where(upper, lo, hi)
            got = lax.ppermute(send, axis, [(i, i ^ k) for i in range(n)])
            x = merge(keep, got, span)
            k //= 2
    return x


def doubling_gather(a):
    for axis in ("rows", "cols"):
        n = lax.axis_size(axis)
        idx = lax.axis_index(axis)
        k = 1
        while k < n:
            got = lax.ppermute(a, axis, [(i, i ^ k) for i in range(n)])
            upper = (idx // k) % 2 == 1
            a = jnp.where(upper, jnp.concatenate([got, a]), jnp.concatenate([a, got]))
            k *= 2
    return a


def prep_kernel(m_ref, fg_ref, cnt_ref):
    queries = fg_ref.shape[1]
    tile_rows = m_ref.shape[1] // queries
    tile_cols = m_ref.shape[2]
    acc = jnp.zeros((queries, tile_cols), jnp.float32)
    for r in range(tile_rows):
        rows = m_ref[0, pl.ds(r, queries, stride=tile_rows), :]
        fg = (rows == 1).astype(jnp.float32)
        acc = acc + fg
        fg_ref[0, :, r * tile_cols : (r + 1) * tile_cols] = fg.astype(jnp.bfloat16)
    cnt_ref[0] = jnp.sum(acc, axis=1, keepdims=True)


def prep(masks):
    images, queries, tile_rows, tile_cols = masks.shape
    flat = masks.reshape(images, queries * tile_rows, tile_cols)
    return pl.pallas_call(
        prep_kernel,
        grid=(images,),
        in_specs=[pl.BlockSpec((1, queries * tile_rows, tile_cols), lambda i: (i, 0, 0))],
        out_specs=[
            pl.BlockSpec((1, queries, tile_rows * tile_cols), lambda i: (i, 0, 0)),
            pl.BlockSpec((1, queries, 1), lambda i: (i, 0, 0)),
        ],
        out_shape=[
            jax.ShapeDtypeStruct((images, queries, tile_rows * tile_cols), jnp.bfloat16),
            jax.ShapeDtypeStruct((images, queries, 1), jnp.float32),
        ],
    )(flat)


def attention_kernel(q_ref, k_ref, v_ref, fg_ref, zero_ref, top_ref, tot_ref, wv_ref, *, heads, scale):
    queries = fg_ref.shape[1]
    width = k_ref.shape[2]
    head_size = width // heads
    k = k_ref[0]
    v = v_ref[0]
    allowed = (fg_ref[0] != 0) | (zero_ref[0] != 0)
    lane = lax.broadcasted_iota(jnp.int32, (queries, width), 1)
    acc = jnp.zeros((queries, width), jnp.float32)
    for h in range(heads):
        q = q_ref[0, h * queries : (h + 1) * queries, :]
        s = lax.dot_general(q, k, (((1,), (1,)), ((), ())), preferred_element_type=jnp.float32) * scale
        top = jnp.max(jnp.where(allowed, s, NEG), axis=1, keepdims=True)
        w = jnp.where(allowed, jnp.exp(s - top), 0.0).astype(jnp.bfloat16)
        tot_ref[0, :, h : h + 1] = jnp.sum(w.astype(jnp.float32), axis=1, keepdims=True)
        top_ref[0, :, h : h + 1] = top
        r = jnp.dot(w, v, preferred_element_type=jnp.float32)
        inside = (lane >= h * head_size) & (lane < (h + 1) * head_size)
        acc = acc + jnp.where(inside, r, 0.0)
    wv_ref[0] = acc


def attention(qbd, keys, vals, fg, zero, heads, scale):
    images, pixels, width = keys.shape
    queries = fg.shape[1]
    kernel = lambda *refs: attention_kernel(*refs, heads=heads, scale=scale)
    return pl.pallas_call(
        kernel,
        grid=(images,),
        in_specs=[
            pl.BlockSpec((1, heads * queries, width), lambda i: (i, 0, 0)),
            pl.BlockSpec((1, pixels, width), lambda i: (i, 0, 0)),
            pl.BlockSpec((1, pixels, width), lambda i: (i, 0, 0)),
            pl.BlockSpec((1, queries, pixels), lambda i: (i, 0, 0)),
            pl.BlockSpec((1, queries, 1), lambda i: (i, 0, 0)),
        ],
        out_specs=[
            pl.BlockSpec((1, queries, heads), lambda i: (i, 0, 0)),
            pl.BlockSpec((1, queries, heads), lambda i: (i, 0, 0)),
            pl.BlockSpec((1, queries, width), lambda i: (i, 0, 0)),
        ],
        out_shape=[
            jax.ShapeDtypeStruct((images, queries, heads), jnp.float32),
            jax.ShapeDtypeStruct((images, queries, heads), jnp.float32),
            jax.ShapeDtypeStruct((images, queries, width), jnp.float32),
        ],
    )(qbd, keys, vals, fg, zero)


def on_device(
    features,
    masks,
    queries,
    conv_weight,
    gn_gain,
    gn_bias,
    query_weight,
    key_weight,
    value_weight,
    out_weight,
    ln_gain,
    ln_bias,
    embed_one,
    embed_two,
):
    images, tile_rows, tile_cols, width = features.shape
    query_count = queries.shape[1]
    heads = HEADS
    head_size = width // heads
    pixels = tile_rows * tile_cols
    devices = lax.axis_size("rows") * lax.axis_size("cols")
    fg, local_count = prep(masks)
    padded = with_halo(features, (("rows", 1), ("cols", 2)), 1)
    conv = lax.conv_general_dilated(
        padded,
        conv_weight,
        (1, 1),
        "VALID",
        dimension_numbers=("NHWC", "HWIO", "NHWC"),
        preferred_element_type=jnp.float32,
    )
    grouped = conv.reshape(images, pixels, GROUPS, width // GROUPS)
    first_sum = jnp.sum(grouped, axis=(1, 3))
    second_sum = jnp.sum(grouped * grouped, axis=(1, 3))
    stats = butterfly_sum(jnp.concatenate([local_count[..., 0], first_sum, second_sum], axis=1))
    count = stats[:, :query_count]
    first_sum = stats[:, query_count : query_count + GROUPS]
    second_sum = stats[:, query_count + GROUPS :]
    number = devices * pixels * (width // GROUPS)
    mean = first_sum / number
    var = second_sum / number - mean * mean
    normed = (grouped - mean[:, None, :, None]) / jnp.sqrt(var[:, None, :, None] + 1e-05)
    mask_feat = jax.nn.relu(normed.reshape(images, pixels, width) * gn_gain + gn_bias).astype(
        jnp.bfloat16
    )
    keys = jnp.dot(mask_feat, key_weight, preferred_element_type=jnp.float32).astype(jnp.bfloat16)
    vals = jnp.dot(mask_feat, value_weight, preferred_element_type=jnp.float32).astype(jnp.bfloat16)
    qproj = jnp.dot(
        queries.astype(jnp.bfloat16), query_weight, preferred_element_type=jnp.float32
    ).astype(jnp.bfloat16)
    zero = (count == 0.0).astype(jnp.float32)[:, :, None]
    head_of_lane = jnp.arange(width) // head_size
    qbd = jnp.where(
        head_of_lane[None, None, None, :] == jnp.arange(heads)[None, :, None, None],
        qproj[:, None, :, :],
        jnp.zeros((), jnp.bfloat16),
    ).reshape(images, heads * query_count, width)
    top, total, weighted = attention(qbd, keys, vals, fg, zero, heads, 1.0 / head_size**0.5)
    span = images * query_count * width // devices
    packed = jnp.concatenate(
        [
            weighted.reshape(devices, span),
            total.reshape(devices, span // 32),
            top.reshape(devices, span // 32),
        ],
        axis=1,
    )
    reduced = halving_merge(packed, span)
    sums, totals, _ = split_parts(reduced, span)
    attn_block = (sums / jnp.repeat(totals, 32, axis=1)).astype(jnp.bfloat16)
    attn = doubling_gather(attn_block).reshape(images, query_count, width)
    mixed = queries + jnp.dot(attn, out_weight, preferred_element_type=jnp.float32)
    centre = jnp.mean(mixed, axis=2, keepdims=True)
    spread = jnp.mean((mixed - centre) ** 2, axis=2, keepdims=True)
    updated = (mixed - centre) / jnp.sqrt(spread + 1e-05) * ln_gain + ln_bias
    hidden = jax.nn.relu(
        jnp.dot(updated.astype(jnp.bfloat16), embed_one, preferred_element_type=jnp.float32)
    ).astype(jnp.bfloat16)
    embed = jnp.dot(hidden, embed_two, preferred_element_type=jnp.float32).astype(jnp.bfloat16)
    logits = jnp.einsum(
        "bqc,bpc->bqp", embed, mask_feat, preferred_element_type=jnp.float32
    ).astype(jnp.bfloat16)
    return (updated, logits.reshape(images, query_count, tile_rows, tile_cols))


def solution(mesh):
    return jax.shard_map(
        on_device,
        mesh=mesh,
        in_specs=(
            P(None, "rows", "cols", None),
            P(None, None, "rows", "cols"),
            P(),
            P(),
            P(),
            P(),
            P(),
            P(),
            P(),
            P(),
            P(),
            P(),
            P(),
            P(),
        ),
        out_specs=(P(), P(None, None, "rows", "cols")),
        check_vma=False,
    )
```

```python
import jax
import jax.numpy as jnp
from jax import lax
from jax.experimental import pallas as pl
from jax.sharding import PartitionSpec as P

HEADS = 8
GROUPS = 32
NEG = -1e30


def with_halo(cells, sides, width):
    for axis, dim in sides:
        count = lax.axis_size(axis)
        ends = count - 1
        head = lax.slice_in_dim(cells, 0, width, axis=dim)
        tail = lax.slice_in_dim(cells, cells.shape[dim] - width, cells.shape[dim], axis=dim)
        cells = jnp.concatenate(
            [
                lax.ppermute(tail, axis, [(i, (i + 1) % count) for i in range(ends)]),
                cells,
                lax.ppermute(head, axis, [((i + 1) % count, i) for i in range(ends)]),
            ],
            axis=dim,
        )
    return cells


def butterfly_sum(x):
    for axis in ("cols", "rows"):
        n = lax.axis_size(axis)
        if n & (n - 1):
            x = jax.tree.map(lambda v: lax.psum(v, axis), x)
            continue
        k = 1
        while k < n:
            got = lax.ppermute(x, axis, [(i, i ^ k) for i in range(n)])
            x = jax.tree.map(lambda a, b: a + b, x, got)
            k *= 2
    return x


def split_parts(x, span):
    return x[:, :span], x[:, span : span + span // 32], x[:, span + span // 32 :]


def merge(a, b, span):
    wa, ta, ma = split_parts(a, span)
    wb, tb, mb = split_parts(b, span)
    m = jnp.maximum(ma, mb)
    fa = jnp.exp(ma - m)
    fb = jnp.exp(mb - m)
    t = ta * fa + tb * fb
    w = wa * jnp.repeat(fa, 32, axis=1) + wb * jnp.repeat(fb, 32, axis=1)
    return jnp.concatenate([w, t, m], axis=1)


def halving_merge(x, span):
    for axis in ("cols", "rows"):
        n = lax.axis_size(axis)
        idx = lax.axis_index(axis)
        k = n // 2
        while k >= 1:
            h = x.shape[0] // 2
            lo, hi = x[:h], x[h:]
            upper = (idx // k) % 2 == 1
            keep = jnp.where(upper, hi, lo)
            send = jnp.where(upper, lo, hi)
            got = lax.ppermute(send, axis, [(i, i ^ k) for i in range(n)])
            x = merge(keep, got, span)
            k //= 2
    return x


def doubling_gather(a):
    for axis in ("rows", "cols"):
        n = lax.axis_size(axis)
        idx = lax.axis_index(axis)
        k = 1
        while k < n:
            got = lax.ppermute(a, axis, [(i, i ^ k) for i in range(n)])
            upper = (idx // k) % 2 == 1
            a = jnp.where(upper, jnp.concatenate([got, a]), jnp.concatenate([a, got]))
            k *= 2
    return a


def prep_kernel(m_ref, fg_ref, cnt_ref):
    queries = fg_ref.shape[1]
    tile_rows = m_ref.shape[1] // queries
    tile_cols = m_ref.shape[2]
    acc = jnp.zeros((queries, tile_cols), jnp.float32)
    for r in range(tile_rows):
        rows = m_ref[0, pl.ds(r, queries, stride=tile_rows), :]
        fg = (rows == 1).astype(jnp.float32)
        acc = acc + fg
        fg_ref[0, :, r * tile_cols : (r + 1) * tile_cols] = fg.astype(jnp.bfloat16)
    cnt_ref[0] = jnp.sum(acc, axis=1, keepdims=True)


def prep(masks):
    images, queries, tile_rows, tile_cols = masks.shape
    flat = masks.reshape(images, queries * tile_rows, tile_cols)
    return pl.pallas_call(
        prep_kernel,
        grid=(images,),
        in_specs=[pl.BlockSpec((1, queries * tile_rows, tile_cols), lambda i: (i, 0, 0))],
        out_specs=[
            pl.BlockSpec((1, queries, tile_rows * tile_cols), lambda i: (i, 0, 0)),
            pl.BlockSpec((1, queries, 1), lambda i: (i, 0, 0)),
        ],
        out_shape=[
            jax.ShapeDtypeStruct((images, queries, tile_rows * tile_cols), jnp.bfloat16),
            jax.ShapeDtypeStruct((images, queries, 1), jnp.float32),
        ],
    )(flat)


def attention_kernel(q_ref, k_ref, v_ref, fg_ref, zero_ref, top_ref, tot_ref, wv_ref, *, heads, scale):
    queries = fg_ref.shape[1]
    width = k_ref.shape[2]
    head_size = width // heads
    k = k_ref[0]
    v = v_ref[0]
    allowed = (fg_ref[0] != 0) | (zero_ref[0] != 0)
    lane = lax.broadcasted_iota(jnp.int32, (queries, width), 1)
    acc = jnp.zeros((queries, width), jnp.float32)
    for h in range(heads):
        q = q_ref[0, h * queries : (h + 1) * queries, :]
        s = lax.dot_general(q, k, (((1,), (1,)), ((), ())), preferred_element_type=jnp.float32) * scale
        top = jnp.max(jnp.where(allowed, s, NEG), axis=1, keepdims=True)
        w = jnp.where(allowed, jnp.exp(s - top), 0.0).astype(jnp.bfloat16)
        tot_ref[0, :, h : h + 1] = jnp.sum(w.astype(jnp.float32), axis=1, keepdims=True)
        top_ref[0, :, h : h + 1] = top
        r = jnp.dot(w, v, preferred_element_type=jnp.float32)
        inside = (lane >= h * head_size) & (lane < (h + 1) * head_size)
        acc = acc + jnp.where(inside, r, 0.0)
    wv_ref[0] = acc


def attention(qbd, keys, vals, fg, zero, heads, scale):
    images, pixels, width = keys.shape
    queries = fg.shape[1]
    kernel = lambda *refs: attention_kernel(*refs, heads=heads, scale=scale)
    return pl.pallas_call(
        kernel,
        grid=(images,),
        in_specs=[
            pl.BlockSpec((1, heads * queries, width), lambda i: (i, 0, 0)),
            pl.BlockSpec((1, pixels, width), lambda i: (i, 0, 0)),
            pl.BlockSpec((1, pixels, width), lambda i: (i, 0, 0)),
            pl.BlockSpec((1, queries, pixels), lambda i: (i, 0, 0)),
            pl.BlockSpec((1, queries, 1), lambda i: (i, 0, 0)),
        ],
        out_specs=[
            pl.BlockSpec((1, queries, heads), lambda i: (i, 0, 0)),
            pl.BlockSpec((1, queries, heads), lambda i: (i, 0, 0)),
            pl.BlockSpec((1, queries, width), lambda i: (i, 0, 0)),
        ],
        out_shape=[
            jax.ShapeDtypeStruct((images, queries, heads), jnp.float32),
            jax.ShapeDtypeStruct((images, queries, heads), jnp.float32),
            jax.ShapeDtypeStruct((images, queries, width), jnp.float32),
        ],
    )(qbd, keys, vals, fg, zero)


def on_device(
    features,
    masks,
    queries,
    conv_weight,
    gn_gain,
    gn_bias,
    query_weight,
    key_weight,
    value_weight,
    out_weight,
    ln_gain,
    ln_bias,
    embed_one,
    embed_two,
):
    images, tile_rows, tile_cols, width = features.shape
    query_count = queries.shape[1]
    heads = HEADS
    head_size = width // heads
    pixels = tile_rows * tile_cols
    devices = lax.axis_size("rows") * lax.axis_size("cols")
    fg, local_count = prep(masks)
    padded = with_halo(features, (("rows", 1), ("cols", 2)), 1)
    conv = lax.conv_general_dilated(
        padded,
        conv_weight,
        (1, 1),
        "VALID",
        dimension_numbers=("NHWC", "HWIO", "NHWC"),
        preferred_element_type=jnp.float32,
    )
    grouped = conv.reshape(images, pixels, GROUPS, width // GROUPS)
    first_sum = jnp.sum(grouped, axis=(1, 3))
    second_sum = jnp.sum(grouped * grouped, axis=(1, 3))
    stats = butterfly_sum(jnp.concatenate([local_count[..., 0], first_sum, second_sum], axis=1))
    count = stats[:, :query_count]
    first_sum = stats[:, query_count : query_count + GROUPS]
    second_sum = stats[:, query_count + GROUPS :]
    number = devices * pixels * (width // GROUPS)
    mean = first_sum / number
    var = second_sum / number - mean * mean
    normed = (grouped - mean[:, None, :, None]) / jnp.sqrt(var[:, None, :, None] + 1e-05)
    mask_feat = jax.nn.relu(normed.reshape(images, pixels, width) * gn_gain + gn_bias).astype(
        jnp.bfloat16
    )
    keys = jnp.dot(mask_feat, key_weight, preferred_element_type=jnp.float32).astype(jnp.bfloat16)
    vals = jnp.dot(mask_feat, value_weight, preferred_element_type=jnp.float32).astype(jnp.bfloat16)
    qproj = jnp.dot(
        queries.astype(jnp.bfloat16), query_weight, preferred_element_type=jnp.float32
    ).astype(jnp.bfloat16)
    zero = (count == 0.0).astype(jnp.float32)[:, :, None]
    head_of_lane = jnp.arange(width) // head_size
    qbd = jnp.where(
        head_of_lane[None, None, None, :] == jnp.arange(heads)[None, :, None, None],
        qproj[:, None, :, :],
        jnp.zeros((), jnp.bfloat16),
    ).reshape(images, heads * query_count, width)
    top, total, weighted = attention(qbd, keys, vals, fg, zero, heads, 1.0 / head_size**0.5)
    span = images * query_count * width // devices
    packed = jnp.concatenate(
        [
            weighted.reshape(devices, span),
            total.reshape(devices, span // 32),
            top.reshape(devices, span // 32),
        ],
        axis=1,
    )
    parts = lax.all_to_all(packed, ("rows", "cols"), 0, 0, tiled=True)
    sums, totals, tops = split_parts(parts, span)
    highest = jnp.max(tops, axis=0, keepdims=True)
    factor = jnp.exp(tops - highest)
    totals = jnp.sum(totals * factor, axis=0, keepdims=True)
    sums = jnp.sum(sums * jnp.repeat(factor, 32, axis=1), axis=0, keepdims=True)
    attn_block = (sums / jnp.repeat(totals, 32, axis=1)).astype(jnp.bfloat16)
    attn = lax.all_to_all(
        jnp.broadcast_to(attn_block, (devices, span)), ("rows", "cols"), 0, 0, tiled=True
    ).reshape(images, query_count, width)
    mixed = queries + jnp.dot(attn, out_weight, preferred_element_type=jnp.float32)
    centre = jnp.mean(mixed, axis=2, keepdims=True)
    spread = jnp.mean((mixed - centre) ** 2, axis=2, keepdims=True)
    updated = (mixed - centre) / jnp.sqrt(spread + 1e-05) * ln_gain + ln_bias
    hidden = jax.nn.relu(
        jnp.dot(updated.astype(jnp.bfloat16), embed_one, preferred_element_type=jnp.float32)
    ).astype(jnp.bfloat16)
    embed = jnp.dot(hidden, embed_two, preferred_element_type=jnp.float32).astype(jnp.bfloat16)
    logits = jnp.einsum(
        "bqc,bpc->bqp", embed, mask_feat, preferred_element_type=jnp.float32
    ).astype(jnp.bfloat16)
    return (updated, logits.reshape(images, query_count, tile_rows, tile_cols))


def solution(mesh):
    return jax.shard_map(
        on_device,
        mesh=mesh,
        in_specs=(
            P(None, "rows", "cols", None),
            P(None, None, "rows", "cols"),
            P(),
            P(),
            P(),
            P(),
            P(),
            P(),
            P(),
            P(),
            P(),
            P(),
            P(),
            P(),
        ),
        out_specs=(P(), P(None, None, "rows", "cols")),
        check_vma=False,
    )
```

```python
import jax
import jax.numpy as jnp
from jax import lax
from jax.experimental import pallas as pl
from jax.sharding import PartitionSpec as P

HEADS = 8
GROUPS = 32
NEG = -1e30


def with_halo(cells, sides, width):
    for axis, dim in sides:
        count = lax.axis_size(axis)
        ends = count - 1
        head = lax.slice_in_dim(cells, 0, width, axis=dim)
        tail = lax.slice_in_dim(cells, cells.shape[dim] - width, cells.shape[dim], axis=dim)
        cells = jnp.concatenate(
            [
                lax.ppermute(tail, axis, [(i, (i + 1) % count) for i in range(ends)]),
                cells,
                lax.ppermute(head, axis, [((i + 1) % count, i) for i in range(ends)]),
            ],
            axis=dim,
        )
    return cells


def butterfly_sum(x):
    for axis in ("cols", "rows"):
        n = lax.axis_size(axis)
        if n & (n - 1):
            x = jax.tree.map(lambda v: lax.psum(v, axis), x)
            continue
        k = 1
        while k < n:
            got = lax.ppermute(x, axis, [(i, i ^ k) for i in range(n)])
            x = jax.tree.map(lambda a, b: a + b, x, got)
            k *= 2
    return x


def split_parts(x, span):
    return x[:, :span], x[:, span : span + span // 32], x[:, span + span // 32 :]


def merge(a, b, span):
    wa, ta, ma = split_parts(a, span)
    wb, tb, mb = split_parts(b, span)
    m = jnp.maximum(ma, mb)
    fa = jnp.exp(ma - m)
    fb = jnp.exp(mb - m)
    t = ta * fa + tb * fb
    w = wa * jnp.repeat(fa, 32, axis=1) + wb * jnp.repeat(fb, 32, axis=1)
    return jnp.concatenate([w, t, m], axis=1)


def halving_merge(x, span):
    for axis in ("cols", "rows"):
        n = lax.axis_size(axis)
        idx = lax.axis_index(axis)
        k = n // 2
        while k >= 1:
            h = x.shape[0] // 2
            lo, hi = x[:h], x[h:]
            upper = (idx // k) % 2 == 1
            keep = jnp.where(upper, hi, lo)
            send = jnp.where(upper, lo, hi)
            got = lax.ppermute(send, axis, [(i, i ^ k) for i in range(n)])
            x = merge(keep, got, span)
            k //= 2
    return x


def doubling_gather(a):
    for axis in ("rows", "cols"):
        n = lax.axis_size(axis)
        idx = lax.axis_index(axis)
        k = 1
        while k < n:
            got = lax.ppermute(a, axis, [(i, i ^ k) for i in range(n)])
            upper = (idx // k) % 2 == 1
            a = jnp.where(upper, jnp.concatenate([got, a]), jnp.concatenate([a, got]))
            k *= 2
    return a


def prep_kernel(m_ref, fg_ref, cnt_ref):
    queries = fg_ref.shape[1]
    tile_rows = m_ref.shape[1] // queries
    tile_cols = m_ref.shape[2]
    acc = jnp.zeros((queries, tile_cols), jnp.float32)
    for r in range(tile_rows):
        rows = m_ref[0, pl.ds(r, queries, stride=tile_rows), :]
        fg = (rows == 1).astype(jnp.float32)
        acc = acc + fg
        fg_ref[0, :, r * tile_cols : (r + 1) * tile_cols] = fg.astype(jnp.bfloat16)
    cnt_ref[0] = jnp.sum(acc, axis=1, keepdims=True)


def prep(masks):
    images, queries, tile_rows, tile_cols = masks.shape
    flat = masks.reshape(images, queries * tile_rows, tile_cols)
    return pl.pallas_call(
        prep_kernel,
        grid=(images,),
        in_specs=[pl.BlockSpec((1, queries * tile_rows, tile_cols), lambda i: (i, 0, 0))],
        out_specs=[
            pl.BlockSpec((1, queries, tile_rows * tile_cols), lambda i: (i, 0, 0)),
            pl.BlockSpec((1, queries, 1), lambda i: (i, 0, 0)),
        ],
        out_shape=[
            jax.ShapeDtypeStruct((images, queries, tile_rows * tile_cols), jnp.bfloat16),
            jax.ShapeDtypeStruct((images, queries, 1), jnp.float32),
        ],
    )(flat)


def attention_kernel(q_ref, k_ref, v_ref, fg_ref, zero_ref, top_ref, tot_ref, wv_ref, *, heads, scale):
    queries = fg_ref.shape[1]
    width = k_ref.shape[2]
    head_size = width // heads
    k = k_ref[0]
    v = v_ref[0]
    allowed = (fg_ref[0] != 0) | (zero_ref[0] != 0)
    lane = lax.broadcasted_iota(jnp.int32, (queries, width), 1)
    acc = jnp.zeros((queries, width), jnp.float32)
    for h in range(heads):
        q = q_ref[0, h * queries : (h + 1) * queries, :]
        s = lax.dot_general(q, k, (((1,), (1,)), ((), ())), preferred_element_type=jnp.float32) * scale
        top = jnp.max(jnp.where(allowed, s, NEG), axis=1, keepdims=True)
        w = jnp.where(allowed, jnp.exp(s - top), 0.0).astype(jnp.bfloat16)
        tot_ref[0, :, h : h + 1] = jnp.sum(w.astype(jnp.float32), axis=1, keepdims=True)
        top_ref[0, :, h : h + 1] = top
        r = jnp.dot(w, v, preferred_element_type=jnp.float32)
        inside = (lane >= h * head_size) & (lane < (h + 1) * head_size)
        acc = acc + jnp.where(inside, r, 0.0)
    wv_ref[0] = acc


def attention(qbd, keys, vals, fg, zero, heads, scale):
    images, pixels, width = keys.shape
    queries = fg.shape[1]
    kernel = lambda *refs: attention_kernel(*refs, heads=heads, scale=scale)
    return pl.pallas_call(
        kernel,
        grid=(images,),
        in_specs=[
            pl.BlockSpec((1, heads * queries, width), lambda i: (i, 0, 0)),
            pl.BlockSpec((1, pixels, width), lambda i: (i, 0, 0)),
            pl.BlockSpec((1, pixels, width), lambda i: (i, 0, 0)),
            pl.BlockSpec((1, queries, pixels), lambda i: (i, 0, 0)),
            pl.BlockSpec((1, queries, 1), lambda i: (i, 0, 0)),
        ],
        out_specs=[
            pl.BlockSpec((1, queries, heads), lambda i: (i, 0, 0)),
            pl.BlockSpec((1, queries, heads), lambda i: (i, 0, 0)),
            pl.BlockSpec((1, queries, width), lambda i: (i, 0, 0)),
        ],
        out_shape=[
            jax.ShapeDtypeStruct((images, queries, heads), jnp.float32),
            jax.ShapeDtypeStruct((images, queries, heads), jnp.float32),
            jax.ShapeDtypeStruct((images, queries, width), jnp.float32),
        ],
    )(qbd, keys, vals, fg, zero)


def on_device(
    features,
    masks,
    queries,
    conv_weight,
    gn_gain,
    gn_bias,
    query_weight,
    key_weight,
    value_weight,
    out_weight,
    ln_gain,
    ln_bias,
    embed_one,
    embed_two,
):
    images, tile_rows, tile_cols, width = features.shape
    query_count = queries.shape[1]
    heads = HEADS
    head_size = width // heads
    pixels = tile_rows * tile_cols
    devices = lax.axis_size("rows") * lax.axis_size("cols")
    fg, local_count = prep(masks)
    padded = with_halo(features, (("rows", 1), ("cols", 2)), 1)
    conv = lax.conv_general_dilated(
        padded,
        conv_weight,
        (1, 1),
        "VALID",
        dimension_numbers=("NHWC", "HWIO", "NHWC"),
        preferred_element_type=jnp.float32,
    )
    grouped = conv.reshape(images, pixels, GROUPS, width // GROUPS)
    first_sum = jnp.sum(grouped, axis=(1, 3))
    second_sum = jnp.sum(grouped * grouped, axis=(1, 3))
    stats = jnp.concatenate([local_count[..., 0], first_sum, second_sum], axis=1).reshape(1, -1)
    stats = lax.all_to_all(
        jnp.broadcast_to(stats, (devices, stats.shape[1])), ("rows", "cols"), 0, 0, tiled=True
    )
    stats = jnp.sum(stats, axis=0).reshape(images, -1)
    count = stats[:, :query_count]
    first_sum = stats[:, query_count : query_count + GROUPS]
    second_sum = stats[:, query_count + GROUPS :]
    number = devices * pixels * (width // GROUPS)
    mean = first_sum / number
    var = second_sum / number - mean * mean
    normed = (grouped - mean[:, None, :, None]) / jnp.sqrt(var[:, None, :, None] + 1e-05)
    mask_feat = jax.nn.relu(normed.reshape(images, pixels, width) * gn_gain + gn_bias).astype(
        jnp.bfloat16
    )
    keys = jnp.dot(mask_feat, key_weight, preferred_element_type=jnp.float32).astype(jnp.bfloat16)
    vals = jnp.dot(mask_feat, value_weight, preferred_element_type=jnp.float32).astype(jnp.bfloat16)
    qproj = jnp.dot(
        queries.astype(jnp.bfloat16), query_weight, preferred_element_type=jnp.float32
    ).astype(jnp.bfloat16)
    zero = (count == 0.0).astype(jnp.float32)[:, :, None]
    head_of_lane = jnp.arange(width) // head_size
    qbd = jnp.where(
        head_of_lane[None, None, None, :] == jnp.arange(heads)[None, :, None, None],
        qproj[:, None, :, :],
        jnp.zeros((), jnp.bfloat16),
    ).reshape(images, heads * query_count, width)
    top, total, weighted = attention(qbd, keys, vals, fg, zero, heads, 1.0 / head_size**0.5)
    span = images * query_count * width // devices
    packed = jnp.concatenate(
        [
            weighted.reshape(devices, span),
            total.reshape(devices, span // 32),
            top.reshape(devices, span // 32),
        ],
        axis=1,
    )
    parts = lax.all_to_all(packed, ("rows", "cols"), 0, 0, tiled=True)
    sums, totals, tops = split_parts(parts, span)
    highest = jnp.max(tops, axis=0, keepdims=True)
    factor = jnp.exp(tops - highest)
    totals = jnp.sum(totals * factor, axis=0, keepdims=True)
    sums = jnp.sum(sums * jnp.repeat(factor, 32, axis=1), axis=0, keepdims=True)
    attn_block = (sums / jnp.repeat(totals, 32, axis=1)).astype(jnp.bfloat16)
    attn = lax.all_to_all(
        jnp.broadcast_to(attn_block, (devices, span)), ("rows", "cols"), 0, 0, tiled=True
    ).reshape(images, query_count, width)
    mixed = queries + jnp.dot(attn, out_weight, preferred_element_type=jnp.float32)
    centre = jnp.mean(mixed, axis=2, keepdims=True)
    spread = jnp.mean((mixed - centre) ** 2, axis=2, keepdims=True)
    updated = (mixed - centre) / jnp.sqrt(spread + 1e-05) * ln_gain + ln_bias
    hidden = jax.nn.relu(
        jnp.dot(updated.astype(jnp.bfloat16), embed_one, preferred_element_type=jnp.float32)
    ).astype(jnp.bfloat16)
    embed = jnp.dot(hidden, embed_two, preferred_element_type=jnp.float32).astype(jnp.bfloat16)
    logits = jnp.einsum(
        "bqc,bpc->bqp", embed, mask_feat, preferred_element_type=jnp.float32
    ).astype(jnp.bfloat16)
    return (updated, logits.reshape(images, query_count, tile_rows, tile_cols))


def solution(mesh):
    return jax.shard_map(
        on_device,
        mesh=mesh,
        in_specs=(
            P(None, "rows", "cols", None),
            P(None, None, "rows", "cols"),
            P(),
            P(),
            P(),
            P(),
            P(),
            P(),
            P(),
            P(),
            P(),
            P(),
            P(),
            P(),
        ),
        out_specs=(P(), P(None, None, "rows", "cols")),
        check_vma=False,
    )
```

```python
import jax
import jax.numpy as jnp
from jax import lax
from jax.experimental import pallas as pl
from jax.sharding import PartitionSpec as P

HEADS = 8
GROUPS = 32
NEG = -1e30


def with_halo(cells, sides, width):
    for axis, dim in sides:
        count = lax.axis_size(axis)
        ends = count - 1
        head = lax.slice_in_dim(cells, 0, width, axis=dim)
        tail = lax.slice_in_dim(cells, cells.shape[dim] - width, cells.shape[dim], axis=dim)
        cells = jnp.concatenate(
            [
                lax.ppermute(tail, axis, [(i, (i + 1) % count) for i in range(ends)]),
                cells,
                lax.ppermute(head, axis, [((i + 1) % count, i) for i in range(ends)]),
            ],
            axis=dim,
        )
    return cells


def butterfly_sum(x):
    for axis in ("cols", "rows"):
        n = lax.axis_size(axis)
        if n & (n - 1):
            x = jax.tree.map(lambda v: lax.psum(v, axis), x)
            continue
        k = 1
        while k < n:
            got = lax.ppermute(x, axis, [(i, i ^ k) for i in range(n)])
            x = jax.tree.map(lambda a, b: a + b, x, got)
            k *= 2
    return x


def split_parts(x, span):
    return x[:, :span], x[:, span : span + span // 32], x[:, span + span // 32 :]


def merge(a, b, span):
    wa, ta, ma = split_parts(a, span)
    wb, tb, mb = split_parts(b, span)
    m = jnp.maximum(ma, mb)
    fa = jnp.exp(ma - m)
    fb = jnp.exp(mb - m)
    t = ta * fa + tb * fb
    w = wa * jnp.repeat(fa, 32, axis=1) + wb * jnp.repeat(fb, 32, axis=1)
    return jnp.concatenate([w, t, m], axis=1)


def halving_merge(x, span):
    for axis in ("cols", "rows"):
        n = lax.axis_size(axis)
        idx = lax.axis_index(axis)
        k = n // 2
        while k >= 1:
            h = x.shape[0] // 2
            lo, hi = x[:h], x[h:]
            upper = (idx // k) % 2 == 1
            keep = jnp.where(upper, hi, lo)
            send = jnp.where(upper, lo, hi)
            got = lax.ppermute(send, axis, [(i, i ^ k) for i in range(n)])
            x = merge(keep, got, span)
            k //= 2
    return x


def doubling_gather(a):
    for axis in ("rows", "cols"):
        n = lax.axis_size(axis)
        idx = lax.axis_index(axis)
        k = 1
        while k < n:
            got = lax.ppermute(a, axis, [(i, i ^ k) for i in range(n)])
            upper = (idx // k) % 2 == 1
            a = jnp.where(upper, jnp.concatenate([got, a]), jnp.concatenate([a, got]))
            k *= 2
    return a


def prep_kernel(m_ref, fg_ref, cnt_ref):
    queries = fg_ref.shape[1]
    tile_rows = m_ref.shape[1] // queries
    tile_cols = m_ref.shape[2]
    acc = jnp.zeros((queries, tile_cols), jnp.float32)
    for r in range(tile_rows):
        rows = m_ref[0, pl.ds(r, queries, stride=tile_rows), :]
        fg = (rows == 1).astype(jnp.float32)
        acc = acc + fg
        fg_ref[0, :, r * tile_cols : (r + 1) * tile_cols] = fg.astype(jnp.bfloat16)
    cnt_ref[0] = jnp.sum(acc, axis=1, keepdims=True)


def prep(masks):
    images, queries, tile_rows, tile_cols = masks.shape
    flat = masks.reshape(images, queries * tile_rows, tile_cols)
    return pl.pallas_call(
        prep_kernel,
        grid=(images,),
        in_specs=[pl.BlockSpec((1, queries * tile_rows, tile_cols), lambda i: (i, 0, 0))],
        out_specs=[
            pl.BlockSpec((1, queries, tile_rows * tile_cols), lambda i: (i, 0, 0)),
            pl.BlockSpec((1, queries, 1), lambda i: (i, 0, 0)),
        ],
        out_shape=[
            jax.ShapeDtypeStruct((images, queries, tile_rows * tile_cols), jnp.bfloat16),
            jax.ShapeDtypeStruct((images, queries, 1), jnp.float32),
        ],
    )(flat)


def attention_kernel(q_ref, k_ref, v_ref, fg_ref, zero_ref, top_ref, tot_ref, wv_ref, *, heads, scale):
    queries = fg_ref.shape[1]
    width = k_ref.shape[2]
    head_size = width // heads
    k = k_ref[0]
    v = v_ref[0]
    allowed = (fg_ref[0] != 0) | (zero_ref[0] != 0)
    bias = jnp.where(allowed, 0.0, -jnp.inf)
    lane = lax.broadcasted_iota(jnp.int32, (queries, width), 1)
    acc = jnp.zeros((queries, width), jnp.float32)
    for h in range(heads):
        q = q_ref[0, h * queries : (h + 1) * queries, :]
        s = lax.dot_general(q, k, (((1,), (1,)), ((), ())), preferred_element_type=jnp.float32) * scale
        top = jnp.maximum(jnp.max(s + bias, axis=1, keepdims=True), NEG)
        w = jnp.exp(s + bias - top).astype(jnp.bfloat16)
        tot_ref[0, :, h : h + 1] = jnp.sum(w.astype(jnp.float32), axis=1, keepdims=True)
        top_ref[0, :, h : h + 1] = top
        r = jnp.dot(w, v, preferred_element_type=jnp.float32)
        inside = (lane >= h * head_size) & (lane < (h + 1) * head_size)
        acc = acc + jnp.where(inside, r, 0.0)
    wv_ref[0] = acc


def attention(qbd, keys, vals, fg, zero, heads, scale):
    images, pixels, width = keys.shape
    queries = fg.shape[1]
    kernel = lambda *refs: attention_kernel(*refs, heads=heads, scale=scale)
    return pl.pallas_call(
        kernel,
        grid=(images,),
        in_specs=[
            pl.BlockSpec((1, heads * queries, width), lambda i: (i, 0, 0)),
            pl.BlockSpec((1, pixels, width), lambda i: (i, 0, 0)),
            pl.BlockSpec((1, pixels, width), lambda i: (i, 0, 0)),
            pl.BlockSpec((1, queries, pixels), lambda i: (i, 0, 0)),
            pl.BlockSpec((1, queries, 1), lambda i: (i, 0, 0)),
        ],
        out_specs=[
            pl.BlockSpec((1, queries, heads), lambda i: (i, 0, 0)),
            pl.BlockSpec((1, queries, heads), lambda i: (i, 0, 0)),
            pl.BlockSpec((1, queries, width), lambda i: (i, 0, 0)),
        ],
        out_shape=[
            jax.ShapeDtypeStruct((images, queries, heads), jnp.float32),
            jax.ShapeDtypeStruct((images, queries, heads), jnp.float32),
            jax.ShapeDtypeStruct((images, queries, width), jnp.float32),
        ],
    )(qbd, keys, vals, fg, zero)


def on_device(
    features,
    masks,
    queries,
    conv_weight,
    gn_gain,
    gn_bias,
    query_weight,
    key_weight,
    value_weight,
    out_weight,
    ln_gain,
    ln_bias,
    embed_one,
    embed_two,
):
    images, tile_rows, tile_cols, width = features.shape
    query_count = queries.shape[1]
    heads = HEADS
    head_size = width // heads
    pixels = tile_rows * tile_cols
    devices = lax.axis_size("rows") * lax.axis_size("cols")
    fg, local_count = prep(masks)
    padded = with_halo(features, (("rows", 1), ("cols", 2)), 1)
    conv = lax.conv_general_dilated(
        padded,
        conv_weight,
        (1, 1),
        "VALID",
        dimension_numbers=("NHWC", "HWIO", "NHWC"),
        preferred_element_type=jnp.float32,
    )
    grouped = conv.reshape(images, pixels, GROUPS, width // GROUPS)
    first_sum = jnp.sum(grouped, axis=(1, 3))
    second_sum = jnp.sum(grouped * grouped, axis=(1, 3))
    stats = jnp.concatenate([local_count[..., 0], first_sum, second_sum], axis=1).reshape(1, -1)
    stats = lax.all_to_all(
        jnp.broadcast_to(stats, (devices, stats.shape[1])), ("rows", "cols"), 0, 0, tiled=True
    )
    stats = jnp.sum(stats, axis=0).reshape(images, -1)
    count = stats[:, :query_count]
    first_sum = stats[:, query_count : query_count + GROUPS]
    second_sum = stats[:, query_count + GROUPS :]
    number = devices * pixels * (width // GROUPS)
    mean = first_sum / number
    var = second_sum / number - mean * mean
    normed = (grouped - mean[:, None, :, None]) / jnp.sqrt(var[:, None, :, None] + 1e-05)
    mask_feat = jax.nn.relu(normed.reshape(images, pixels, width) * gn_gain + gn_bias).astype(
        jnp.bfloat16
    )
    keys = jnp.dot(mask_feat, key_weight, preferred_element_type=jnp.float32).astype(jnp.bfloat16)
    vals = jnp.dot(mask_feat, value_weight, preferred_element_type=jnp.float32).astype(jnp.bfloat16)
    qproj = jnp.dot(
        queries.astype(jnp.bfloat16), query_weight, preferred_element_type=jnp.float32
    ).astype(jnp.bfloat16)
    zero = (count == 0.0).astype(jnp.float32)[:, :, None]
    head_of_lane = jnp.arange(width) // head_size
    qbd = jnp.where(
        head_of_lane[None, None, None, :] == jnp.arange(heads)[None, :, None, None],
        qproj[:, None, :, :],
        jnp.zeros((), jnp.bfloat16),
    ).reshape(images, heads * query_count, width)
    top, total, weighted = attention(qbd, keys, vals, fg, zero, heads, 1.0 / head_size**0.5)
    span = images * query_count * width // devices
    packed = jnp.concatenate(
        [
            weighted.reshape(devices, span),
            total.reshape(devices, span // 32),
            top.reshape(devices, span // 32),
        ],
        axis=1,
    )
    parts = lax.all_to_all(packed, ("rows", "cols"), 0, 0, tiled=True)
    sums, totals, tops = split_parts(parts, span)
    highest = jnp.max(tops, axis=0, keepdims=True)
    factor = jnp.exp(tops - highest)
    totals = jnp.sum(totals * factor, axis=0, keepdims=True)
    sums = jnp.sum(sums * jnp.repeat(factor, 32, axis=1), axis=0, keepdims=True)
    attn_block = (sums / jnp.repeat(totals, 32, axis=1)).astype(jnp.bfloat16)
    attn = lax.all_to_all(
        jnp.broadcast_to(attn_block, (devices, span)), ("rows", "cols"), 0, 0, tiled=True
    ).reshape(images, query_count, width)
    mixed = queries + jnp.dot(attn, out_weight, preferred_element_type=jnp.float32)
    centre = jnp.mean(mixed, axis=2, keepdims=True)
    spread = jnp.mean((mixed - centre) ** 2, axis=2, keepdims=True)
    updated = (mixed - centre) / jnp.sqrt(spread + 1e-05) * ln_gain + ln_bias
    hidden = jax.nn.relu(
        jnp.dot(updated.astype(jnp.bfloat16), embed_one, preferred_element_type=jnp.float32)
    ).astype(jnp.bfloat16)
    embed = jnp.dot(hidden, embed_two, preferred_element_type=jnp.float32).astype(jnp.bfloat16)
    logits = jnp.einsum(
        "bqc,bpc->bqp", embed, mask_feat, preferred_element_type=jnp.float32
    ).astype(jnp.bfloat16)
    return (updated, logits.reshape(images, query_count, tile_rows, tile_cols))


def solution(mesh):
    return jax.shard_map(
        on_device,
        mesh=mesh,
        in_specs=(
            P(None, "rows", "cols", None),
            P(None, None, "rows", "cols"),
            P(),
            P(),
            P(),
            P(),
            P(),
            P(),
            P(),
            P(),
            P(),
            P(),
            P(),
            P(),
        ),
        out_specs=(P(), P(None, None, "rows", "cols")),
        check_vma=False,
    )
```

```python
import jax
import jax.numpy as jnp
from jax import lax
from jax.experimental import pallas as pl
from jax.experimental.pallas import tpu as pltpu
from jax.sharding import PartitionSpec as P

HEADS = 8
GROUPS = 32
NEG = -1e30


def with_halo(cells, sides, width):
    for axis, dim in sides:
        count = lax.axis_size(axis)
        ends = count - 1
        head = lax.slice_in_dim(cells, 0, width, axis=dim)
        tail = lax.slice_in_dim(cells, cells.shape[dim] - width, cells.shape[dim], axis=dim)
        cells = jnp.concatenate(
            [
                lax.ppermute(tail, axis, [(i, (i + 1) % count) for i in range(ends)]),
                cells,
                lax.ppermute(head, axis, [((i + 1) % count, i) for i in range(ends)]),
            ],
            axis=dim,
        )
    return cells


def butterfly_sum(x):
    for axis in ("cols", "rows"):
        n = lax.axis_size(axis)
        if n & (n - 1):
            x = jax.tree.map(lambda v: lax.psum(v, axis), x)
            continue
        k = 1
        while k < n:
            got = lax.ppermute(x, axis, [(i, i ^ k) for i in range(n)])
            x = jax.tree.map(lambda a, b: a + b, x, got)
            k *= 2
    return x


def split_parts(x, span):
    return x[:, :span], x[:, span : span + span // 32], x[:, span + span // 32 :]


def merge(a, b, span):
    wa, ta, ma = split_parts(a, span)
    wb, tb, mb = split_parts(b, span)
    m = jnp.maximum(ma, mb)
    fa = jnp.exp(ma - m)
    fb = jnp.exp(mb - m)
    t = ta * fa + tb * fb
    w = wa * jnp.repeat(fa, 32, axis=1) + wb * jnp.repeat(fb, 32, axis=1)
    return jnp.concatenate([w, t, m], axis=1)


def halving_merge(x, span):
    for axis in ("cols", "rows"):
        n = lax.axis_size(axis)
        idx = lax.axis_index(axis)
        k = n // 2
        while k >= 1:
            h = x.shape[0] // 2
            lo, hi = x[:h], x[h:]
            upper = (idx // k) % 2 == 1
            keep = jnp.where(upper, hi, lo)
            send = jnp.where(upper, lo, hi)
            got = lax.ppermute(send, axis, [(i, i ^ k) for i in range(n)])
            x = merge(keep, got, span)
            k //= 2
    return x


def doubling_gather(a):
    for axis in ("rows", "cols"):
        n = lax.axis_size(axis)
        idx = lax.axis_index(axis)
        k = 1
        while k < n:
            got = lax.ppermute(a, axis, [(i, i ^ k) for i in range(n)])
            upper = (idx // k) % 2 == 1
            a = jnp.where(upper, jnp.concatenate([got, a]), jnp.concatenate([a, got]))
            k *= 2
    return a


def prep_kernel(m_ref, fg_ref, cnt_ref):
    queries = fg_ref.shape[1]
    tile_rows = m_ref.shape[1] // queries
    tile_cols = m_ref.shape[2]
    acc = jnp.zeros((queries, tile_cols), jnp.float32)
    for r in range(tile_rows):
        rows = m_ref[0, pl.ds(r, queries, stride=tile_rows), :]
        fg = (rows == 1).astype(jnp.float32)
        acc = acc + fg
        fg_ref[0, :, r * tile_cols : (r + 1) * tile_cols] = fg.astype(jnp.bfloat16)
    cnt_ref[0] = jnp.sum(acc, axis=1, keepdims=True)


def prep(masks):
    images, queries, tile_rows, tile_cols = masks.shape
    flat = masks.reshape(images, queries * tile_rows, tile_cols)
    return pl.pallas_call(
        prep_kernel,
        grid=(images,),
        in_specs=[pl.BlockSpec((1, queries * tile_rows, tile_cols), lambda i: (i, 0, 0))],
        out_specs=[
            pl.BlockSpec((1, queries, tile_rows * tile_cols), lambda i: (i, 0, 0)),
            pl.BlockSpec((1, queries, 1), lambda i: (i, 0, 0)),
        ],
        out_shape=[
            jax.ShapeDtypeStruct((images, queries, tile_rows * tile_cols), jnp.bfloat16),
            jax.ShapeDtypeStruct((images, queries, 1), jnp.float32),
        ],
    )(flat)


def attention_kernel(q_ref, k_ref, v_ref, fg_ref, zero_ref, top_ref, tot_ref, wv_ref, *, heads, scale):
    queries = fg_ref.shape[1]
    width = k_ref.shape[2]
    head_size = width // heads
    k = k_ref[0]
    v = v_ref[0]
    allowed = (fg_ref[0] != 0) | (zero_ref[0] != 0)
    bias = jnp.where(allowed, 0.0, -jnp.inf)
    lane = lax.broadcasted_iota(jnp.int32, (queries, width), 1)
    acc = jnp.zeros((queries, width), jnp.float32)
    for h in range(heads):
        q = q_ref[0, h * queries : (h + 1) * queries, :]
        s = lax.dot_general(q, k, (((1,), (1,)), ((), ())), preferred_element_type=jnp.float32) * scale
        top = jnp.maximum(jnp.max(s + bias, axis=1, keepdims=True), NEG)
        w = jnp.exp(s + bias - top).astype(jnp.bfloat16)
        tot_ref[0, :, h : h + 1] = jnp.sum(w.astype(jnp.float32), axis=1, keepdims=True)
        top_ref[0, :, h : h + 1] = top
        r = jnp.dot(w, v, preferred_element_type=jnp.float32)
        inside = (lane >= h * head_size) & (lane < (h + 1) * head_size)
        acc = acc + jnp.where(inside, r, 0.0)
    wv_ref[0] = acc


def attention(qbd, keys, vals, fg, zero, heads, scale):
    images, pixels, width = keys.shape
    queries = fg.shape[1]
    kernel = lambda *refs: attention_kernel(*refs, heads=heads, scale=scale)
    return pl.pallas_call(
        kernel,
        grid=(images,),
        in_specs=[
            pl.BlockSpec((1, heads * queries, width), lambda i: (i, 0, 0)),
            pl.BlockSpec((1, pixels, width), lambda i: (i, 0, 0)),
            pl.BlockSpec((1, pixels, width), lambda i: (i, 0, 0)),
            pl.BlockSpec((1, queries, pixels), lambda i: (i, 0, 0)),
            pl.BlockSpec((1, queries, 1), lambda i: (i, 0, 0)),
        ],
        out_specs=[
            pl.BlockSpec((1, queries, heads), lambda i: (i, 0, 0)),
            pl.BlockSpec((1, queries, heads), lambda i: (i, 0, 0)),
            pl.BlockSpec((1, queries, width), lambda i: (i, 0, 0)),
        ],
        out_shape=[
            jax.ShapeDtypeStruct((images, queries, heads), jnp.float32),
            jax.ShapeDtypeStruct((images, queries, heads), jnp.float32),
            jax.ShapeDtypeStruct((images, queries, width), jnp.float32),
        ],
    )(qbd, keys, vals, fg, zero)


def logits_kernel(e_ref, f_ref, o_ref, acc_ref):
    queries = e_ref.shape[1]
    tile_cols = o_ref.shape[2]
    tile_rows = o_ref.shape[1] // queries
    e = e_ref[0]
    for r in range(tile_rows):
        f = f_ref[0, r * tile_cols : (r + 1) * tile_cols, :]
        res = lax.dot_general(e, f, (((1,), (1,)), ((), ())), preferred_element_type=jnp.float32)
        acc_ref[pl.ds(r, queries, stride=tile_rows), :] = res
    o_ref[0] = acc_ref[...].astype(o_ref.dtype)


def logits_of(embed, mask_feat, tile_rows, tile_cols):
    images, queries, width = embed.shape
    pixels = mask_feat.shape[1]
    return pl.pallas_call(
        logits_kernel,
        grid=(images,),
        in_specs=[
            pl.BlockSpec((1, queries, width), lambda i: (i, 0, 0)),
            pl.BlockSpec((1, pixels, width), lambda i: (i, 0, 0)),
        ],
        out_specs=pl.BlockSpec((1, queries * tile_rows, tile_cols), lambda i: (i, 0, 0)),
        out_shape=jax.ShapeDtypeStruct((images, queries * tile_rows, tile_cols), jnp.bfloat16),
        scratch_shapes=[pltpu.VMEM((queries * tile_rows, tile_cols), jnp.float32)],
    )(embed, mask_feat)


def on_device(
    features,
    masks,
    queries,
    conv_weight,
    gn_gain,
    gn_bias,
    query_weight,
    key_weight,
    value_weight,
    out_weight,
    ln_gain,
    ln_bias,
    embed_one,
    embed_two,
):
    images, tile_rows, tile_cols, width = features.shape
    query_count = queries.shape[1]
    heads = HEADS
    head_size = width // heads
    pixels = tile_rows * tile_cols
    devices = lax.axis_size("rows") * lax.axis_size("cols")
    fg, local_count = prep(masks)
    padded = with_halo(features, (("rows", 1), ("cols", 2)), 1)
    conv = lax.conv_general_dilated(
        padded,
        conv_weight,
        (1, 1),
        "VALID",
        dimension_numbers=("NHWC", "HWIO", "NHWC"),
        preferred_element_type=jnp.float32,
    )
    grouped = conv.reshape(images, pixels, GROUPS, width // GROUPS)
    first_sum = jnp.sum(grouped, axis=(1, 3))
    second_sum = jnp.sum(grouped * grouped, axis=(1, 3))
    stats = jnp.concatenate([local_count[..., 0], first_sum, second_sum], axis=1).reshape(1, -1)
    stats = lax.all_to_all(
        jnp.broadcast_to(stats, (devices, stats.shape[1])), ("rows", "cols"), 0, 0, tiled=True
    )
    stats = jnp.sum(stats, axis=0).reshape(images, -1)
    count = stats[:, :query_count]
    first_sum = stats[:, query_count : query_count + GROUPS]
    second_sum = stats[:, query_count + GROUPS :]
    number = devices * pixels * (width // GROUPS)
    mean = first_sum / number
    var = second_sum / number - mean * mean
    normed = (grouped - mean[:, None, :, None]) / jnp.sqrt(var[:, None, :, None] + 1e-05)
    mask_feat = jax.nn.relu(normed.reshape(images, pixels, width) * gn_gain + gn_bias).astype(
        jnp.bfloat16
    )
    keys = jnp.dot(mask_feat, key_weight, preferred_element_type=jnp.float32).astype(jnp.bfloat16)
    vals = jnp.dot(mask_feat, value_weight, preferred_element_type=jnp.float32).astype(jnp.bfloat16)
    qproj = jnp.dot(
        queries.astype(jnp.bfloat16), query_weight, preferred_element_type=jnp.float32
    ).astype(jnp.bfloat16)
    zero = (count == 0.0).astype(jnp.float32)[:, :, None]
    head_of_lane = jnp.arange(width) // head_size
    qbd = jnp.where(
        head_of_lane[None, None, None, :] == jnp.arange(heads)[None, :, None, None],
        qproj[:, None, :, :],
        jnp.zeros((), jnp.bfloat16),
    ).reshape(images, heads * query_count, width)
    top, total, weighted = attention(qbd, keys, vals, fg, zero, heads, 1.0 / head_size**0.5)
    span = images * query_count * width // devices
    packed = jnp.concatenate(
        [
            weighted.reshape(devices, span),
            total.reshape(devices, span // 32),
            top.reshape(devices, span // 32),
        ],
        axis=1,
    )
    parts = lax.all_to_all(packed, ("rows", "cols"), 0, 0, tiled=True)
    sums, totals, tops = split_parts(parts, span)
    highest = jnp.max(tops, axis=0, keepdims=True)
    factor = jnp.exp(tops - highest)
    totals = jnp.sum(totals * factor, axis=0, keepdims=True)
    sums = jnp.sum(sums * jnp.repeat(factor, 32, axis=1), axis=0, keepdims=True)
    attn_block = (sums / jnp.repeat(totals, 32, axis=1)).astype(jnp.bfloat16)
    attn = lax.all_to_all(
        jnp.broadcast_to(attn_block, (devices, span)), ("rows", "cols"), 0, 0, tiled=True
    ).reshape(images, query_count, width)
    mixed = queries + jnp.dot(attn, out_weight, preferred_element_type=jnp.float32)
    centre = jnp.mean(mixed, axis=2, keepdims=True)
    spread = jnp.mean((mixed - centre) ** 2, axis=2, keepdims=True)
    updated = (mixed - centre) / jnp.sqrt(spread + 1e-05) * ln_gain + ln_bias
    hidden = jax.nn.relu(
        jnp.dot(updated.astype(jnp.bfloat16), embed_one, preferred_element_type=jnp.float32)
    ).astype(jnp.bfloat16)
    embed = jnp.dot(hidden, embed_two, preferred_element_type=jnp.float32).astype(jnp.bfloat16)
    logits = logits_of(embed, mask_feat, tile_rows, tile_cols)
    return (updated, logits.reshape(images, query_count, tile_rows, tile_cols))


def solution(mesh):
    return jax.shard_map(
        on_device,
        mesh=mesh,
        in_specs=(
            P(None, "rows", "cols", None),
            P(None, None, "rows", "cols"),
            P(),
            P(),
            P(),
            P(),
            P(),
            P(),
            P(),
            P(),
            P(),
            P(),
            P(),
            P(),
        ),
        out_specs=(P(), P(None, None, "rows", "cols")),
        check_vma=False,
    )
```

```python
import jax
import jax.numpy as jnp
from jax import lax
from jax.experimental import pallas as pl
from jax.experimental.pallas import tpu as pltpu
from jax.sharding import PartitionSpec as P

HEADS = 8
GROUPS = 32
NEG = -1e30


def with_halo(cells, sides, width):
    for axis, dim in sides:
        count = lax.axis_size(axis)
        ends = count - 1
        head = lax.slice_in_dim(cells, 0, width, axis=dim)
        tail = lax.slice_in_dim(cells, cells.shape[dim] - width, cells.shape[dim], axis=dim)
        cells = jnp.concatenate(
            [
                lax.ppermute(tail, axis, [(i, (i + 1) % count) for i in range(ends)]),
                cells,
                lax.ppermute(head, axis, [((i + 1) % count, i) for i in range(ends)]),
            ],
            axis=dim,
        )
    return cells


def butterfly_sum(x):
    for axis in ("cols", "rows"):
        n = lax.axis_size(axis)
        if n & (n - 1):
            x = jax.tree.map(lambda v: lax.psum(v, axis), x)
            continue
        k = 1
        while k < n:
            got = lax.ppermute(x, axis, [(i, i ^ k) for i in range(n)])
            x = jax.tree.map(lambda a, b: a + b, x, got)
            k *= 2
    return x


def split_parts(x, span):
    return x[:, :span], x[:, span : span + span // 32], x[:, span + span // 32 :]


def merge(a, b, span):
    wa, ta, ma = split_parts(a, span)
    wb, tb, mb = split_parts(b, span)
    m = jnp.maximum(ma, mb)
    fa = jnp.exp(ma - m)
    fb = jnp.exp(mb - m)
    t = ta * fa + tb * fb
    w = wa * jnp.repeat(fa, 32, axis=1) + wb * jnp.repeat(fb, 32, axis=1)
    return jnp.concatenate([w, t, m], axis=1)


def halving_merge(x, span):
    for axis in ("cols", "rows"):
        n = lax.axis_size(axis)
        idx = lax.axis_index(axis)
        k = n // 2
        while k >= 1:
            h = x.shape[0] // 2
            lo, hi = x[:h], x[h:]
            upper = (idx // k) % 2 == 1
            keep = jnp.where(upper, hi, lo)
            send = jnp.where(upper, lo, hi)
            got = lax.ppermute(send, axis, [(i, i ^ k) for i in range(n)])
            x = merge(keep, got, span)
            k //= 2
    return x


def doubling_gather(a):
    for axis in ("rows", "cols"):
        n = lax.axis_size(axis)
        idx = lax.axis_index(axis)
        k = 1
        while k < n:
            got = lax.ppermute(a, axis, [(i, i ^ k) for i in range(n)])
            upper = (idx // k) % 2 == 1
            a = jnp.where(upper, jnp.concatenate([got, a]), jnp.concatenate([a, got]))
            k *= 2
    return a


def prep_kernel(m_ref, fg_ref, cnt_ref):
    queries = fg_ref.shape[1]
    tile_rows = m_ref.shape[1] // queries
    tile_cols = m_ref.shape[2]
    acc = jnp.zeros((queries, tile_cols), jnp.float32)
    for r in range(tile_rows):
        rows = m_ref[0, pl.ds(r, queries, stride=tile_rows), :]
        fg = (rows == 1).astype(jnp.float32)
        acc = acc + fg
        fg_ref[0, :, r * tile_cols : (r + 1) * tile_cols] = fg.astype(jnp.bfloat16)
    cnt_ref[0] = jnp.sum(acc, axis=1, keepdims=True)


def prep(masks):
    images, queries, tile_rows, tile_cols = masks.shape
    flat = masks.reshape(images, queries * tile_rows, tile_cols)
    return pl.pallas_call(
        prep_kernel,
        grid=(images,),
        in_specs=[pl.BlockSpec((1, queries * tile_rows, tile_cols), lambda i: (i, 0, 0))],
        out_specs=[
            pl.BlockSpec((1, queries, tile_rows * tile_cols), lambda i: (i, 0, 0)),
            pl.BlockSpec((1, queries, 1), lambda i: (i, 0, 0)),
        ],
        out_shape=[
            jax.ShapeDtypeStruct((images, queries, tile_rows * tile_cols), jnp.bfloat16),
            jax.ShapeDtypeStruct((images, queries, 1), jnp.float32),
        ],
    )(flat)


def attention_kernel(q_ref, k_ref, v_ref, fg_ref, zero_ref, top_ref, tot_ref, wv_ref, *, heads, scale):
    queries = fg_ref.shape[1]
    width = k_ref.shape[2]
    head_size = width // heads
    k = k_ref[0]
    v = v_ref[0]
    allowed = (fg_ref[0] != 0) | (zero_ref[0] != 0)
    bias = jnp.where(allowed, 0.0, -jnp.inf)
    lane = lax.broadcasted_iota(jnp.int32, (queries, width), 1)
    acc = jnp.zeros((queries, width), jnp.float32)
    for h in range(heads):
        q = q_ref[0, h * queries : (h + 1) * queries, :]
        s = lax.dot_general(q, k, (((1,), (1,)), ((), ())), preferred_element_type=jnp.float32) * scale
        top = jnp.maximum(jnp.max(s + bias, axis=1, keepdims=True), NEG)
        w = jnp.exp(s + bias - top).astype(jnp.bfloat16)
        tot_ref[0, :, h : h + 1] = jnp.sum(w.astype(jnp.float32), axis=1, keepdims=True)
        top_ref[0, :, h : h + 1] = top
        r = jnp.dot(w, v, preferred_element_type=jnp.float32)
        inside = (lane >= h * head_size) & (lane < (h + 1) * head_size)
        acc = acc + jnp.where(inside, r, 0.0)
    wv_ref[0] = acc


def attention(qbd, keys, vals, fg, zero, heads, scale):
    images, pixels, width = keys.shape
    queries = fg.shape[1]
    kernel = lambda *refs: attention_kernel(*refs, heads=heads, scale=scale)
    return pl.pallas_call(
        kernel,
        grid=(images,),
        in_specs=[
            pl.BlockSpec((1, heads * queries, width), lambda i: (i, 0, 0)),
            pl.BlockSpec((1, pixels, width), lambda i: (i, 0, 0)),
            pl.BlockSpec((1, pixels, width), lambda i: (i, 0, 0)),
            pl.BlockSpec((1, queries, pixels), lambda i: (i, 0, 0)),
            pl.BlockSpec((1, queries, 1), lambda i: (i, 0, 0)),
        ],
        out_specs=[
            pl.BlockSpec((1, queries, heads), lambda i: (i, 0, 0)),
            pl.BlockSpec((1, queries, heads), lambda i: (i, 0, 0)),
            pl.BlockSpec((1, queries, width), lambda i: (i, 0, 0)),
        ],
        out_shape=[
            jax.ShapeDtypeStruct((images, queries, heads), jnp.float32),
            jax.ShapeDtypeStruct((images, queries, heads), jnp.float32),
            jax.ShapeDtypeStruct((images, queries, width), jnp.float32),
        ],
    )(qbd, keys, vals, fg, zero)


def logits_kernel(e_ref, f_ref, o_ref, acc_ref):
    queries = e_ref.shape[1]
    tile_cols = o_ref.shape[2]
    tile_rows = o_ref.shape[1] // queries
    e = e_ref[0]
    for r in range(tile_rows):
        f = f_ref[0, r * tile_cols : (r + 1) * tile_cols, :]
        res = lax.dot_general(e, f, (((1,), (1,)), ((), ())), preferred_element_type=jnp.float32)
        acc_ref[pl.ds(r, queries, stride=tile_rows), :] = res
    o_ref[0] = acc_ref[...].astype(o_ref.dtype)


def logits_of(embed, mask_feat, tile_rows, tile_cols):
    images, queries, width = embed.shape
    pixels = mask_feat.shape[1]
    return pl.pallas_call(
        logits_kernel,
        grid=(images,),
        in_specs=[
            pl.BlockSpec((1, queries, width), lambda i: (i, 0, 0)),
            pl.BlockSpec((1, pixels, width), lambda i: (i, 0, 0)),
        ],
        out_specs=pl.BlockSpec((1, queries * tile_rows, tile_cols), lambda i: (i, 0, 0)),
        out_shape=jax.ShapeDtypeStruct((images, queries * tile_rows, tile_cols), jnp.bfloat16),
        scratch_shapes=[pltpu.VMEM((queries * tile_rows, tile_cols), jnp.float32)],
    )(embed, mask_feat)


def conv_with_halo(features, weight):
    images, tile_rows, tile_cols, width = features.shape
    dims = ("NHWC", "HWIO", "NHWC")
    conv = lambda x, w, pad: lax.conv_general_dilated(
        x, w, (1, 1), pad, dimension_numbers=dims, preferred_element_type=jnp.float32
    )
    main = conv(features, weight, ((1, 1), (1, 1)))
    rows = lax.axis_size("rows")
    cols = lax.axis_size("cols")
    down = [(i, i + 1) for i in range(rows - 1)]
    up = [(i + 1, i) for i in range(rows - 1)]
    rightward = [(i, i + 1) for i in range(cols - 1)]
    leftward = [(i + 1, i) for i in range(cols - 1)]
    above = lax.ppermute(features[:, -1:], "rows", down)
    below = lax.ppermute(features[:, :1], "rows", up)
    left = lax.ppermute(features[:, :, -1:], "cols", rightward)
    right = lax.ppermute(features[:, :, :1], "cols", leftward)
    edges = jnp.concatenate([above, below], axis=1)
    west = lax.ppermute(edges[:, :, -1:], "cols", rightward)
    east = lax.ppermute(edges[:, :, :1], "cols", leftward)
    above = jnp.concatenate([west[:, :1], above, east[:, :1]], axis=2)
    below = jnp.concatenate([west[:, 1:], below, east[:, 1:]], axis=2)
    valid = ((0, 0), (0, 0))
    column = ((1, 1), (0, 0))
    row_terms = jnp.concatenate(
        [
            conv(above, weight[0:1], valid),
            jnp.zeros((images, tile_rows - 2, tile_cols, width), jnp.float32),
            conv(below, weight[2:3], valid),
        ],
        axis=1,
    )
    col_terms = jnp.concatenate(
        [
            conv(left, weight[:, 0:1], column),
            jnp.zeros((images, tile_rows, tile_cols - 2, width), jnp.float32),
            conv(right, weight[:, 2:3], column),
        ],
        axis=2,
    )
    return main + row_terms + col_terms


def on_device(
    features,
    masks,
    queries,
    conv_weight,
    gn_gain,
    gn_bias,
    query_weight,
    key_weight,
    value_weight,
    out_weight,
    ln_gain,
    ln_bias,
    embed_one,
    embed_two,
):
    images, tile_rows, tile_cols, width = features.shape
    query_count = queries.shape[1]
    heads = HEADS
    head_size = width // heads
    pixels = tile_rows * tile_cols
    devices = lax.axis_size("rows") * lax.axis_size("cols")
    fg, local_count = prep(masks)
    conv = conv_with_halo(features, conv_weight)
    grouped = conv.reshape(images, pixels, GROUPS, width // GROUPS)
    first_sum = jnp.sum(grouped, axis=(1, 3))
    second_sum = jnp.sum(grouped * grouped, axis=(1, 3))
    stats = jnp.concatenate([local_count[..., 0], first_sum, second_sum], axis=1).reshape(1, -1)
    stats = lax.all_to_all(
        jnp.broadcast_to(stats, (devices, stats.shape[1])), ("rows", "cols"), 0, 0, tiled=True
    )
    stats = jnp.sum(stats, axis=0).reshape(images, -1)
    count = stats[:, :query_count]
    first_sum = stats[:, query_count : query_count + GROUPS]
    second_sum = stats[:, query_count + GROUPS :]
    number = devices * pixels * (width // GROUPS)
    mean = first_sum / number
    var = second_sum / number - mean * mean
    normed = (grouped - mean[:, None, :, None]) / jnp.sqrt(var[:, None, :, None] + 1e-05)
    mask_feat = jax.nn.relu(normed.reshape(images, pixels, width) * gn_gain + gn_bias).astype(
        jnp.bfloat16
    )
    keys = jnp.dot(mask_feat, key_weight, preferred_element_type=jnp.float32).astype(jnp.bfloat16)
    vals = jnp.dot(mask_feat, value_weight, preferred_element_type=jnp.float32).astype(jnp.bfloat16)
    qproj = jnp.dot(
        queries.astype(jnp.bfloat16), query_weight, preferred_element_type=jnp.float32
    ).astype(jnp.bfloat16)
    zero = (count == 0.0).astype(jnp.float32)[:, :, None]
    head_of_lane = jnp.arange(width) // head_size
    qbd = jnp.where(
        head_of_lane[None, None, None, :] == jnp.arange(heads)[None, :, None, None],
        qproj[:, None, :, :],
        jnp.zeros((), jnp.bfloat16),
    ).reshape(images, heads * query_count, width)
    top, total, weighted = attention(qbd, keys, vals, fg, zero, heads, 1.0 / head_size**0.5)
    span = images * query_count * width // devices
    packed = jnp.concatenate(
        [
            weighted.reshape(devices, span),
            total.reshape(devices, span // 32),
            top.reshape(devices, span // 32),
        ],
        axis=1,
    )
    parts = lax.all_to_all(packed, ("rows", "cols"), 0, 0, tiled=True)
    sums, totals, tops = split_parts(parts, span)
    highest = jnp.max(tops, axis=0, keepdims=True)
    factor = jnp.exp(tops - highest)
    totals = jnp.sum(totals * factor, axis=0, keepdims=True)
    sums = jnp.sum(sums * jnp.repeat(factor, 32, axis=1), axis=0, keepdims=True)
    attn_block = (sums / jnp.repeat(totals, 32, axis=1)).astype(jnp.bfloat16)
    attn = lax.all_to_all(
        jnp.broadcast_to(attn_block, (devices, span)), ("rows", "cols"), 0, 0, tiled=True
    ).reshape(images, query_count, width)
    mixed = queries + jnp.dot(attn, out_weight, preferred_element_type=jnp.float32)
    centre = jnp.mean(mixed, axis=2, keepdims=True)
    spread = jnp.mean((mixed - centre) ** 2, axis=2, keepdims=True)
    updated = (mixed - centre) / jnp.sqrt(spread + 1e-05) * ln_gain + ln_bias
    hidden = jax.nn.relu(
        jnp.dot(updated.astype(jnp.bfloat16), embed_one, preferred_element_type=jnp.float32)
    ).astype(jnp.bfloat16)
    embed = jnp.dot(hidden, embed_two, preferred_element_type=jnp.float32).astype(jnp.bfloat16)
    logits = logits_of(embed, mask_feat, tile_rows, tile_cols)
    return (updated, logits.reshape(images, query_count, tile_rows, tile_cols))


def solution(mesh):
    return jax.shard_map(
        on_device,
        mesh=mesh,
        in_specs=(
            P(None, "rows", "cols", None),
            P(None, None, "rows", "cols"),
            P(),
            P(),
            P(),
            P(),
            P(),
            P(),
            P(),
            P(),
            P(),
            P(),
            P(),
            P(),
        ),
        out_specs=(P(), P(None, None, "rows", "cols")),
        check_vma=False,
    )
```

```python
import jax
import jax.numpy as jnp
from jax import lax
from jax.experimental import pallas as pl
from jax.experimental.pallas import tpu as pltpu
from jax.sharding import PartitionSpec as P

HEADS = 8
GROUPS = 32
NEG = -1e30


def with_halo(cells, sides, width):
    for axis, dim in sides:
        count = lax.axis_size(axis)
        ends = count - 1
        head = lax.slice_in_dim(cells, 0, width, axis=dim)
        tail = lax.slice_in_dim(cells, cells.shape[dim] - width, cells.shape[dim], axis=dim)
        cells = jnp.concatenate(
            [
                lax.ppermute(tail, axis, [(i, (i + 1) % count) for i in range(ends)]),
                cells,
                lax.ppermute(head, axis, [((i + 1) % count, i) for i in range(ends)]),
            ],
            axis=dim,
        )
    return cells


def butterfly_sum(x):
    for axis in ("cols", "rows"):
        n = lax.axis_size(axis)
        if n & (n - 1):
            x = jax.tree.map(lambda v: lax.psum(v, axis), x)
            continue
        k = 1
        while k < n:
            got = lax.ppermute(x, axis, [(i, i ^ k) for i in range(n)])
            x = jax.tree.map(lambda a, b: a + b, x, got)
            k *= 2
    return x


def split_parts(x, span):
    return x[:, :span], x[:, span : span + span // 32], x[:, span + span // 32 :]


def merge(a, b, span):
    wa, ta, ma = split_parts(a, span)
    wb, tb, mb = split_parts(b, span)
    m = jnp.maximum(ma, mb)
    fa = jnp.exp(ma - m)
    fb = jnp.exp(mb - m)
    t = ta * fa + tb * fb
    w = wa * jnp.repeat(fa, 32, axis=1) + wb * jnp.repeat(fb, 32, axis=1)
    return jnp.concatenate([w, t, m], axis=1)


def halving_merge(x, span):
    for axis in ("cols", "rows"):
        n = lax.axis_size(axis)
        idx = lax.axis_index(axis)
        k = n // 2
        while k >= 1:
            h = x.shape[0] // 2
            lo, hi = x[:h], x[h:]
            upper = (idx // k) % 2 == 1
            keep = jnp.where(upper, hi, lo)
            send = jnp.where(upper, lo, hi)
            got = lax.ppermute(send, axis, [(i, i ^ k) for i in range(n)])
            x = merge(keep, got, span)
            k //= 2
    return x


def doubling_gather(a):
    for axis in ("rows", "cols"):
        n = lax.axis_size(axis)
        idx = lax.axis_index(axis)
        k = 1
        while k < n:
            got = lax.ppermute(a, axis, [(i, i ^ k) for i in range(n)])
            upper = (idx // k) % 2 == 1
            a = jnp.where(upper, jnp.concatenate([got, a]), jnp.concatenate([a, got]))
            k *= 2
    return a


def prep_kernel(m_ref, fg_ref, cnt_ref):
    queries = fg_ref.shape[1]
    tile_rows = m_ref.shape[1] // queries
    tile_cols = m_ref.shape[2]
    acc = jnp.zeros((queries, tile_cols), jnp.float32)
    for r in range(tile_rows):
        rows = m_ref[0, pl.ds(r, queries, stride=tile_rows), :]
        fg = (rows == 1).astype(jnp.float32)
        acc = acc + fg
        fg_ref[0, :, r * tile_cols : (r + 1) * tile_cols] = fg.astype(jnp.bfloat16)
    cnt_ref[0] = jnp.sum(acc, axis=1, keepdims=True)


def prep(masks):
    images, queries, tile_rows, tile_cols = masks.shape
    flat = masks.reshape(images, queries * tile_rows, tile_cols)
    return pl.pallas_call(
        prep_kernel,
        grid=(images,),
        in_specs=[pl.BlockSpec((1, queries * tile_rows, tile_cols), lambda i: (i, 0, 0))],
        out_specs=[
            pl.BlockSpec((1, queries, tile_rows * tile_cols), lambda i: (i, 0, 0)),
            pl.BlockSpec((1, queries, 1), lambda i: (i, 0, 0)),
        ],
        out_shape=[
            jax.ShapeDtypeStruct((images, queries, tile_rows * tile_cols), jnp.bfloat16),
            jax.ShapeDtypeStruct((images, queries, 1), jnp.float32),
        ],
    )(flat)


def attention_kernel(q_ref, k_ref, v_ref, fg_ref, zero_ref, top_ref, tot_ref, wv_ref, *, heads, scale):
    queries = fg_ref.shape[1]
    width = k_ref.shape[2]
    head_size = width // heads
    k = k_ref[0]
    v = v_ref[0]
    allowed = (fg_ref[0] != 0) | (zero_ref[0] != 0)
    bias = jnp.where(allowed, 0.0, -jnp.inf)
    lane = lax.broadcasted_iota(jnp.int32, (queries, width), 1)
    acc = jnp.zeros((queries, width), jnp.float32)
    for h in range(heads):
        q = q_ref[0, h * queries : (h + 1) * queries, :]
        s = lax.dot_general(q, k, (((1,), (1,)), ((), ())), preferred_element_type=jnp.float32) * scale
        top = jnp.maximum(jnp.max(s + bias, axis=1, keepdims=True), NEG)
        w = jnp.exp(s + bias - top).astype(jnp.bfloat16)
        tot_ref[0, :, h : h + 1] = jnp.sum(w.astype(jnp.float32), axis=1, keepdims=True)
        top_ref[0, :, h : h + 1] = top
        r = jnp.dot(w, v, preferred_element_type=jnp.float32)
        inside = (lane >= h * head_size) & (lane < (h + 1) * head_size)
        acc = acc + jnp.where(inside, r, 0.0)
    wv_ref[0] = acc


def attention(qbd, keys, vals, fg, zero, heads, scale):
    images, pixels, width = keys.shape
    queries = fg.shape[1]
    kernel = lambda *refs: attention_kernel(*refs, heads=heads, scale=scale)
    return pl.pallas_call(
        kernel,
        grid=(images,),
        in_specs=[
            pl.BlockSpec((1, heads * queries, width), lambda i: (i, 0, 0)),
            pl.BlockSpec((1, pixels, width), lambda i: (i, 0, 0)),
            pl.BlockSpec((1, pixels, width), lambda i: (i, 0, 0)),
            pl.BlockSpec((1, queries, pixels), lambda i: (i, 0, 0)),
            pl.BlockSpec((1, queries, 1), lambda i: (i, 0, 0)),
        ],
        out_specs=[
            pl.BlockSpec((1, queries, heads), lambda i: (i, 0, 0)),
            pl.BlockSpec((1, queries, heads), lambda i: (i, 0, 0)),
            pl.BlockSpec((1, queries, width), lambda i: (i, 0, 0)),
        ],
        out_shape=[
            jax.ShapeDtypeStruct((images, queries, heads), jnp.float32),
            jax.ShapeDtypeStruct((images, queries, heads), jnp.float32),
            jax.ShapeDtypeStruct((images, queries, width), jnp.float32),
        ],
    )(qbd, keys, vals, fg, zero)


def logits_kernel(e_ref, f_ref, o_ref, acc_ref):
    queries = e_ref.shape[1]
    tile_cols = o_ref.shape[2]
    tile_rows = o_ref.shape[1] // queries
    e = e_ref[0]
    for r in range(tile_rows):
        f = f_ref[0, r * tile_cols : (r + 1) * tile_cols, :]
        res = lax.dot_general(e, f, (((1,), (1,)), ((), ())), preferred_element_type=jnp.float32)
        acc_ref[pl.ds(r, queries, stride=tile_rows), :] = res
    o_ref[0] = acc_ref[...].astype(o_ref.dtype)


def logits_of(embed, mask_feat, tile_rows, tile_cols):
    images, queries, width = embed.shape
    pixels = mask_feat.shape[1]
    return pl.pallas_call(
        logits_kernel,
        grid=(images,),
        in_specs=[
            pl.BlockSpec((1, queries, width), lambda i: (i, 0, 0)),
            pl.BlockSpec((1, pixels, width), lambda i: (i, 0, 0)),
        ],
        out_specs=pl.BlockSpec((1, queries * tile_rows, tile_cols), lambda i: (i, 0, 0)),
        out_shape=jax.ShapeDtypeStruct((images, queries * tile_rows, tile_cols), jnp.bfloat16),
        scratch_shapes=[pltpu.VMEM((queries * tile_rows, tile_cols), jnp.float32)],
    )(embed, mask_feat)


def conv_with_halo(features, weight):
    images, tile_rows, tile_cols, width = features.shape
    dims = ("NHWC", "HWIO", "NHWC")
    conv = lambda x, w, pad: lax.conv_general_dilated(
        x, w, (1, 1), pad, dimension_numbers=dims, preferred_element_type=jnp.float32
    )
    main = lax.optimization_barrier(conv(features, weight, ((1, 1), (1, 1))))
    rows = lax.axis_size("rows")
    cols = lax.axis_size("cols")
    down = [(i, i + 1) for i in range(rows - 1)]
    up = [(i + 1, i) for i in range(rows - 1)]
    rightward = [(i, i + 1) for i in range(cols - 1)]
    leftward = [(i + 1, i) for i in range(cols - 1)]
    above = lax.ppermute(features[:, -1:], "rows", down)
    below = lax.ppermute(features[:, :1], "rows", up)
    left = lax.ppermute(features[:, :, -1:], "cols", rightward)
    right = lax.ppermute(features[:, :, :1], "cols", leftward)
    edges = jnp.concatenate([above, below], axis=1)
    west = lax.ppermute(edges[:, :, -1:], "cols", rightward)
    east = lax.ppermute(edges[:, :, :1], "cols", leftward)
    above = jnp.concatenate([west[:, :1], above, east[:, :1]], axis=2)
    below = jnp.concatenate([west[:, 1:], below, east[:, 1:]], axis=2)
    valid = ((0, 0), (0, 0))
    column = ((1, 1), (0, 0))
    row_terms = jnp.concatenate(
        [
            conv(above, weight[0:1], valid),
            jnp.zeros((images, tile_rows - 2, tile_cols, width), jnp.float32),
            conv(below, weight[2:3], valid),
        ],
        axis=1,
    )
    col_terms = jnp.concatenate(
        [
            conv(left, weight[:, 0:1], column),
            jnp.zeros((images, tile_rows, tile_cols - 2, width), jnp.float32),
            conv(right, weight[:, 2:3], column),
        ],
        axis=2,
    )
    return main + row_terms + col_terms


def on_device(
    features,
    masks,
    queries,
    conv_weight,
    gn_gain,
    gn_bias,
    query_weight,
    key_weight,
    value_weight,
    out_weight,
    ln_gain,
    ln_bias,
    embed_one,
    embed_two,
):
    images, tile_rows, tile_cols, width = features.shape
    query_count = queries.shape[1]
    heads = HEADS
    head_size = width // heads
    pixels = tile_rows * tile_cols
    devices = lax.axis_size("rows") * lax.axis_size("cols")
    fg, local_count = prep(masks)
    conv = conv_with_halo(features, conv_weight)
    grouped = conv.reshape(images, pixels, GROUPS, width // GROUPS)
    first_sum = jnp.sum(grouped, axis=(1, 3))
    second_sum = jnp.sum(grouped * grouped, axis=(1, 3))
    stats = jnp.concatenate([local_count[..., 0], first_sum, second_sum], axis=1).reshape(1, -1)
    stats = lax.all_to_all(
        jnp.broadcast_to(stats, (devices, stats.shape[1])), ("rows", "cols"), 0, 0, tiled=True
    )
    stats = jnp.sum(stats, axis=0).reshape(images, -1)
    count = stats[:, :query_count]
    first_sum = stats[:, query_count : query_count + GROUPS]
    second_sum = stats[:, query_count + GROUPS :]
    number = devices * pixels * (width // GROUPS)
    mean = first_sum / number
    var = second_sum / number - mean * mean
    normed = (grouped - mean[:, None, :, None]) / jnp.sqrt(var[:, None, :, None] + 1e-05)
    mask_feat = jax.nn.relu(normed.reshape(images, pixels, width) * gn_gain + gn_bias).astype(
        jnp.bfloat16
    )
    keys = jnp.dot(mask_feat, key_weight, preferred_element_type=jnp.float32).astype(jnp.bfloat16)
    vals = jnp.dot(mask_feat, value_weight, preferred_element_type=jnp.float32).astype(jnp.bfloat16)
    qproj = jnp.dot(
        queries.astype(jnp.bfloat16), query_weight, preferred_element_type=jnp.float32
    ).astype(jnp.bfloat16)
    zero = (count == 0.0).astype(jnp.float32)[:, :, None]
    head_of_lane = jnp.arange(width) // head_size
    qbd = jnp.where(
        head_of_lane[None, None, None, :] == jnp.arange(heads)[None, :, None, None],
        qproj[:, None, :, :],
        jnp.zeros((), jnp.bfloat16),
    ).reshape(images, heads * query_count, width)
    top, total, weighted = attention(qbd, keys, vals, fg, zero, heads, 1.0 / head_size**0.5)
    span = images * query_count * width // devices
    packed = jnp.concatenate(
        [
            weighted.reshape(devices, span),
            total.reshape(devices, span // 32),
            top.reshape(devices, span // 32),
        ],
        axis=1,
    )
    parts = lax.all_to_all(packed, ("rows", "cols"), 0, 0, tiled=True)
    sums, totals, tops = split_parts(parts, span)
    highest = jnp.max(tops, axis=0, keepdims=True)
    factor = jnp.exp(tops - highest)
    totals = jnp.sum(totals * factor, axis=0, keepdims=True)
    sums = jnp.sum(sums * jnp.repeat(factor, 32, axis=1), axis=0, keepdims=True)
    attn_block = (sums / jnp.repeat(totals, 32, axis=1)).astype(jnp.bfloat16)
    attn = lax.all_to_all(
        jnp.broadcast_to(attn_block, (devices, span)), ("rows", "cols"), 0, 0, tiled=True
    ).reshape(images, query_count, width)
    mixed = queries + jnp.dot(attn, out_weight, preferred_element_type=jnp.float32)
    centre = jnp.mean(mixed, axis=2, keepdims=True)
    spread = jnp.mean((mixed - centre) ** 2, axis=2, keepdims=True)
    updated = (mixed - centre) / jnp.sqrt(spread + 1e-05) * ln_gain + ln_bias
    hidden = jax.nn.relu(
        jnp.dot(updated.astype(jnp.bfloat16), embed_one, preferred_element_type=jnp.float32)
    ).astype(jnp.bfloat16)
    embed = jnp.dot(hidden, embed_two, preferred_element_type=jnp.float32).astype(jnp.bfloat16)
    logits = logits_of(embed, mask_feat, tile_rows, tile_cols)
    return (updated, logits.reshape(images, query_count, tile_rows, tile_cols))


def solution(mesh):
    return jax.shard_map(
        on_device,
        mesh=mesh,
        in_specs=(
            P(None, "rows", "cols", None),
            P(None, None, "rows", "cols"),
            P(),
            P(),
            P(),
            P(),
            P(),
            P(),
            P(),
            P(),
            P(),
            P(),
            P(),
            P(),
        ),
        out_specs=(P(), P(None, None, "rows", "cols")),
        check_vma=False,
    )
```

```python
import jax
import jax.numpy as jnp
from jax import lax
from jax.experimental import pallas as pl
from jax.experimental.pallas import tpu as pltpu
from jax.sharding import PartitionSpec as P

HEADS = 8
GROUPS = 32
NEG = -1e30


def with_halo(cells, sides, width):
    for axis, dim in sides:
        count = lax.axis_size(axis)
        ends = count - 1
        head = lax.slice_in_dim(cells, 0, width, axis=dim)
        tail = lax.slice_in_dim(cells, cells.shape[dim] - width, cells.shape[dim], axis=dim)
        cells = jnp.concatenate(
            [
                lax.ppermute(tail, axis, [(i, (i + 1) % count) for i in range(ends)]),
                cells,
                lax.ppermute(head, axis, [((i + 1) % count, i) for i in range(ends)]),
            ],
            axis=dim,
        )
    return cells


def butterfly_sum(x):
    for axis in ("cols", "rows"):
        n = lax.axis_size(axis)
        if n & (n - 1):
            x = jax.tree.map(lambda v: lax.psum(v, axis), x)
            continue
        k = 1
        while k < n:
            got = lax.ppermute(x, axis, [(i, i ^ k) for i in range(n)])
            x = jax.tree.map(lambda a, b: a + b, x, got)
            k *= 2
    return x


def split_parts(x, span):
    return x[:, :span], x[:, span : span + span // 32], x[:, span + span // 32 :]


def merge(a, b, span):
    wa, ta, ma = split_parts(a, span)
    wb, tb, mb = split_parts(b, span)
    m = jnp.maximum(ma, mb)
    fa = jnp.exp(ma - m)
    fb = jnp.exp(mb - m)
    t = ta * fa + tb * fb
    w = wa * jnp.repeat(fa, 32, axis=1) + wb * jnp.repeat(fb, 32, axis=1)
    return jnp.concatenate([w, t, m], axis=1)


def halving_merge(x, span):
    for axis in ("cols", "rows"):
        n = lax.axis_size(axis)
        idx = lax.axis_index(axis)
        k = n // 2
        while k >= 1:
            h = x.shape[0] // 2
            lo, hi = x[:h], x[h:]
            upper = (idx // k) % 2 == 1
            keep = jnp.where(upper, hi, lo)
            send = jnp.where(upper, lo, hi)
            got = lax.ppermute(send, axis, [(i, i ^ k) for i in range(n)])
            x = merge(keep, got, span)
            k //= 2
    return x


def doubling_gather(a):
    for axis in ("rows", "cols"):
        n = lax.axis_size(axis)
        idx = lax.axis_index(axis)
        k = 1
        while k < n:
            got = lax.ppermute(a, axis, [(i, i ^ k) for i in range(n)])
            upper = (idx // k) % 2 == 1
            a = jnp.where(upper, jnp.concatenate([got, a]), jnp.concatenate([a, got]))
            k *= 2
    return a


def count_kernel(m_ref, cnt_ref):
    queries = cnt_ref.shape[1]
    tile_rows = m_ref.shape[1] // queries
    acc = jnp.zeros((queries, m_ref.shape[2]), jnp.float32)
    for r in range(tile_rows):
        acc = acc + (m_ref[0, pl.ds(r, queries, stride=tile_rows), :] == 1).astype(jnp.float32)
    cnt_ref[0] = jnp.sum(acc, axis=1, keepdims=True)


def count_of(flat, queries):
    images, rows, tile_cols = flat.shape
    return pl.pallas_call(
        count_kernel,
        grid=(images,),
        in_specs=[pl.BlockSpec((1, rows, tile_cols), lambda i: (i, 0, 0))],
        out_specs=pl.BlockSpec((1, queries, 1), lambda i: (i, 0, 0)),
        out_shape=jax.ShapeDtypeStruct((images, queries, 1), jnp.float32),
    )(flat)


def attention_kernel(q_ref, k_ref, v_ref, m_ref, zero_ref, top_ref, tot_ref, wv_ref, bias_ref, *, heads, scale):
    queries = zero_ref.shape[1]
    width = k_ref.shape[2]
    head_size = width // heads
    tile_rows = m_ref.shape[1] // queries
    tile_cols = m_ref.shape[2]
    k = k_ref[0]
    v = v_ref[0]
    empty = zero_ref[0] != 0
    for r in range(tile_rows):
        allowed = (m_ref[0, pl.ds(r, queries, stride=tile_rows), :] == 1) | empty
        bias_ref[:, r * tile_cols : (r + 1) * tile_cols] = jnp.where(allowed, 0.0, -jnp.inf)
    bias = bias_ref[...]
    lane = lax.broadcasted_iota(jnp.int32, (queries, width), 1)
    acc = jnp.zeros((queries, width), jnp.float32)
    for h in range(heads):
        q = q_ref[0, h * queries : (h + 1) * queries, :]
        s = lax.dot_general(q, k, (((1,), (1,)), ((), ())), preferred_element_type=jnp.float32) * scale
        top = jnp.maximum(jnp.max(s + bias, axis=1, keepdims=True), NEG)
        w = jnp.exp(s + bias - top).astype(jnp.bfloat16)
        tot_ref[0, :, h : h + 1] = jnp.sum(w.astype(jnp.float32), axis=1, keepdims=True)
        top_ref[0, :, h : h + 1] = top
        r = jnp.dot(w, v, preferred_element_type=jnp.float32)
        inside = (lane >= h * head_size) & (lane < (h + 1) * head_size)
        acc = acc + jnp.where(inside, r, 0.0)
    wv_ref[0] = acc


def attention(qbd, keys, vals, flat, zero, heads, scale):
    images, pixels, width = keys.shape
    queries = zero.shape[1]
    kernel = lambda *refs: attention_kernel(*refs, heads=heads, scale=scale)
    return pl.pallas_call(
        kernel,
        grid=(images,),
        in_specs=[
            pl.BlockSpec((1, heads * queries, width), lambda i: (i, 0, 0)),
            pl.BlockSpec((1, pixels, width), lambda i: (i, 0, 0)),
            pl.BlockSpec((1, pixels, width), lambda i: (i, 0, 0)),
            pl.BlockSpec((1,) + flat.shape[1:], lambda i: (i, 0, 0)),
            pl.BlockSpec((1, queries, 1), lambda i: (i, 0, 0)),
        ],
        out_specs=[
            pl.BlockSpec((1, queries, heads), lambda i: (i, 0, 0)),
            pl.BlockSpec((1, queries, heads), lambda i: (i, 0, 0)),
            pl.BlockSpec((1, queries, width), lambda i: (i, 0, 0)),
        ],
        out_shape=[
            jax.ShapeDtypeStruct((images, queries, heads), jnp.float32),
            jax.ShapeDtypeStruct((images, queries, heads), jnp.float32),
            jax.ShapeDtypeStruct((images, queries, width), jnp.float32),
        ],
        scratch_shapes=[pltpu.VMEM((queries, pixels), jnp.float32)],
    )(qbd, keys, vals, flat, zero)


def logits_kernel(e_ref, f_ref, o_ref, acc_ref):
    queries = e_ref.shape[1]
    tile_cols = o_ref.shape[2]
    tile_rows = o_ref.shape[1] // queries
    e = e_ref[0]
    for r in range(tile_rows):
        f = f_ref[0, r * tile_cols : (r + 1) * tile_cols, :]
        res = lax.dot_general(e, f, (((1,), (1,)), ((), ())), preferred_element_type=jnp.float32)
        acc_ref[pl.ds(r, queries, stride=tile_rows), :] = res
    o_ref[0] = acc_ref[...].astype(o_ref.dtype)


def logits_of(embed, mask_feat, tile_rows, tile_cols):
    images, queries, width = embed.shape
    pixels = mask_feat.shape[1]
    return pl.pallas_call(
        logits_kernel,
        grid=(images,),
        in_specs=[
            pl.BlockSpec((1, queries, width), lambda i: (i, 0, 0)),
            pl.BlockSpec((1, pixels, width), lambda i: (i, 0, 0)),
        ],
        out_specs=pl.BlockSpec((1, queries * tile_rows, tile_cols), lambda i: (i, 0, 0)),
        out_shape=jax.ShapeDtypeStruct((images, queries * tile_rows, tile_cols), jnp.bfloat16),
        scratch_shapes=[pltpu.VMEM((queries * tile_rows, tile_cols), jnp.float32)],
    )(embed, mask_feat)


def on_device(
    features,
    masks,
    queries,
    conv_weight,
    gn_gain,
    gn_bias,
    query_weight,
    key_weight,
    value_weight,
    out_weight,
    ln_gain,
    ln_bias,
    embed_one,
    embed_two,
):
    images, tile_rows, tile_cols, width = features.shape
    query_count = queries.shape[1]
    heads = HEADS
    head_size = width // heads
    pixels = tile_rows * tile_cols
    devices = lax.axis_size("rows") * lax.axis_size("cols")
    flat_masks = masks.reshape(images, query_count * tile_rows, tile_cols)
    local_count = count_of(flat_masks, query_count)
    padded = with_halo(features, (("rows", 1), ("cols", 2)), 1)
    conv = lax.conv_general_dilated(
        padded,
        conv_weight,
        (1, 1),
        "VALID",
        dimension_numbers=("NHWC", "HWIO", "NHWC"),
        preferred_element_type=jnp.float32,
    )
    grouped = conv.reshape(images, pixels, GROUPS, width // GROUPS)
    first_sum = jnp.sum(grouped, axis=(1, 3))
    second_sum = jnp.sum(grouped * grouped, axis=(1, 3))
    stats = jnp.concatenate([local_count[..., 0], first_sum, second_sum], axis=1).reshape(1, -1)
    stats = lax.all_to_all(
        jnp.broadcast_to(stats, (devices, stats.shape[1])), ("rows", "cols"), 0, 0, tiled=True
    )
    stats = jnp.sum(stats, axis=0).reshape(images, -1)
    count = stats[:, :query_count]
    first_sum = stats[:, query_count : query_count + GROUPS]
    second_sum = stats[:, query_count + GROUPS :]
    number = devices * pixels * (width // GROUPS)
    mean = first_sum / number
    var = second_sum / number - mean * mean
    normed = (grouped - mean[:, None, :, None]) / jnp.sqrt(var[:, None, :, None] + 1e-05)
    mask_feat = jax.nn.relu(normed.reshape(images, pixels, width) * gn_gain + gn_bias).astype(
        jnp.bfloat16
    )
    keys = jnp.dot(mask_feat, key_weight, preferred_element_type=jnp.float32).astype(jnp.bfloat16)
    vals = jnp.dot(mask_feat, value_weight, preferred_element_type=jnp.float32).astype(jnp.bfloat16)
    qproj = jnp.dot(
        queries.astype(jnp.bfloat16), query_weight, preferred_element_type=jnp.float32
    ).astype(jnp.bfloat16)
    zero = (count == 0.0).astype(jnp.float32)[:, :, None]
    head_of_lane = jnp.arange(width) // head_size
    qbd = jnp.where(
        head_of_lane[None, None, None, :] == jnp.arange(heads)[None, :, None, None],
        qproj[:, None, :, :],
        jnp.zeros((), jnp.bfloat16),
    ).reshape(images, heads * query_count, width)
    top, total, weighted = attention(qbd, keys, vals, flat_masks, zero, heads, 1.0 / head_size**0.5)
    span = images * query_count * width // devices
    packed = jnp.concatenate(
        [
            weighted.reshape(devices, span),
            total.reshape(devices, span // 32),
            top.reshape(devices, span // 32),
        ],
        axis=1,
    )
    parts = lax.all_to_all(packed, ("rows", "cols"), 0, 0, tiled=True)
    sums, totals, tops = split_parts(parts, span)
    highest = jnp.max(tops, axis=0, keepdims=True)
    factor = jnp.exp(tops - highest)
    totals = jnp.sum(totals * factor, axis=0, keepdims=True)
    sums = jnp.sum(sums * jnp.repeat(factor, 32, axis=1), axis=0, keepdims=True)
    attn_block = (sums / jnp.repeat(totals, 32, axis=1)).astype(jnp.bfloat16)
    attn = lax.all_to_all(
        jnp.broadcast_to(attn_block, (devices, span)), ("rows", "cols"), 0, 0, tiled=True
    ).reshape(images, query_count, width)
    mixed = queries + jnp.dot(attn, out_weight, preferred_element_type=jnp.float32)
    centre = jnp.mean(mixed, axis=2, keepdims=True)
    spread = jnp.mean((mixed - centre) ** 2, axis=2, keepdims=True)
    updated = (mixed - centre) / jnp.sqrt(spread + 1e-05) * ln_gain + ln_bias
    hidden = jax.nn.relu(
        jnp.dot(updated.astype(jnp.bfloat16), embed_one, preferred_element_type=jnp.float32)
    ).astype(jnp.bfloat16)
    embed = jnp.dot(hidden, embed_two, preferred_element_type=jnp.float32).astype(jnp.bfloat16)
    logits = logits_of(embed, mask_feat, tile_rows, tile_cols)
    return (updated, logits.reshape(images, query_count, tile_rows, tile_cols))


def solution(mesh):
    return jax.shard_map(
        on_device,
        mesh=mesh,
        in_specs=(
            P(None, "rows", "cols", None),
            P(None, None, "rows", "cols"),
            P(),
            P(),
            P(),
            P(),
            P(),
            P(),
            P(),
            P(),
            P(),
            P(),
            P(),
            P(),
        ),
        out_specs=(P(), P(None, None, "rows", "cols")),
        check_vma=False,
    )
```

```python
import jax
import jax.numpy as jnp
from jax import lax
from jax.experimental import pallas as pl
from jax.experimental.pallas import tpu as pltpu
from jax.sharding import PartitionSpec as P

HEADS = 8
GROUPS = 32
NEG = -1e30


def with_halo(cells, sides, width):
    for axis, dim in sides:
        count = lax.axis_size(axis)
        ends = count - 1
        head = lax.slice_in_dim(cells, 0, width, axis=dim)
        tail = lax.slice_in_dim(cells, cells.shape[dim] - width, cells.shape[dim], axis=dim)
        cells = jnp.concatenate(
            [
                lax.ppermute(tail, axis, [(i, (i + 1) % count) for i in range(ends)]),
                cells,
                lax.ppermute(head, axis, [((i + 1) % count, i) for i in range(ends)]),
            ],
            axis=dim,
        )
    return cells


def butterfly_sum(x):
    for axis in ("cols", "rows"):
        n = lax.axis_size(axis)
        if n & (n - 1):
            x = jax.tree.map(lambda v: lax.psum(v, axis), x)
            continue
        k = 1
        while k < n:
            got = lax.ppermute(x, axis, [(i, i ^ k) for i in range(n)])
            x = jax.tree.map(lambda a, b: a + b, x, got)
            k *= 2
    return x


def split_parts(x, span):
    return x[:, :span], x[:, span : span + span // 32], x[:, span + span // 32 :]


def merge(a, b, span):
    wa, ta, ma = split_parts(a, span)
    wb, tb, mb = split_parts(b, span)
    m = jnp.maximum(ma, mb)
    fa = jnp.exp(ma - m)
    fb = jnp.exp(mb - m)
    t = ta * fa + tb * fb
    w = wa * jnp.repeat(fa, 32, axis=1) + wb * jnp.repeat(fb, 32, axis=1)
    return jnp.concatenate([w, t, m], axis=1)


def halving_merge(x, span):
    for axis in ("cols", "rows"):
        n = lax.axis_size(axis)
        idx = lax.axis_index(axis)
        k = n // 2
        while k >= 1:
            h = x.shape[0] // 2
            lo, hi = x[:h], x[h:]
            upper = (idx // k) % 2 == 1
            keep = jnp.where(upper, hi, lo)
            send = jnp.where(upper, lo, hi)
            got = lax.ppermute(send, axis, [(i, i ^ k) for i in range(n)])
            x = merge(keep, got, span)
            k //= 2
    return x


def doubling_gather(a):
    for axis in ("rows", "cols"):
        n = lax.axis_size(axis)
        idx = lax.axis_index(axis)
        k = 1
        while k < n:
            got = lax.ppermute(a, axis, [(i, i ^ k) for i in range(n)])
            upper = (idx // k) % 2 == 1
            a = jnp.where(upper, jnp.concatenate([got, a]), jnp.concatenate([a, got]))
            k *= 2
    return a


def prep_kernel(m_ref, fg_ref, cnt_ref):
    queries = fg_ref.shape[1]
    tile_rows = m_ref.shape[1] // queries
    tile_cols = m_ref.shape[2]
    acc = jnp.zeros((queries, tile_cols), jnp.float32)
    for r in range(tile_rows):
        rows = m_ref[0, pl.ds(r, queries, stride=tile_rows), :]
        fg = (rows == 1).astype(jnp.float32)
        acc = acc + fg
        fg_ref[0, :, r * tile_cols : (r + 1) * tile_cols] = fg.astype(jnp.bfloat16)
    cnt_ref[0] = jnp.sum(acc, axis=1, keepdims=True)


def prep(masks):
    images, queries, tile_rows, tile_cols = masks.shape
    flat = masks.reshape(images, queries * tile_rows, tile_cols)
    return pl.pallas_call(
        prep_kernel,
        grid=(images,),
        in_specs=[pl.BlockSpec((1, queries * tile_rows, tile_cols), lambda i: (i, 0, 0))],
        out_specs=[
            pl.BlockSpec((1, queries, tile_rows * tile_cols), lambda i: (i, 0, 0)),
            pl.BlockSpec((1, queries, 1), lambda i: (i, 0, 0)),
        ],
        out_shape=[
            jax.ShapeDtypeStruct((images, queries, tile_rows * tile_cols), jnp.bfloat16),
            jax.ShapeDtypeStruct((images, queries, 1), jnp.float32),
        ],
    )(flat)


def attention_kernel(q_ref, k_ref, v_ref, fg_ref, zero_ref, top_ref, tot_ref, wv_ref, *, heads, scale):
    queries = fg_ref.shape[1]
    width = k_ref.shape[2]
    head_size = width // heads
    k = k_ref[0]
    v = v_ref[0]
    allowed = (fg_ref[0] != 0) | (zero_ref[0] != 0)
    bias = jnp.where(allowed, 0.0, -jnp.inf)
    lane = lax.broadcasted_iota(jnp.int32, (queries, width), 1)
    acc = jnp.zeros((queries, width), jnp.float32)
    for h in range(heads):
        q = q_ref[0, h * queries : (h + 1) * queries, :]
        s = lax.dot_general(q, k, (((1,), (1,)), ((), ())), preferred_element_type=jnp.float32) * scale
        top = jnp.maximum(jnp.max(s + bias, axis=1, keepdims=True), NEG)
        w = jnp.exp(s + bias - top).astype(jnp.bfloat16)
        tot_ref[0, :, h : h + 1] = jnp.sum(w.astype(jnp.float32), axis=1, keepdims=True)
        top_ref[0, :, h : h + 1] = top
        r = jnp.dot(w, v, preferred_element_type=jnp.float32)
        inside = (lane >= h * head_size) & (lane < (h + 1) * head_size)
        acc = acc + jnp.where(inside, r, 0.0)
    wv_ref[0] = acc


def attention(qbd, keys_vals, fg, zero, heads, scale):
    images, pixels, width = keys_vals.shape
    width //= 2
    queries = fg.shape[1]
    kernel = lambda *refs: attention_kernel(*refs, heads=heads, scale=scale)
    return pl.pallas_call(
        kernel,
        grid=(images,),
        in_specs=[
            pl.BlockSpec((1, heads * queries, width), lambda i: (i, 0, 0)),
            pl.BlockSpec((1, pixels, width), lambda i: (i, 0, 0)),
            pl.BlockSpec((1, pixels, width), lambda i: (i, 0, 1)),
            pl.BlockSpec((1, queries, pixels), lambda i: (i, 0, 0)),
            pl.BlockSpec((1, queries, 1), lambda i: (i, 0, 0)),
        ],
        out_specs=[
            pl.BlockSpec((1, queries, heads), lambda i: (i, 0, 0)),
            pl.BlockSpec((1, queries, heads), lambda i: (i, 0, 0)),
            pl.BlockSpec((1, queries, width), lambda i: (i, 0, 0)),
        ],
        out_shape=[
            jax.ShapeDtypeStruct((images, queries, heads), jnp.float32),
            jax.ShapeDtypeStruct((images, queries, heads), jnp.float32),
            jax.ShapeDtypeStruct((images, queries, width), jnp.float32),
        ],
    )(qbd, keys_vals, keys_vals, fg, zero)


def logits_kernel(e_ref, f_ref, o_ref, acc_ref):
    queries = e_ref.shape[1]
    tile_cols = o_ref.shape[2]
    tile_rows = o_ref.shape[1] // queries
    e = e_ref[0]
    for r in range(tile_rows):
        f = f_ref[0, r * tile_cols : (r + 1) * tile_cols, :]
        res = lax.dot_general(e, f, (((1,), (1,)), ((), ())), preferred_element_type=jnp.float32)
        acc_ref[pl.ds(r, queries, stride=tile_rows), :] = res
    o_ref[0] = acc_ref[...].astype(o_ref.dtype)


def logits_of(embed, mask_feat, tile_rows, tile_cols):
    images, queries, width = embed.shape
    pixels = mask_feat.shape[1]
    return pl.pallas_call(
        logits_kernel,
        grid=(images,),
        in_specs=[
            pl.BlockSpec((1, queries, width), lambda i: (i, 0, 0)),
            pl.BlockSpec((1, pixels, width), lambda i: (i, 0, 0)),
        ],
        out_specs=pl.BlockSpec((1, queries * tile_rows, tile_cols), lambda i: (i, 0, 0)),
        out_shape=jax.ShapeDtypeStruct((images, queries * tile_rows, tile_cols), jnp.bfloat16),
        scratch_shapes=[pltpu.VMEM((queries * tile_rows, tile_cols), jnp.float32)],
    )(embed, mask_feat)


def on_device(
    features,
    masks,
    queries,
    conv_weight,
    gn_gain,
    gn_bias,
    query_weight,
    key_weight,
    value_weight,
    out_weight,
    ln_gain,
    ln_bias,
    embed_one,
    embed_two,
):
    images, tile_rows, tile_cols, width = features.shape
    query_count = queries.shape[1]
    heads = HEADS
    head_size = width // heads
    pixels = tile_rows * tile_cols
    devices = lax.axis_size("rows") * lax.axis_size("cols")
    fg, local_count = prep(masks)
    padded = with_halo(features, (("rows", 1), ("cols", 2)), 1)
    conv = lax.conv_general_dilated(
        padded,
        conv_weight,
        (1, 1),
        "VALID",
        dimension_numbers=("NHWC", "HWIO", "NHWC"),
        preferred_element_type=jnp.float32,
    )
    grouped = conv.reshape(images, pixels, GROUPS, width // GROUPS)
    first_sum = jnp.sum(grouped, axis=(1, 3))
    second_sum = jnp.sum(grouped * grouped, axis=(1, 3))
    stats = jnp.concatenate([local_count[..., 0], first_sum, second_sum], axis=1).reshape(1, -1)
    stats = lax.all_to_all(
        jnp.broadcast_to(stats, (devices, stats.shape[1])), ("rows", "cols"), 0, 0, tiled=True
    )
    stats = jnp.sum(stats, axis=0).reshape(images, -1)
    count = stats[:, :query_count]
    first_sum = stats[:, query_count : query_count + GROUPS]
    second_sum = stats[:, query_count + GROUPS :]
    number = devices * pixels * (width // GROUPS)
    mean = first_sum / number
    var = second_sum / number - mean * mean
    normed = (grouped - mean[:, None, :, None]) / jnp.sqrt(var[:, None, :, None] + 1e-05)
    mask_feat = jax.nn.relu(normed.reshape(images, pixels, width) * gn_gain + gn_bias).astype(
        jnp.bfloat16
    )
    keys_vals = jnp.dot(
        mask_feat, jnp.concatenate([key_weight, value_weight], axis=1), preferred_element_type=jnp.float32
    ).astype(jnp.bfloat16)
    qproj = jnp.dot(
        queries.astype(jnp.bfloat16), query_weight, preferred_element_type=jnp.float32
    ).astype(jnp.bfloat16)
    zero = (count == 0.0).astype(jnp.float32)[:, :, None]
    head_of_lane = jnp.arange(width) // head_size
    qbd = jnp.where(
        head_of_lane[None, None, None, :] == jnp.arange(heads)[None, :, None, None],
        qproj[:, None, :, :],
        jnp.zeros((), jnp.bfloat16),
    ).reshape(images, heads * query_count, width)
    top, total, weighted = attention(qbd, keys_vals, fg, zero, heads, 1.0 / head_size**0.5)
    span = images * query_count * width // devices
    packed = jnp.concatenate(
        [
            weighted.reshape(devices, span),
            total.reshape(devices, span // 32),
            top.reshape(devices, span // 32),
        ],
        axis=1,
    )
    parts = lax.all_to_all(packed, ("rows", "cols"), 0, 0, tiled=True)
    sums, totals, tops = split_parts(parts, span)
    highest = jnp.max(tops, axis=0, keepdims=True)
    factor = jnp.exp(tops - highest)
    totals = jnp.sum(totals * factor, axis=0, keepdims=True)
    sums = jnp.sum(sums * jnp.repeat(factor, 32, axis=1), axis=0, keepdims=True)
    attn_block = (sums / jnp.repeat(totals, 32, axis=1)).astype(jnp.bfloat16)
    attn = lax.all_to_all(
        jnp.broadcast_to(attn_block, (devices, span)), ("rows", "cols"), 0, 0, tiled=True
    ).reshape(images, query_count, width)
    mixed = queries + jnp.dot(attn, out_weight, preferred_element_type=jnp.float32)
    centre = jnp.mean(mixed, axis=2, keepdims=True)
    spread = jnp.mean((mixed - centre) ** 2, axis=2, keepdims=True)
    updated = (mixed - centre) / jnp.sqrt(spread + 1e-05) * ln_gain + ln_bias
    hidden = jax.nn.relu(
        jnp.dot(updated.astype(jnp.bfloat16), embed_one, preferred_element_type=jnp.float32)
    ).astype(jnp.bfloat16)
    embed = jnp.dot(hidden, embed_two, preferred_element_type=jnp.float32).astype(jnp.bfloat16)
    logits = logits_of(embed, mask_feat, tile_rows, tile_cols)
    return (updated, logits.reshape(images, query_count, tile_rows, tile_cols))


def solution(mesh):
    return jax.shard_map(
        on_device,
        mesh=mesh,
        in_specs=(
            P(None, "rows", "cols", None),
            P(None, None, "rows", "cols"),
            P(),
            P(),
            P(),
            P(),
            P(),
            P(),
            P(),
            P(),
            P(),
            P(),
            P(),
            P(),
        ),
        out_specs=(P(), P(None, None, "rows", "cols")),
        check_vma=False,
    )
```

```python
import jax
import jax.numpy as jnp
from jax import lax
from jax.experimental import pallas as pl
from jax.experimental.pallas import tpu as pltpu
from jax.sharding import PartitionSpec as P

HEADS = 8
GROUPS = 32
NEG = -1e30


def with_halo(cells, sides, width):
    for axis, dim in sides:
        count = lax.axis_size(axis)
        ends = count - 1
        head = lax.slice_in_dim(cells, 0, width, axis=dim)
        tail = lax.slice_in_dim(cells, cells.shape[dim] - width, cells.shape[dim], axis=dim)
        cells = jnp.concatenate(
            [
                lax.ppermute(tail, axis, [(i, (i + 1) % count) for i in range(ends)]),
                cells,
                lax.ppermute(head, axis, [((i + 1) % count, i) for i in range(ends)]),
            ],
            axis=dim,
        )
    return cells


def butterfly_sum(x):
    for axis in ("cols", "rows"):
        n = lax.axis_size(axis)
        if n & (n - 1):
            x = jax.tree.map(lambda v: lax.psum(v, axis), x)
            continue
        k = 1
        while k < n:
            got = lax.ppermute(x, axis, [(i, i ^ k) for i in range(n)])
            x = jax.tree.map(lambda a, b: a + b, x, got)
            k *= 2
    return x


def split_parts(x, span):
    return x[:, :span], x[:, span : span + span // 32], x[:, span + span // 32 :]


def merge(a, b, span):
    wa, ta, ma = split_parts(a, span)
    wb, tb, mb = split_parts(b, span)
    m = jnp.maximum(ma, mb)
    fa = jnp.exp(ma - m)
    fb = jnp.exp(mb - m)
    t = ta * fa + tb * fb
    w = wa * jnp.repeat(fa, 32, axis=1) + wb * jnp.repeat(fb, 32, axis=1)
    return jnp.concatenate([w, t, m], axis=1)


def halving_merge(x, span):
    for axis in ("cols", "rows"):
        n = lax.axis_size(axis)
        idx = lax.axis_index(axis)
        k = n // 2
        while k >= 1:
            h = x.shape[0] // 2
            lo, hi = x[:h], x[h:]
            upper = (idx // k) % 2 == 1
            keep = jnp.where(upper, hi, lo)
            send = jnp.where(upper, lo, hi)
            got = lax.ppermute(send, axis, [(i, i ^ k) for i in range(n)])
            x = merge(keep, got, span)
            k //= 2
    return x


def doubling_gather(a):
    for axis in ("rows", "cols"):
        n = lax.axis_size(axis)
        idx = lax.axis_index(axis)
        k = 1
        while k < n:
            got = lax.ppermute(a, axis, [(i, i ^ k) for i in range(n)])
            upper = (idx // k) % 2 == 1
            a = jnp.where(upper, jnp.concatenate([got, a]), jnp.concatenate([a, got]))
            k *= 2
    return a


def prep_kernel(m_ref, fg_ref, cnt_ref):
    queries = fg_ref.shape[1]
    tile_rows = m_ref.shape[1] // queries
    tile_cols = m_ref.shape[2]
    acc = jnp.zeros((queries, tile_cols), jnp.float32)
    for r in range(tile_rows):
        rows = m_ref[0, pl.ds(r, queries, stride=tile_rows), :]
        fg = (rows == 1).astype(jnp.float32)
        acc = acc + fg
        fg_ref[0, :, r * tile_cols : (r + 1) * tile_cols] = fg.astype(jnp.bfloat16)
    cnt_ref[0] = jnp.sum(acc, axis=1, keepdims=True)


def prep(masks):
    images, queries, tile_rows, tile_cols = masks.shape
    flat = masks.reshape(images, queries * tile_rows, tile_cols)
    return pl.pallas_call(
        prep_kernel,
        grid=(images,),
        in_specs=[pl.BlockSpec((1, queries * tile_rows, tile_cols), lambda i: (i, 0, 0))],
        out_specs=[
            pl.BlockSpec((1, queries, tile_rows * tile_cols), lambda i: (i, 0, 0)),
            pl.BlockSpec((1, queries, 1), lambda i: (i, 0, 0)),
        ],
        out_shape=[
            jax.ShapeDtypeStruct((images, queries, tile_rows * tile_cols), jnp.bfloat16),
            jax.ShapeDtypeStruct((images, queries, 1), jnp.float32),
        ],
    )(flat)


def attention_kernel(q_ref, k_ref, v_ref, fg_ref, zero_ref, top_ref, tot_ref, wv_ref, *, heads, scale):
    queries = fg_ref.shape[1]
    width = k_ref.shape[2]
    head_size = width // heads
    k = k_ref[0]
    v = v_ref[0]
    allowed = (fg_ref[0] != 0) | (zero_ref[0] != 0)
    bias = jnp.where(allowed, 0.0, -jnp.inf)
    lane = lax.broadcasted_iota(jnp.int32, (queries, width), 1)
    acc = jnp.zeros((queries, width), jnp.float32)
    for h in range(heads):
        q = q_ref[0, h * queries : (h + 1) * queries, :]
        s = lax.dot_general(q, k, (((1,), (1,)), ((), ())), preferred_element_type=jnp.float32) * scale
        top = jnp.maximum(jnp.max(s + bias, axis=1, keepdims=True), NEG)
        w = jnp.exp(s + bias - top).astype(jnp.bfloat16)
        tot_ref[0, :, h : h + 1] = jnp.sum(w.astype(jnp.float32), axis=1, keepdims=True)
        top_ref[0, :, h : h + 1] = top
        r = jnp.dot(w, v, preferred_element_type=jnp.float32)
        inside = (lane >= h * head_size) & (lane < (h + 1) * head_size)
        acc = acc + jnp.where(inside, r, 0.0)
    wv_ref[0] = acc


def attention(qbd, keys_vals, fg, zero, heads, scale):
    images, pixels, width = keys_vals.shape
    width //= 2
    queries = fg.shape[1]
    kernel = lambda *refs: attention_kernel(*refs, heads=heads, scale=scale)
    return pl.pallas_call(
        kernel,
        grid=(images,),
        in_specs=[
            pl.BlockSpec((1, heads * queries, width), lambda i: (i, 0, 0)),
            pl.BlockSpec((1, pixels, width), lambda i: (i, 0, 0)),
            pl.BlockSpec((1, pixels, width), lambda i: (i, 0, 1)),
            pl.BlockSpec((1, queries, pixels), lambda i: (i, 0, 0)),
            pl.BlockSpec((1, queries, 1), lambda i: (i, 0, 0)),
        ],
        out_specs=[
            pl.BlockSpec((1, queries, heads), lambda i: (i, 0, 0)),
            pl.BlockSpec((1, queries, heads), lambda i: (i, 0, 0)),
            pl.BlockSpec((1, queries, width), lambda i: (i, 0, 0)),
        ],
        out_shape=[
            jax.ShapeDtypeStruct((images, queries, heads), jnp.float32),
            jax.ShapeDtypeStruct((images, queries, heads), jnp.float32),
            jax.ShapeDtypeStruct((images, queries, width), jnp.float32),
        ],
    )(qbd, keys_vals, keys_vals, fg, zero)


def logits_kernel(e_ref, f_ref, o_ref, acc_ref):
    queries = e_ref.shape[1]
    tile_cols = o_ref.shape[2]
    tile_rows = o_ref.shape[1] // queries
    e = e_ref[0]
    for r in range(tile_rows):
        f = f_ref[0, r * tile_cols : (r + 1) * tile_cols, :]
        res = lax.dot_general(e, f, (((1,), (1,)), ((), ())), preferred_element_type=jnp.float32)
        acc_ref[pl.ds(r, queries, stride=tile_rows), :] = res
    o_ref[0] = acc_ref[...].astype(o_ref.dtype)


def logits_of(embed, mask_feat, tile_rows, tile_cols):
    images, queries, width = embed.shape
    pixels = mask_feat.shape[1]
    return pl.pallas_call(
        logits_kernel,
        grid=(images,),
        in_specs=[
            pl.BlockSpec((1, queries, width), lambda i: (i, 0, 0)),
            pl.BlockSpec((1, pixels, width), lambda i: (i, 0, 0)),
        ],
        out_specs=pl.BlockSpec((1, queries * tile_rows, tile_cols), lambda i: (i, 0, 0)),
        out_shape=jax.ShapeDtypeStruct((images, queries * tile_rows, tile_cols), jnp.bfloat16),
        scratch_shapes=[pltpu.VMEM((queries * tile_rows, tile_cols), jnp.float32)],
    )(embed, mask_feat)


def on_device(
    features,
    masks,
    queries,
    conv_weight,
    gn_gain,
    gn_bias,
    query_weight,
    key_weight,
    value_weight,
    out_weight,
    ln_gain,
    ln_bias,
    embed_one,
    embed_two,
):
    images, tile_rows, tile_cols, width = features.shape
    query_count = queries.shape[1]
    heads = HEADS
    head_size = width // heads
    pixels = tile_rows * tile_cols
    devices = lax.axis_size("rows") * lax.axis_size("cols")
    fg, local_count = prep(masks)
    padded = with_halo(features, (("rows", 1), ("cols", 2)), 1)
    conv = lax.conv_general_dilated(
        padded,
        conv_weight,
        (1, 1),
        "VALID",
        dimension_numbers=("NHWC", "HWIO", "NHWC"),
        preferred_element_type=jnp.float32,
    )
    grouped = conv.reshape(images, pixels, GROUPS, width // GROUPS)
    first_sum = jnp.sum(grouped, axis=(1, 3))
    second_sum = jnp.sum(grouped * grouped, axis=(1, 3))
    stats = jnp.concatenate([local_count[..., 0], first_sum, second_sum], axis=1).reshape(1, -1)
    stats = lax.all_to_all(
        jnp.broadcast_to(stats, (devices, stats.shape[1])), ("rows", "cols"), 0, 0, tiled=True
    )
    stats = jnp.sum(stats, axis=0).reshape(images, -1)
    count = stats[:, :query_count]
    first_sum = stats[:, query_count : query_count + GROUPS]
    second_sum = stats[:, query_count + GROUPS :]
    number = devices * pixels * (width // GROUPS)
    mean = first_sum / number
    var = second_sum / number - mean * mean
    normed = (grouped - mean[:, None, :, None]) / jnp.sqrt(var[:, None, :, None] + 1e-05)
    mask_feat = jax.nn.relu(normed.reshape(images, pixels, width) * gn_gain + gn_bias).astype(
        jnp.bfloat16
    )
    keys_vals = jnp.dot(
        mask_feat, jnp.concatenate([key_weight, value_weight], axis=1), preferred_element_type=jnp.float32
    ).astype(jnp.bfloat16)
    qproj = jnp.dot(
        queries.astype(jnp.bfloat16), query_weight, preferred_element_type=jnp.float32
    ).astype(jnp.bfloat16)
    zero = (count == 0.0).astype(jnp.float32)[:, :, None]
    head_of_lane = jnp.arange(width) // head_size
    qbd = jnp.where(
        head_of_lane[None, None, None, :] == jnp.arange(heads)[None, :, None, None],
        qproj[:, None, :, :],
        jnp.zeros((), jnp.bfloat16),
    ).reshape(images, heads * query_count, width)
    top, total, weighted = attention(qbd, keys_vals, fg, zero, heads, 1.0 / head_size**0.5)
    span = images * query_count * width // devices
    groups = span // 32

    def halves(x):
        high = x.astype(jnp.bfloat16)
        return [high, (x - high.astype(jnp.float32)).astype(jnp.bfloat16)]

    packed = jnp.concatenate(
        [weighted.reshape(devices, span).astype(jnp.bfloat16)]
        + halves(total.reshape(devices, groups))
        + halves(top.reshape(devices, groups)),
        axis=1,
    )
    parts = lax.all_to_all(packed, ("rows", "cols"), 0, 0, tiled=True).astype(jnp.float32)
    sums = parts[:, :span]
    pieces = [parts[:, span + n * groups : span + (n + 1) * groups] for n in range(4)]
    totals = pieces[0] + pieces[1]
    tops = pieces[2] + pieces[3]
    highest = jnp.max(tops, axis=0, keepdims=True)
    factor = jnp.exp(tops - highest)
    totals = jnp.sum(totals * factor, axis=0, keepdims=True)
    sums = jnp.sum(sums * jnp.repeat(factor, 32, axis=1), axis=0, keepdims=True)
    attn_block = (sums / jnp.repeat(totals, 32, axis=1)).astype(jnp.bfloat16)
    attn = lax.all_to_all(
        jnp.broadcast_to(attn_block, (devices, span)), ("rows", "cols"), 0, 0, tiled=True
    ).reshape(images, query_count, width)
    mixed = queries + jnp.dot(attn, out_weight, preferred_element_type=jnp.float32)
    centre = jnp.mean(mixed, axis=2, keepdims=True)
    spread = jnp.mean((mixed - centre) ** 2, axis=2, keepdims=True)
    updated = (mixed - centre) / jnp.sqrt(spread + 1e-05) * ln_gain + ln_bias
    hidden = jax.nn.relu(
        jnp.dot(updated.astype(jnp.bfloat16), embed_one, preferred_element_type=jnp.float32)
    ).astype(jnp.bfloat16)
    embed = jnp.dot(hidden, embed_two, preferred_element_type=jnp.float32).astype(jnp.bfloat16)
    logits = logits_of(embed, mask_feat, tile_rows, tile_cols)
    return (updated, logits.reshape(images, query_count, tile_rows, tile_cols))


def solution(mesh):
    return jax.shard_map(
        on_device,
        mesh=mesh,
        in_specs=(
            P(None, "rows", "cols", None),
            P(None, None, "rows", "cols"),
            P(),
            P(),
            P(),
            P(),
            P(),
            P(),
            P(),
            P(),
            P(),
            P(),
            P(),
            P(),
        ),
        out_specs=(P(), P(None, None, "rows", "cols")),
        check_vma=False,
    )
```

```python
import jax
import jax.numpy as jnp
from jax import lax
from jax.experimental import pallas as pl
from jax.experimental.pallas import tpu as pltpu
from jax.sharding import PartitionSpec as P

HEADS = 8
GROUPS = 32
NEG = -1e30


def with_halo(cells, sides, width):
    for axis, dim in sides:
        count = lax.axis_size(axis)
        ends = count - 1
        head = lax.slice_in_dim(cells, 0, width, axis=dim)
        tail = lax.slice_in_dim(cells, cells.shape[dim] - width, cells.shape[dim], axis=dim)
        cells = jnp.concatenate(
            [
                lax.ppermute(tail, axis, [(i, (i + 1) % count) for i in range(ends)]),
                cells,
                lax.ppermute(head, axis, [((i + 1) % count, i) for i in range(ends)]),
            ],
            axis=dim,
        )
    return cells


def butterfly_sum(x):
    for axis in ("cols", "rows"):
        n = lax.axis_size(axis)
        if n & (n - 1):
            x = jax.tree.map(lambda v: lax.psum(v, axis), x)
            continue
        k = 1
        while k < n:
            got = lax.ppermute(x, axis, [(i, i ^ k) for i in range(n)])
            x = jax.tree.map(lambda a, b: a + b, x, got)
            k *= 2
    return x


def split_parts(x, span):
    return x[:, :span], x[:, span : span + span // 32], x[:, span + span // 32 :]


def merge(a, b, span):
    wa, ta, ma = split_parts(a, span)
    wb, tb, mb = split_parts(b, span)
    m = jnp.maximum(ma, mb)
    fa = jnp.exp(ma - m)
    fb = jnp.exp(mb - m)
    t = ta * fa + tb * fb
    w = wa * jnp.repeat(fa, 32, axis=1) + wb * jnp.repeat(fb, 32, axis=1)
    return jnp.concatenate([w, t, m], axis=1)


def halving_merge(x, span):
    for axis in ("cols", "rows"):
        n = lax.axis_size(axis)
        idx = lax.axis_index(axis)
        k = n // 2
        while k >= 1:
            h = x.shape[0] // 2
            lo, hi = x[:h], x[h:]
            upper = (idx // k) % 2 == 1
            keep = jnp.where(upper, hi, lo)
            send = jnp.where(upper, lo, hi)
            got = lax.ppermute(send, axis, [(i, i ^ k) for i in range(n)])
            x = merge(keep, got, span)
            k //= 2
    return x


def doubling_gather(a):
    for axis in ("rows", "cols"):
        n = lax.axis_size(axis)
        idx = lax.axis_index(axis)
        k = 1
        while k < n:
            got = lax.ppermute(a, axis, [(i, i ^ k) for i in range(n)])
            upper = (idx // k) % 2 == 1
            a = jnp.where(upper, jnp.concatenate([got, a]), jnp.concatenate([a, got]))
            k *= 2
    return a


def prep_kernel(m_ref, fg_ref, cnt_ref):
    queries = fg_ref.shape[1]
    tile_rows = m_ref.shape[1] // queries
    tile_cols = m_ref.shape[2]
    acc = jnp.zeros((queries, tile_cols), jnp.float32)
    for r in range(tile_rows):
        rows = m_ref[0, pl.ds(r, queries, stride=tile_rows), :]
        fg = (rows == 1).astype(jnp.float32)
        acc = acc + fg
        fg_ref[0, :, r * tile_cols : (r + 1) * tile_cols] = fg.astype(jnp.bfloat16)
    cnt_ref[0] = jnp.sum(acc, axis=1, keepdims=True)


def prep(masks):
    images, queries, tile_rows, tile_cols = masks.shape
    flat = masks.reshape(images, queries * tile_rows, tile_cols)
    return pl.pallas_call(
        prep_kernel,
        grid=(images,),
        in_specs=[pl.BlockSpec((1, queries * tile_rows, tile_cols), lambda i: (i, 0, 0))],
        out_specs=[
            pl.BlockSpec((1, queries, tile_rows * tile_cols), lambda i: (i, 0, 0)),
            pl.BlockSpec((1, queries, 1), lambda i: (i, 0, 0)),
        ],
        out_shape=[
            jax.ShapeDtypeStruct((images, queries, tile_rows * tile_cols), jnp.bfloat16),
            jax.ShapeDtypeStruct((images, queries, 1), jnp.float32),
        ],
    )(flat)


def attention_kernel(q_ref, k_ref, v_ref, fg_ref, zero_ref, top_ref, tot_ref, wv_ref, *, heads, scale):
    queries = fg_ref.shape[1]
    width = k_ref.shape[2]
    head_size = width // heads
    k = k_ref[0]
    v = v_ref[0]
    allowed = (fg_ref[0] != 0) | (zero_ref[0] != 0)
    bias = jnp.where(allowed, 0.0, -jnp.inf)
    lane = lax.broadcasted_iota(jnp.int32, (queries, width), 1)
    acc = jnp.zeros((queries, width), jnp.float32)
    for h in range(heads):
        q = q_ref[0, h * queries : (h + 1) * queries, :]
        s = lax.dot_general(q, k, (((1,), (1,)), ((), ())), preferred_element_type=jnp.float32) * scale
        top = jnp.maximum(jnp.max(s + bias, axis=1, keepdims=True), NEG)
        w = jnp.exp(s + bias - top).astype(jnp.bfloat16)
        tot_ref[0, :, h : h + 1] = jnp.sum(w.astype(jnp.float32), axis=1, keepdims=True)
        top_ref[0, :, h : h + 1] = top
        r = jnp.dot(w, v, preferred_element_type=jnp.float32)
        inside = (lane >= h * head_size) & (lane < (h + 1) * head_size)
        acc = acc + jnp.where(inside, r, 0.0)
    wv_ref[0] = acc


def attention(qbd, keys_vals, fg, zero, heads, scale):
    images, pixels, width = keys_vals.shape
    width //= 2
    queries = fg.shape[1]
    kernel = lambda *refs: attention_kernel(*refs, heads=heads, scale=scale)
    return pl.pallas_call(
        kernel,
        grid=(images,),
        in_specs=[
            pl.BlockSpec((1, heads * queries, width), lambda i: (i, 0, 0)),
            pl.BlockSpec((1, pixels, width), lambda i: (i, 0, 0)),
            pl.BlockSpec((1, pixels, width), lambda i: (i, 0, 1)),
            pl.BlockSpec((1, queries, pixels), lambda i: (i, 0, 0)),
            pl.BlockSpec((1, queries, 1), lambda i: (i, 0, 0)),
        ],
        out_specs=[
            pl.BlockSpec((1, queries, heads), lambda i: (i, 0, 0)),
            pl.BlockSpec((1, queries, heads), lambda i: (i, 0, 0)),
            pl.BlockSpec((1, queries, width), lambda i: (i, 0, 0)),
        ],
        out_shape=[
            jax.ShapeDtypeStruct((images, queries, heads), jnp.float32),
            jax.ShapeDtypeStruct((images, queries, heads), jnp.float32),
            jax.ShapeDtypeStruct((images, queries, width), jnp.float32),
        ],
    )(qbd, keys_vals, keys_vals, fg, zero)


def logits_kernel(e_ref, f_ref, o_ref, acc_ref):
    queries = e_ref.shape[1]
    tile_cols = o_ref.shape[2]
    tile_rows = o_ref.shape[1] // queries
    e = e_ref[0]
    for r in range(tile_rows):
        f = f_ref[0, r * tile_cols : (r + 1) * tile_cols, :]
        res = lax.dot_general(e, f, (((1,), (1,)), ((), ())), preferred_element_type=jnp.float32)
        acc_ref[pl.ds(r, queries, stride=tile_rows), :] = res
    o_ref[0] = acc_ref[...].astype(o_ref.dtype)


def logits_of(embed, mask_feat, tile_rows, tile_cols):
    images, queries, width = embed.shape
    pixels = mask_feat.shape[1]
    return pl.pallas_call(
        logits_kernel,
        grid=(images,),
        in_specs=[
            pl.BlockSpec((1, queries, width), lambda i: (i, 0, 0)),
            pl.BlockSpec((1, pixels, width), lambda i: (i, 0, 0)),
        ],
        out_specs=pl.BlockSpec((1, queries * tile_rows, tile_cols), lambda i: (i, 0, 0)),
        out_shape=jax.ShapeDtypeStruct((images, queries * tile_rows, tile_cols), jnp.bfloat16),
        scratch_shapes=[pltpu.VMEM((queries * tile_rows, tile_cols), jnp.float32)],
    )(embed, mask_feat)


def on_device(
    features,
    masks,
    queries,
    conv_weight,
    gn_gain,
    gn_bias,
    query_weight,
    key_weight,
    value_weight,
    out_weight,
    ln_gain,
    ln_bias,
    embed_one,
    embed_two,
):
    images, tile_rows, tile_cols, width = features.shape
    query_count = queries.shape[1]
    heads = HEADS
    head_size = width // heads
    pixels = tile_rows * tile_cols
    devices = lax.axis_size("rows") * lax.axis_size("cols")
    fg, local_count = prep(masks)
    padded = with_halo(features, (("rows", 1), ("cols", 2)), 1)
    conv = lax.conv_general_dilated(
        padded,
        conv_weight,
        (1, 1),
        "VALID",
        dimension_numbers=("NHWC", "HWIO", "NHWC"),
        preferred_element_type=jnp.float32,
    )
    grouped = conv.reshape(images, pixels, GROUPS, width // GROUPS)
    first_sum = jnp.sum(grouped, axis=(1, 3))
    second_sum = jnp.sum(grouped * grouped, axis=(1, 3))
    present = jnp.minimum(local_count[..., 0], 1.0).reshape(1, -1)
    sums = jnp.concatenate([first_sum, second_sum], axis=1).reshape(1, -1)
    high = sums.astype(jnp.bfloat16)
    rest = sums - high.astype(jnp.float32)
    middle = rest.astype(jnp.bfloat16)
    low = (rest - middle.astype(jnp.float32)).astype(jnp.bfloat16)
    stats = jnp.concatenate([present.astype(jnp.bfloat16), high, middle, low], axis=1)
    stats = lax.all_to_all(
        jnp.broadcast_to(stats, (devices, stats.shape[1])), ("rows", "cols"), 0, 0, tiled=True
    ).astype(jnp.float32)
    flags = images * query_count
    count = jnp.sum(stats[:, :flags], axis=0).reshape(images, query_count)
    parts = stats[:, flags:]
    width_sums = parts.shape[1] // 3
    parts = parts[:, :width_sums] + parts[:, width_sums : 2 * width_sums] + parts[:, 2 * width_sums :]
    sums = jnp.sum(parts, axis=0).reshape(images, 2 * GROUPS)
    first_sum = sums[:, :GROUPS]
    second_sum = sums[:, GROUPS:]
    number = devices * pixels * (width // GROUPS)
    mean = first_sum / number
    var = second_sum / number - mean * mean
    normed = (grouped - mean[:, None, :, None]) / jnp.sqrt(var[:, None, :, None] + 1e-05)
    mask_feat = jax.nn.relu(normed.reshape(images, pixels, width) * gn_gain + gn_bias).astype(
        jnp.bfloat16
    )
    keys_vals = jnp.dot(
        mask_feat, jnp.concatenate([key_weight, value_weight], axis=1), preferred_element_type=jnp.float32
    ).astype(jnp.bfloat16)
    qproj = jnp.dot(
        queries.astype(jnp.bfloat16), query_weight, preferred_element_type=jnp.float32
    ).astype(jnp.bfloat16)
    zero = (count == 0.0).astype(jnp.float32)[:, :, None]
    head_of_lane = jnp.arange(width) // head_size
    qbd = jnp.where(
        head_of_lane[None, None, None, :] == jnp.arange(heads)[None, :, None, None],
        qproj[:, None, :, :],
        jnp.zeros((), jnp.bfloat16),
    ).reshape(images, heads * query_count, width)
    top, total, weighted = attention(qbd, keys_vals, fg, zero, heads, 1.0 / head_size**0.5)
    span = images * query_count * width // devices
    groups = span // 32

    def halves(x):
        high = x.astype(jnp.bfloat16)
        return [high, (x - high.astype(jnp.float32)).astype(jnp.bfloat16)]

    packed = jnp.concatenate(
        [weighted.reshape(devices, span).astype(jnp.bfloat16)]
        + halves(total.reshape(devices, groups))
        + halves(top.reshape(devices, groups)),
        axis=1,
    )
    parts = lax.all_to_all(packed, ("rows", "cols"), 0, 0, tiled=True).astype(jnp.float32)
    sums = parts[:, :span]
    pieces = [parts[:, span + n * groups : span + (n + 1) * groups] for n in range(4)]
    totals = pieces[0] + pieces[1]
    tops = pieces[2] + pieces[3]
    highest = jnp.max(tops, axis=0, keepdims=True)
    factor = jnp.exp(tops - highest)
    totals = jnp.sum(totals * factor, axis=0, keepdims=True)
    sums = jnp.sum(sums * jnp.repeat(factor, 32, axis=1), axis=0, keepdims=True)
    attn_block = (sums / jnp.repeat(totals, 32, axis=1)).astype(jnp.bfloat16)
    attn = lax.all_to_all(
        jnp.broadcast_to(attn_block, (devices, span)), ("rows", "cols"), 0, 0, tiled=True
    ).reshape(images, query_count, width)
    mixed = queries + jnp.dot(attn, out_weight, preferred_element_type=jnp.float32)
    centre = jnp.mean(mixed, axis=2, keepdims=True)
    spread = jnp.mean((mixed - centre) ** 2, axis=2, keepdims=True)
    updated = (mixed - centre) / jnp.sqrt(spread + 1e-05) * ln_gain + ln_bias
    hidden = jax.nn.relu(
        jnp.dot(updated.astype(jnp.bfloat16), embed_one, preferred_element_type=jnp.float32)
    ).astype(jnp.bfloat16)
    embed = jnp.dot(hidden, embed_two, preferred_element_type=jnp.float32).astype(jnp.bfloat16)
    logits = logits_of(embed, mask_feat, tile_rows, tile_cols)
    return (updated, logits.reshape(images, query_count, tile_rows, tile_cols))


def solution(mesh):
    return jax.shard_map(
        on_device,
        mesh=mesh,
        in_specs=(
            P(None, "rows", "cols", None),
            P(None, None, "rows", "cols"),
            P(),
            P(),
            P(),
            P(),
            P(),
            P(),
            P(),
            P(),
            P(),
            P(),
            P(),
            P(),
        ),
        out_specs=(P(), P(None, None, "rows", "cols")),
        check_vma=False,
    )
```

```python
import jax
import jax.numpy as jnp
from jax import lax
from jax.experimental import pallas as pl
from jax.experimental.pallas import tpu as pltpu
from jax.sharding import PartitionSpec as P

HEADS = 8
GROUPS = 32
NEG = -1e30


def with_halo(cells, sides, width):
    for axis, dim in sides:
        count = lax.axis_size(axis)
        ends = count - 1
        head = lax.slice_in_dim(cells, 0, width, axis=dim)
        tail = lax.slice_in_dim(cells, cells.shape[dim] - width, cells.shape[dim], axis=dim)
        cells = jnp.concatenate(
            [
                lax.ppermute(tail, axis, [(i, (i + 1) % count) for i in range(ends)]),
                cells,
                lax.ppermute(head, axis, [((i + 1) % count, i) for i in range(ends)]),
            ],
            axis=dim,
        )
    return cells


def butterfly_sum(x):
    for axis in ("cols", "rows"):
        n = lax.axis_size(axis)
        if n & (n - 1):
            x = jax.tree.map(lambda v: lax.psum(v, axis), x)
            continue
        k = 1
        while k < n:
            got = lax.ppermute(x, axis, [(i, i ^ k) for i in range(n)])
            x = jax.tree.map(lambda a, b: a + b, x, got)
            k *= 2
    return x


def split_parts(x, span):
    return x[:, :span], x[:, span : span + span // 32], x[:, span + span // 32 :]


def merge(a, b, span):
    wa, ta, ma = split_parts(a, span)
    wb, tb, mb = split_parts(b, span)
    m = jnp.maximum(ma, mb)
    fa = jnp.exp(ma - m)
    fb = jnp.exp(mb - m)
    t = ta * fa + tb * fb
    w = wa * jnp.repeat(fa, 32, axis=1) + wb * jnp.repeat(fb, 32, axis=1)
    return jnp.concatenate([w, t, m], axis=1)


def halving_merge(x, span):
    for axis in ("cols", "rows"):
        n = lax.axis_size(axis)
        idx = lax.axis_index(axis)
        k = n // 2
        while k >= 1:
            h = x.shape[0] // 2
            lo, hi = x[:h], x[h:]
            upper = (idx // k) % 2 == 1
            keep = jnp.where(upper, hi, lo)
            send = jnp.where(upper, lo, hi)
            got = lax.ppermute(send, axis, [(i, i ^ k) for i in range(n)])
            x = merge(keep, got, span)
            k //= 2
    return x


def doubling_gather(a):
    for axis in ("rows", "cols"):
        n = lax.axis_size(axis)
        idx = lax.axis_index(axis)
        k = 1
        while k < n:
            got = lax.ppermute(a, axis, [(i, i ^ k) for i in range(n)])
            upper = (idx // k) % 2 == 1
            a = jnp.where(upper, jnp.concatenate([got, a]), jnp.concatenate([a, got]))
            k *= 2
    return a


def prep_kernel(m_ref, fg_ref, cnt_ref):
    queries = fg_ref.shape[1]
    tile_rows = m_ref.shape[1] // queries
    tile_cols = m_ref.shape[2]
    acc = jnp.zeros((queries, tile_cols), jnp.float32)
    for r in range(tile_rows):
        rows = m_ref[0, pl.ds(r, queries, stride=tile_rows), :]
        fg = (rows == 1).astype(jnp.float32)
        acc = acc + fg
        fg_ref[0, :, r * tile_cols : (r + 1) * tile_cols] = fg.astype(jnp.bfloat16)
    cnt_ref[0] = jnp.sum(acc, axis=1, keepdims=True)


def prep(masks):
    images, queries, tile_rows, tile_cols = masks.shape
    flat = masks.reshape(images, queries * tile_rows, tile_cols)
    return pl.pallas_call(
        prep_kernel,
        grid=(images,),
        in_specs=[pl.BlockSpec((1, queries * tile_rows, tile_cols), lambda i: (i, 0, 0))],
        out_specs=[
            pl.BlockSpec((1, queries, tile_rows * tile_cols), lambda i: (i, 0, 0)),
            pl.BlockSpec((1, queries, 1), lambda i: (i, 0, 0)),
        ],
        out_shape=[
            jax.ShapeDtypeStruct((images, queries, tile_rows * tile_cols), jnp.bfloat16),
            jax.ShapeDtypeStruct((images, queries, 1), jnp.float32),
        ],
    )(flat)


def attention_kernel(q_ref, k_ref, v_ref, fg_ref, zero_ref, top_ref, tot_ref, wv_ref, *, heads, scale):
    queries = fg_ref.shape[1]
    width = k_ref.shape[2]
    head_size = width // heads
    k = k_ref[0]
    v = v_ref[0]
    allowed = (fg_ref[0] != 0) | (zero_ref[0] != 0)
    bias = jnp.where(allowed, 0.0, -jnp.inf)
    for h in range(heads):
        q = q_ref[0, h * queries : (h + 1) * queries, :]
        s = lax.dot_general(q, k, (((1,), (1,)), ((), ())), preferred_element_type=jnp.float32) * scale
        top = jnp.maximum(jnp.max(s + bias, axis=1, keepdims=True), NEG)
        w = jnp.exp(s + bias - top).astype(jnp.bfloat16)
        tot_ref[0, :, h : h + 1] = jnp.sum(w.astype(jnp.float32), axis=1, keepdims=True)
        top_ref[0, :, h : h + 1] = top
        r = jnp.dot(w, v, preferred_element_type=jnp.float32)
        wv_ref[0, :, h * head_size : (h + 1) * head_size] = r[:, h * head_size : (h + 1) * head_size]


def attention(qbd, keys_vals, fg, zero, heads, scale):
    images, pixels, width = keys_vals.shape
    width //= 2
    queries = fg.shape[1]
    kernel = lambda *refs: attention_kernel(*refs, heads=heads, scale=scale)
    return pl.pallas_call(
        kernel,
        grid=(images,),
        in_specs=[
            pl.BlockSpec((1, heads * queries, width), lambda i: (i, 0, 0)),
            pl.BlockSpec((1, pixels, width), lambda i: (i, 0, 0)),
            pl.BlockSpec((1, pixels, width), lambda i: (i, 0, 1)),
            pl.BlockSpec((1, queries, pixels), lambda i: (i, 0, 0)),
            pl.BlockSpec((1, queries, 1), lambda i: (i, 0, 0)),
        ],
        out_specs=[
            pl.BlockSpec((1, queries, heads), lambda i: (i, 0, 0)),
            pl.BlockSpec((1, queries, heads), lambda i: (i, 0, 0)),
            pl.BlockSpec((1, queries, width), lambda i: (i, 0, 0)),
        ],
        out_shape=[
            jax.ShapeDtypeStruct((images, queries, heads), jnp.float32),
            jax.ShapeDtypeStruct((images, queries, heads), jnp.float32),
            jax.ShapeDtypeStruct((images, queries, width), jnp.float32),
        ],
    )(qbd, keys_vals, keys_vals, fg, zero)


def logits_kernel(e_ref, f_ref, o_ref, acc_ref):
    queries = e_ref.shape[1]
    tile_cols = o_ref.shape[2]
    tile_rows = o_ref.shape[1] // queries
    e = e_ref[0]
    for r in range(tile_rows):
        f = f_ref[0, r * tile_cols : (r + 1) * tile_cols, :]
        res = lax.dot_general(e, f, (((1,), (1,)), ((), ())), preferred_element_type=jnp.float32)
        acc_ref[pl.ds(r, queries, stride=tile_rows), :] = res
    o_ref[0] = acc_ref[...].astype(o_ref.dtype)


def logits_of(embed, mask_feat, tile_rows, tile_cols):
    images, queries, width = embed.shape
    pixels = mask_feat.shape[1]
    return pl.pallas_call(
        logits_kernel,
        grid=(images,),
        in_specs=[
            pl.BlockSpec((1, queries, width), lambda i: (i, 0, 0)),
            pl.BlockSpec((1, pixels, width), lambda i: (i, 0, 0)),
        ],
        out_specs=pl.BlockSpec((1, queries * tile_rows, tile_cols), lambda i: (i, 0, 0)),
        out_shape=jax.ShapeDtypeStruct((images, queries * tile_rows, tile_cols), jnp.bfloat16),
        scratch_shapes=[pltpu.VMEM((queries * tile_rows, tile_cols), jnp.float32)],
    )(embed, mask_feat)


def on_device(
    features,
    masks,
    queries,
    conv_weight,
    gn_gain,
    gn_bias,
    query_weight,
    key_weight,
    value_weight,
    out_weight,
    ln_gain,
    ln_bias,
    embed_one,
    embed_two,
):
    images, tile_rows, tile_cols, width = features.shape
    query_count = queries.shape[1]
    heads = HEADS
    head_size = width // heads
    pixels = tile_rows * tile_cols
    devices = lax.axis_size("rows") * lax.axis_size("cols")
    fg, local_count = prep(masks)
    padded = with_halo(features, (("rows", 1), ("cols", 2)), 1)
    conv = lax.conv_general_dilated(
        padded,
        conv_weight,
        (1, 1),
        "VALID",
        dimension_numbers=("NHWC", "HWIO", "NHWC"),
        preferred_element_type=jnp.float32,
    )
    grouped = conv.reshape(images, pixels, GROUPS, width // GROUPS)
    first_sum = jnp.sum(grouped, axis=(1, 3))
    second_sum = jnp.sum(grouped * grouped, axis=(1, 3))
    stats = jnp.concatenate([local_count[..., 0], first_sum, second_sum], axis=1).reshape(1, -1)
    stats = lax.all_to_all(
        jnp.broadcast_to(stats, (devices, stats.shape[1])), ("rows", "cols"), 0, 0, tiled=True
    )
    stats = jnp.sum(stats, axis=0).reshape(images, -1)
    count = stats[:, :query_count]
    first_sum = stats[:, query_count : query_count + GROUPS]
    second_sum = stats[:, query_count + GROUPS :]
    number = devices * pixels * (width // GROUPS)
    mean = first_sum / number
    var = second_sum / number - mean * mean
    normed = (grouped - mean[:, None, :, None]) / jnp.sqrt(var[:, None, :, None] + 1e-05)
    mask_feat = jax.nn.relu(normed.reshape(images, pixels, width) * gn_gain + gn_bias).astype(
        jnp.bfloat16
    )
    keys_vals = jnp.dot(
        mask_feat, jnp.concatenate([key_weight, value_weight], axis=1), preferred_element_type=jnp.float32
    ).astype(jnp.bfloat16)
    qproj = jnp.dot(
        queries.astype(jnp.bfloat16), query_weight, preferred_element_type=jnp.float32
    ).astype(jnp.bfloat16)
    zero = (count == 0.0).astype(jnp.float32)[:, :, None]
    head_of_lane = jnp.arange(width) // head_size
    qbd = jnp.where(
        head_of_lane[None, None, None, :] == jnp.arange(heads)[None, :, None, None],
        qproj[:, None, :, :],
        jnp.zeros((), jnp.bfloat16),
    ).reshape(images, heads * query_count, width)
    top, total, weighted = attention(qbd, keys_vals, fg, zero, heads, 1.0 / head_size**0.5)
    span = images * query_count * width // devices
    groups = span // 32

    def halves(x):
        high = x.astype(jnp.bfloat16)
        return [high, (x - high.astype(jnp.float32)).astype(jnp.bfloat16)]

    packed = jnp.concatenate(
        [weighted.reshape(devices, span).astype(jnp.bfloat16)]
        + halves(total.reshape(devices, groups))
        + halves(top.reshape(devices, groups)),
        axis=1,
    )
    parts = lax.all_to_all(packed, ("rows", "cols"), 0, 0, tiled=True).astype(jnp.float32)
    sums = parts[:, :span]
    pieces = [parts[:, span + n * groups : span + (n + 1) * groups] for n in range(4)]
    totals = pieces[0] + pieces[1]
    tops = pieces[2] + pieces[3]
    highest = jnp.max(tops, axis=0, keepdims=True)
    factor = jnp.exp(tops - highest)
    totals = jnp.sum(totals * factor, axis=0, keepdims=True)
    sums = jnp.sum(sums * jnp.repeat(factor, 32, axis=1), axis=0, keepdims=True)
    attn_block = (sums / jnp.repeat(totals, 32, axis=1)).astype(jnp.bfloat16)
    attn = lax.all_to_all(
        jnp.broadcast_to(attn_block, (devices, span)), ("rows", "cols"), 0, 0, tiled=True
    ).reshape(images, query_count, width)
    mixed = queries + jnp.dot(attn, out_weight, preferred_element_type=jnp.float32)
    centre = jnp.mean(mixed, axis=2, keepdims=True)
    spread = jnp.mean((mixed - centre) ** 2, axis=2, keepdims=True)
    updated = (mixed - centre) / jnp.sqrt(spread + 1e-05) * ln_gain + ln_bias
    hidden = jax.nn.relu(
        jnp.dot(updated.astype(jnp.bfloat16), embed_one, preferred_element_type=jnp.float32)
    ).astype(jnp.bfloat16)
    embed = jnp.dot(hidden, embed_two, preferred_element_type=jnp.float32).astype(jnp.bfloat16)
    logits = logits_of(embed, mask_feat, tile_rows, tile_cols)
    return (updated, logits.reshape(images, query_count, tile_rows, tile_cols))


def solution(mesh):
    return jax.shard_map(
        on_device,
        mesh=mesh,
        in_specs=(
            P(None, "rows", "cols", None),
            P(None, None, "rows", "cols"),
            P(),
            P(),
            P(),
            P(),
            P(),
            P(),
            P(),
            P(),
            P(),
            P(),
            P(),
            P(),
        ),
        out_specs=(P(), P(None, None, "rows", "cols")),
        check_vma=False,
    )
```

```python
import jax
import jax.numpy as jnp
from jax import lax
from jax.experimental import pallas as pl
from jax.experimental.pallas import tpu as pltpu
from jax.sharding import PartitionSpec as P

HEADS = 8
GROUPS = 32
NEG = -1e30


def with_halo(cells, sides, width):
    for axis, dim in sides:
        count = lax.axis_size(axis)
        ends = count - 1
        head = lax.slice_in_dim(cells, 0, width, axis=dim)
        tail = lax.slice_in_dim(cells, cells.shape[dim] - width, cells.shape[dim], axis=dim)
        cells = jnp.concatenate(
            [
                lax.ppermute(tail, axis, [(i, (i + 1) % count) for i in range(ends)]),
                cells,
                lax.ppermute(head, axis, [((i + 1) % count, i) for i in range(ends)]),
            ],
            axis=dim,
        )
    return cells


def butterfly_sum(x):
    for axis in ("cols", "rows"):
        n = lax.axis_size(axis)
        if n & (n - 1):
            x = jax.tree.map(lambda v: lax.psum(v, axis), x)
            continue
        k = 1
        while k < n:
            got = lax.ppermute(x, axis, [(i, i ^ k) for i in range(n)])
            x = jax.tree.map(lambda a, b: a + b, x, got)
            k *= 2
    return x


def split_parts(x, span):
    return x[:, :span], x[:, span : span + span // 32], x[:, span + span // 32 :]


def merge(a, b, span):
    wa, ta, ma = split_parts(a, span)
    wb, tb, mb = split_parts(b, span)
    m = jnp.maximum(ma, mb)
    fa = jnp.exp(ma - m)
    fb = jnp.exp(mb - m)
    t = ta * fa + tb * fb
    w = wa * jnp.repeat(fa, 32, axis=1) + wb * jnp.repeat(fb, 32, axis=1)
    return jnp.concatenate([w, t, m], axis=1)


def halving_merge(x, span):
    for axis in ("cols", "rows"):
        n = lax.axis_size(axis)
        idx = lax.axis_index(axis)
        k = n // 2
        while k >= 1:
            h = x.shape[0] // 2
            lo, hi = x[:h], x[h:]
            upper = (idx // k) % 2 == 1
            keep = jnp.where(upper, hi, lo)
            send = jnp.where(upper, lo, hi)
            got = lax.ppermute(send, axis, [(i, i ^ k) for i in range(n)])
            x = merge(keep, got, span)
            k //= 2
    return x


def doubling_gather(a):
    for axis in ("rows", "cols"):
        n = lax.axis_size(axis)
        idx = lax.axis_index(axis)
        k = 1
        while k < n:
            got = lax.ppermute(a, axis, [(i, i ^ k) for i in range(n)])
            upper = (idx // k) % 2 == 1
            a = jnp.where(upper, jnp.concatenate([got, a]), jnp.concatenate([a, got]))
            k *= 2
    return a


def prep_kernel(m_ref, fg_ref, cnt_ref):
    queries = fg_ref.shape[1]
    tile_rows = m_ref.shape[1] // queries
    tile_cols = m_ref.shape[2]
    acc = jnp.zeros((queries, tile_cols), jnp.float32)
    for r in range(tile_rows):
        rows = m_ref[0, pl.ds(r, queries, stride=tile_rows), :]
        fg = (rows == 1).astype(jnp.float32)
        acc = acc + fg
        fg_ref[0, :, r * tile_cols : (r + 1) * tile_cols] = fg.astype(jnp.bfloat16)
    cnt_ref[0] = jnp.sum(acc, axis=1, keepdims=True)


def prep(masks):
    images, queries, tile_rows, tile_cols = masks.shape
    flat = masks.reshape(images, queries * tile_rows, tile_cols)
    return pl.pallas_call(
        prep_kernel,
        grid=(images,),
        in_specs=[pl.BlockSpec((1, queries * tile_rows, tile_cols), lambda i: (i, 0, 0))],
        out_specs=[
            pl.BlockSpec((1, queries, tile_rows * tile_cols), lambda i: (i, 0, 0)),
            pl.BlockSpec((1, queries, 1), lambda i: (i, 0, 0)),
        ],
        out_shape=[
            jax.ShapeDtypeStruct((images, queries, tile_rows * tile_cols), jnp.bfloat16),
            jax.ShapeDtypeStruct((images, queries, 1), jnp.float32),
        ],
    )(flat)


def attention_kernel(q_ref, k_ref, v_ref, fg_ref, zero_ref, top_ref, tot_ref, wv_ref, *, heads, scale):
    queries = fg_ref.shape[1]
    width = k_ref.shape[2]
    head_size = width // heads
    k = k_ref[0]
    v = v_ref[0]
    allowed = (fg_ref[0] != 0) | (zero_ref[0] != 0)
    bias = jnp.where(allowed, 0.0, -jnp.inf)
    lane = lax.broadcasted_iota(jnp.int32, v.shape, 1)
    for h in range(heads):
        q = q_ref[0, h * queries : (h + 1) * queries, :]
        s = lax.dot_general(q, k, (((1,), (1,)), ((), ())), preferred_element_type=jnp.float32) * scale
        top = jnp.maximum(jnp.max(s + bias, axis=1, keepdims=True), NEG)
        w = jnp.exp(s + bias - top).astype(jnp.bfloat16)
        top_ref[0, :, h : h + 1] = top
        spare = ((h + 1) % heads) * head_size
        r = jnp.dot(w, jnp.where(lane == spare, jnp.ones((), v.dtype), v), preferred_element_type=jnp.float32)
        tot_ref[0, :, h : h + 1] = r[:, spare : spare + 1]
        wv_ref[0, :, h * head_size : (h + 1) * head_size] = r[:, h * head_size : (h + 1) * head_size]


def attention(qbd, keys_vals, fg, zero, heads, scale):
    images, pixels, width = keys_vals.shape
    width //= 2
    queries = fg.shape[1]
    kernel = lambda *refs: attention_kernel(*refs, heads=heads, scale=scale)
    return pl.pallas_call(
        kernel,
        grid=(images,),
        in_specs=[
            pl.BlockSpec((1, heads * queries, width), lambda i: (i, 0, 0)),
            pl.BlockSpec((1, pixels, width), lambda i: (i, 0, 0)),
            pl.BlockSpec((1, pixels, width), lambda i: (i, 0, 1)),
            pl.BlockSpec((1, queries, pixels), lambda i: (i, 0, 0)),
            pl.BlockSpec((1, queries, 1), lambda i: (i, 0, 0)),
        ],
        out_specs=[
            pl.BlockSpec((1, queries, heads), lambda i: (i, 0, 0)),
            pl.BlockSpec((1, queries, heads), lambda i: (i, 0, 0)),
            pl.BlockSpec((1, queries, width), lambda i: (i, 0, 0)),
        ],
        out_shape=[
            jax.ShapeDtypeStruct((images, queries, heads), jnp.float32),
            jax.ShapeDtypeStruct((images, queries, heads), jnp.float32),
            jax.ShapeDtypeStruct((images, queries, width), jnp.float32),
        ],
    )(qbd, keys_vals, keys_vals, fg, zero)


def logits_kernel(e_ref, f_ref, o_ref, acc_ref):
    queries = e_ref.shape[1]
    tile_cols = o_ref.shape[2]
    tile_rows = o_ref.shape[1] // queries
    e = e_ref[0]
    for r in range(tile_rows):
        f = f_ref[0, r * tile_cols : (r + 1) * tile_cols, :]
        res = lax.dot_general(e, f, (((1,), (1,)), ((), ())), preferred_element_type=jnp.float32)
        acc_ref[pl.ds(r, queries, stride=tile_rows), :] = res
    o_ref[0] = acc_ref[...].astype(o_ref.dtype)


def logits_of(embed, mask_feat, tile_rows, tile_cols):
    images, queries, width = embed.shape
    pixels = mask_feat.shape[1]
    return pl.pallas_call(
        logits_kernel,
        grid=(images,),
        in_specs=[
            pl.BlockSpec((1, queries, width), lambda i: (i, 0, 0)),
            pl.BlockSpec((1, pixels, width), lambda i: (i, 0, 0)),
        ],
        out_specs=pl.BlockSpec((1, queries * tile_rows, tile_cols), lambda i: (i, 0, 0)),
        out_shape=jax.ShapeDtypeStruct((images, queries * tile_rows, tile_cols), jnp.bfloat16),
        scratch_shapes=[pltpu.VMEM((queries * tile_rows, tile_cols), jnp.float32)],
    )(embed, mask_feat)


def on_device(
    features,
    masks,
    queries,
    conv_weight,
    gn_gain,
    gn_bias,
    query_weight,
    key_weight,
    value_weight,
    out_weight,
    ln_gain,
    ln_bias,
    embed_one,
    embed_two,
):
    images, tile_rows, tile_cols, width = features.shape
    query_count = queries.shape[1]
    heads = HEADS
    head_size = width // heads
    pixels = tile_rows * tile_cols
    devices = lax.axis_size("rows") * lax.axis_size("cols")
    fg, local_count = prep(masks)
    padded = with_halo(features, (("rows", 1), ("cols", 2)), 1)
    conv = lax.conv_general_dilated(
        padded,
        conv_weight,
        (1, 1),
        "VALID",
        dimension_numbers=("NHWC", "HWIO", "NHWC"),
        preferred_element_type=jnp.float32,
    )
    grouped = conv.reshape(images, pixels, GROUPS, width // GROUPS)
    first_sum = jnp.sum(grouped, axis=(1, 3))
    second_sum = jnp.sum(grouped * grouped, axis=(1, 3))
    stats = jnp.concatenate([local_count[..., 0], first_sum, second_sum], axis=1).reshape(1, -1)
    stats = lax.all_to_all(
        jnp.broadcast_to(stats, (devices, stats.shape[1])), ("rows", "cols"), 0, 0, tiled=True
    )
    stats = jnp.sum(stats, axis=0).reshape(images, -1)
    count = stats[:, :query_count]
    first_sum = stats[:, query_count : query_count + GROUPS]
    second_sum = stats[:, query_count + GROUPS :]
    number = devices * pixels * (width // GROUPS)
    mean = first_sum / number
    var = second_sum / number - mean * mean
    normed = (grouped - mean[:, None, :, None]) / jnp.sqrt(var[:, None, :, None] + 1e-05)
    mask_feat = jax.nn.relu(normed.reshape(images, pixels, width) * gn_gain + gn_bias).astype(
        jnp.bfloat16
    )
    keys_vals = jnp.dot(
        mask_feat, jnp.concatenate([key_weight, value_weight], axis=1), preferred_element_type=jnp.float32
    ).astype(jnp.bfloat16)
    qproj = jnp.dot(
        queries.astype(jnp.bfloat16), query_weight, preferred_element_type=jnp.float32
    ).astype(jnp.bfloat16)
    zero = (count == 0.0).astype(jnp.float32)[:, :, None]
    head_of_lane = jnp.arange(width) // head_size
    qbd = jnp.where(
        head_of_lane[None, None, None, :] == jnp.arange(heads)[None, :, None, None],
        qproj[:, None, :, :],
        jnp.zeros((), jnp.bfloat16),
    ).reshape(images, heads * query_count, width)
    top, total, weighted = attention(qbd, keys_vals, fg, zero, heads, 1.0 / head_size**0.5)
    span = images * query_count * width // devices
    groups = span // 32

    def halves(x):
        high = x.astype(jnp.bfloat16)
        return [high, (x - high.astype(jnp.float32)).astype(jnp.bfloat16)]

    packed = jnp.concatenate(
        [weighted.reshape(devices, span).astype(jnp.bfloat16)]
        + halves(total.reshape(devices, groups))
        + halves(top.reshape(devices, groups)),
        axis=1,
    )
    parts = lax.all_to_all(packed, ("rows", "cols"), 0, 0, tiled=True).astype(jnp.float32)
    sums = parts[:, :span]
    pieces = [parts[:, span + n * groups : span + (n + 1) * groups] for n in range(4)]
    totals = pieces[0] + pieces[1]
    tops = pieces[2] + pieces[3]
    highest = jnp.max(tops, axis=0, keepdims=True)
    factor = jnp.exp(tops - highest)
    totals = jnp.sum(totals * factor, axis=0, keepdims=True)
    sums = jnp.sum(sums * jnp.repeat(factor, 32, axis=1), axis=0, keepdims=True)
    attn_block = (sums / jnp.repeat(totals, 32, axis=1)).astype(jnp.bfloat16)
    attn = lax.all_to_all(
        jnp.broadcast_to(attn_block, (devices, span)), ("rows", "cols"), 0, 0, tiled=True
    ).reshape(images, query_count, width)
    mixed = queries + jnp.dot(attn, out_weight, preferred_element_type=jnp.float32)
    centre = jnp.mean(mixed, axis=2, keepdims=True)
    spread = jnp.mean((mixed - centre) ** 2, axis=2, keepdims=True)
    updated = (mixed - centre) / jnp.sqrt(spread + 1e-05) * ln_gain + ln_bias
    hidden = jax.nn.relu(
        jnp.dot(updated.astype(jnp.bfloat16), embed_one, preferred_element_type=jnp.float32)
    ).astype(jnp.bfloat16)
    embed = jnp.dot(hidden, embed_two, preferred_element_type=jnp.float32).astype(jnp.bfloat16)
    logits = logits_of(embed, mask_feat, tile_rows, tile_cols)
    return (updated, logits.reshape(images, query_count, tile_rows, tile_cols))


def solution(mesh):
    return jax.shard_map(
        on_device,
        mesh=mesh,
        in_specs=(
            P(None, "rows", "cols", None),
            P(None, None, "rows", "cols"),
            P(),
            P(),
            P(),
            P(),
            P(),
            P(),
            P(),
            P(),
            P(),
            P(),
            P(),
            P(),
        ),
        out_specs=(P(), P(None, None, "rows", "cols")),
        check_vma=False,
    )
```

```python
import jax
import jax.numpy as jnp
from jax import lax
from jax.experimental import pallas as pl
from jax.experimental.pallas import tpu as pltpu
from jax.sharding import PartitionSpec as P

HEADS = 8
GROUPS = 32
NEG = -1e30


def with_halo(cells, sides, width):
    for axis, dim in sides:
        count = lax.axis_size(axis)
        ends = count - 1
        head = lax.slice_in_dim(cells, 0, width, axis=dim)
        tail = lax.slice_in_dim(cells, cells.shape[dim] - width, cells.shape[dim], axis=dim)
        cells = jnp.concatenate(
            [
                lax.ppermute(tail, axis, [(i, (i + 1) % count) for i in range(ends)]),
                cells,
                lax.ppermute(head, axis, [((i + 1) % count, i) for i in range(ends)]),
            ],
            axis=dim,
        )
    return cells


def butterfly_sum(x):
    for axis in ("cols", "rows"):
        n = lax.axis_size(axis)
        if n & (n - 1):
            x = jax.tree.map(lambda v: lax.psum(v, axis), x)
            continue
        k = 1
        while k < n:
            got = lax.ppermute(x, axis, [(i, i ^ k) for i in range(n)])
            x = jax.tree.map(lambda a, b: a + b, x, got)
            k *= 2
    return x


def split_parts(x, span):
    return x[:, :span], x[:, span : span + span // 32], x[:, span + span // 32 :]


def merge(a, b, span):
    wa, ta, ma = split_parts(a, span)
    wb, tb, mb = split_parts(b, span)
    m = jnp.maximum(ma, mb)
    fa = jnp.exp(ma - m)
    fb = jnp.exp(mb - m)
    t = ta * fa + tb * fb
    w = wa * jnp.repeat(fa, 32, axis=1) + wb * jnp.repeat(fb, 32, axis=1)
    return jnp.concatenate([w, t, m], axis=1)


def halving_merge(x, span):
    for axis in ("cols", "rows"):
        n = lax.axis_size(axis)
        idx = lax.axis_index(axis)
        k = n // 2
        while k >= 1:
            h = x.shape[0] // 2
            lo, hi = x[:h], x[h:]
            upper = (idx // k) % 2 == 1
            keep = jnp.where(upper, hi, lo)
            send = jnp.where(upper, lo, hi)
            got = lax.ppermute(send, axis, [(i, i ^ k) for i in range(n)])
            x = merge(keep, got, span)
            k //= 2
    return x


def doubling_gather(a):
    for axis in ("rows", "cols"):
        n = lax.axis_size(axis)
        idx = lax.axis_index(axis)
        k = 1
        while k < n:
            got = lax.ppermute(a, axis, [(i, i ^ k) for i in range(n)])
            upper = (idx // k) % 2 == 1
            a = jnp.where(upper, jnp.concatenate([got, a]), jnp.concatenate([a, got]))
            k *= 2
    return a


def prep_kernel(m_ref, fg_ref, cnt_ref):
    queries = fg_ref.shape[1]
    tile_rows = m_ref.shape[1] // queries
    tile_cols = m_ref.shape[2]
    acc = jnp.zeros((queries, tile_cols), jnp.float32)
    for r in range(tile_rows):
        rows = m_ref[0, pl.ds(r, queries, stride=tile_rows), :]
        fg = (rows == 1).astype(jnp.float32)
        acc = acc + fg
        fg_ref[0, :, r * tile_cols : (r + 1) * tile_cols] = fg.astype(jnp.int8)
    cnt_ref[0] = jnp.sum(acc, axis=1, keepdims=True)


def prep(masks):
    images, queries, tile_rows, tile_cols = masks.shape
    flat = masks.reshape(images, queries * tile_rows, tile_cols)
    return pl.pallas_call(
        prep_kernel,
        grid=(images,),
        in_specs=[pl.BlockSpec((1, queries * tile_rows, tile_cols), lambda i: (i, 0, 0))],
        out_specs=[
            pl.BlockSpec((1, queries, tile_rows * tile_cols), lambda i: (i, 0, 0)),
            pl.BlockSpec((1, queries, 1), lambda i: (i, 0, 0)),
        ],
        out_shape=[
            jax.ShapeDtypeStruct((images, queries, tile_rows * tile_cols), jnp.int8),
            jax.ShapeDtypeStruct((images, queries, 1), jnp.float32),
        ],
    )(flat)


def attention_kernel(q_ref, k_ref, v_ref, fg_ref, zero_ref, top_ref, tot_ref, wv_ref, *, heads, scale):
    queries = fg_ref.shape[1]
    width = k_ref.shape[2]
    head_size = width // heads
    k = k_ref[0]
    v = v_ref[0]
    allowed = (fg_ref[0] != 0) | (zero_ref[0] != 0)
    bias = jnp.where(allowed, 0.0, -jnp.inf)
    for h in range(heads):
        q = q_ref[0, h * queries : (h + 1) * queries, :]
        s = lax.dot_general(q, k, (((1,), (1,)), ((), ())), preferred_element_type=jnp.float32) * scale
        top = jnp.maximum(jnp.max(s + bias, axis=1, keepdims=True), NEG)
        w = jnp.exp(s + bias - top).astype(jnp.bfloat16)
        tot_ref[0, :, h : h + 1] = jnp.sum(w.astype(jnp.float32), axis=1, keepdims=True)
        top_ref[0, :, h : h + 1] = top
        r = jnp.dot(w, v, preferred_element_type=jnp.float32)
        wv_ref[0, :, h * head_size : (h + 1) * head_size] = r[:, h * head_size : (h + 1) * head_size]


def attention(qbd, keys_vals, fg, zero, heads, scale):
    images, pixels, width = keys_vals.shape
    width //= 2
    queries = fg.shape[1]
    kernel = lambda *refs: attention_kernel(*refs, heads=heads, scale=scale)
    return pl.pallas_call(
        kernel,
        grid=(images,),
        in_specs=[
            pl.BlockSpec((1, heads * queries, width), lambda i: (i, 0, 0)),
            pl.BlockSpec((1, pixels, width), lambda i: (i, 0, 0)),
            pl.BlockSpec((1, pixels, width), lambda i: (i, 0, 1)),
            pl.BlockSpec((1, queries, pixels), lambda i: (i, 0, 0)),
            pl.BlockSpec((1, queries, 1), lambda i: (i, 0, 0)),
        ],
        out_specs=[
            pl.BlockSpec((1, queries, heads), lambda i: (i, 0, 0)),
            pl.BlockSpec((1, queries, heads), lambda i: (i, 0, 0)),
            pl.BlockSpec((1, queries, width), lambda i: (i, 0, 0)),
        ],
        out_shape=[
            jax.ShapeDtypeStruct((images, queries, heads), jnp.float32),
            jax.ShapeDtypeStruct((images, queries, heads), jnp.float32),
            jax.ShapeDtypeStruct((images, queries, width), jnp.float32),
        ],
    )(qbd, keys_vals, keys_vals, fg, zero)


def logits_kernel(e_ref, f_ref, o_ref, acc_ref):
    queries = e_ref.shape[1]
    tile_cols = o_ref.shape[2]
    tile_rows = o_ref.shape[1] // queries
    e = e_ref[0]
    for r in range(tile_rows):
        f = f_ref[0, r * tile_cols : (r + 1) * tile_cols, :]
        res = lax.dot_general(e, f, (((1,), (1,)), ((), ())), preferred_element_type=jnp.float32)
        acc_ref[pl.ds(r, queries, stride=tile_rows), :] = res
    o_ref[0] = acc_ref[...].astype(o_ref.dtype)


def logits_of(embed, mask_feat, tile_rows, tile_cols):
    images, queries, width = embed.shape
    pixels = mask_feat.shape[1]
    return pl.pallas_call(
        logits_kernel,
        grid=(images,),
        in_specs=[
            pl.BlockSpec((1, queries, width), lambda i: (i, 0, 0)),
            pl.BlockSpec((1, pixels, width), lambda i: (i, 0, 0)),
        ],
        out_specs=pl.BlockSpec((1, queries * tile_rows, tile_cols), lambda i: (i, 0, 0)),
        out_shape=jax.ShapeDtypeStruct((images, queries * tile_rows, tile_cols), jnp.bfloat16),
        scratch_shapes=[pltpu.VMEM((queries * tile_rows, tile_cols), jnp.float32)],
    )(embed, mask_feat)


def on_device(
    features,
    masks,
    queries,
    conv_weight,
    gn_gain,
    gn_bias,
    query_weight,
    key_weight,
    value_weight,
    out_weight,
    ln_gain,
    ln_bias,
    embed_one,
    embed_two,
):
    images, tile_rows, tile_cols, width = features.shape
    query_count = queries.shape[1]
    heads = HEADS
    head_size = width // heads
    pixels = tile_rows * tile_cols
    devices = lax.axis_size("rows") * lax.axis_size("cols")
    fg, local_count = prep(masks)
    padded = with_halo(features, (("rows", 1), ("cols", 2)), 1)
    conv = lax.conv_general_dilated(
        padded,
        conv_weight,
        (1, 1),
        "VALID",
        dimension_numbers=("NHWC", "HWIO", "NHWC"),
        preferred_element_type=jnp.float32,
    )
    grouped = conv.reshape(images, pixels, GROUPS, width // GROUPS)
    first_sum = jnp.sum(grouped, axis=(1, 3))
    second_sum = jnp.sum(grouped * grouped, axis=(1, 3))
    stats = jnp.concatenate([local_count[..., 0], first_sum, second_sum], axis=1).reshape(1, -1)
    stats = lax.all_to_all(
        jnp.broadcast_to(stats, (devices, stats.shape[1])), ("rows", "cols"), 0, 0, tiled=True
    )
    stats = jnp.sum(stats, axis=0).reshape(images, -1)
    count = stats[:, :query_count]
    first_sum = stats[:, query_count : query_count + GROUPS]
    second_sum = stats[:, query_count + GROUPS :]
    number = devices * pixels * (width // GROUPS)
    mean = first_sum / number
    var = second_sum / number - mean * mean
    normed = (grouped - mean[:, None, :, None]) / jnp.sqrt(var[:, None, :, None] + 1e-05)
    mask_feat = jax.nn.relu(normed.reshape(images, pixels, width) * gn_gain + gn_bias).astype(
        jnp.bfloat16
    )
    keys_vals = jnp.dot(
        mask_feat, jnp.concatenate([key_weight, value_weight], axis=1), preferred_element_type=jnp.float32
    ).astype(jnp.bfloat16)
    qproj = jnp.dot(
        queries.astype(jnp.bfloat16), query_weight, preferred_element_type=jnp.float32
    ).astype(jnp.bfloat16)
    zero = (count == 0.0).astype(jnp.float32)[:, :, None]
    head_of_lane = jnp.arange(width) // head_size
    qbd = jnp.where(
        head_of_lane[None, None, None, :] == jnp.arange(heads)[None, :, None, None],
        qproj[:, None, :, :],
        jnp.zeros((), jnp.bfloat16),
    ).reshape(images, heads * query_count, width)
    top, total, weighted = attention(qbd, keys_vals, fg, zero, heads, 1.0 / head_size**0.5)
    span = images * query_count * width // devices
    groups = span // 32

    def halves(x):
        high = x.astype(jnp.bfloat16)
        return [high, (x - high.astype(jnp.float32)).astype(jnp.bfloat16)]

    packed = jnp.concatenate(
        [weighted.reshape(devices, span).astype(jnp.bfloat16)]
        + halves(total.reshape(devices, groups))
        + halves(top.reshape(devices, groups)),
        axis=1,
    )
    parts = lax.all_to_all(packed, ("rows", "cols"), 0, 0, tiled=True).astype(jnp.float32)
    sums = parts[:, :span]
    pieces = [parts[:, span + n * groups : span + (n + 1) * groups] for n in range(4)]
    totals = pieces[0] + pieces[1]
    tops = pieces[2] + pieces[3]
    highest = jnp.max(tops, axis=0, keepdims=True)
    factor = jnp.exp(tops - highest)
    totals = jnp.sum(totals * factor, axis=0, keepdims=True)
    sums = jnp.sum(sums * jnp.repeat(factor, 32, axis=1), axis=0, keepdims=True)
    attn_block = (sums / jnp.repeat(totals, 32, axis=1)).astype(jnp.bfloat16)
    attn = lax.all_to_all(
        jnp.broadcast_to(attn_block, (devices, span)), ("rows", "cols"), 0, 0, tiled=True
    ).reshape(images, query_count, width)
    mixed = queries + jnp.dot(attn, out_weight, preferred_element_type=jnp.float32)
    centre = jnp.mean(mixed, axis=2, keepdims=True)
    spread = jnp.mean((mixed - centre) ** 2, axis=2, keepdims=True)
    updated = (mixed - centre) / jnp.sqrt(spread + 1e-05) * ln_gain + ln_bias
    hidden = jax.nn.relu(
        jnp.dot(updated.astype(jnp.bfloat16), embed_one, preferred_element_type=jnp.float32)
    ).astype(jnp.bfloat16)
    embed = jnp.dot(hidden, embed_two, preferred_element_type=jnp.float32).astype(jnp.bfloat16)
    logits = logits_of(embed, mask_feat, tile_rows, tile_cols)
    return (updated, logits.reshape(images, query_count, tile_rows, tile_cols))


def solution(mesh):
    return jax.shard_map(
        on_device,
        mesh=mesh,
        in_specs=(
            P(None, "rows", "cols", None),
            P(None, None, "rows", "cols"),
            P(),
            P(),
            P(),
            P(),
            P(),
            P(),
            P(),
            P(),
            P(),
            P(),
            P(),
            P(),
        ),
        out_specs=(P(), P(None, None, "rows", "cols")),
        check_vma=False,
    )
```
